128 devices in a mesh: req: 8 (over y, x_hi), row: 4 (over x_lo, core), col: 4 (over z).
Axes of the slice: x: 4 (x_hi: 2, x_lo: 2; x = x_hi * 2 + x_lo), y: 4, z: 4, core: 2. Of those that a mesh axis runs over, the one named last changes fastest.
Arguments:
- text_embed: bfloat16 [6144, 4096], P(('req', 'col'), 'row')
- vis_embed: bfloat16 [4096, 4096], P(('req', 'col'), 'row')
- vis_segment: int32 [4096], P(('req', 'col')), may hold values from 0 to 20, never falling along the last dimension, each value on 1 to 256 neighbouring positions
- vis_valid: int32 [4096], P(('req', 'col')), may hold values 0 or 1
- vis_gain: bfloat16 [4096], P('row'), may hold values from 0.25 to 1.75
- vis_wq: bfloat16 [4096, 4096], P('row', 'col')
- vis_wk: bfloat16 [4096, 4096], P('row', 'col')
- vis_wv: bfloat16 [4096, 4096], P('row', 'col'), may hold values from -0.09375 to 0.09375
- vis_wo: bfloat16 [4096, 4096], P('col', 'row'), may hold values from -0.09375 to 0.09375
- dec_gain: bfloat16 [4096], P('row'), may hold values from 0.25 to 1.75
- dec_wq: bfloat16 [4096, 4096], P('row', 'col')
- dec_wk: bfloat16 [4096, 4096], P('row', 'col')
- dec_wv: bfloat16 [4096, 4096], P('row', 'col'), may hold values from -0.09375 to 0.09375
- dec_wo: bfloat16 [4096, 4096], P('col', 'row'), may hold values from -0.09375 to 0.09375
Outputs:
- hidden_out: bfloat16 [6144, 4096], P(('req', 'col'), 'row')
The draws below stay inside these ranges and needn't reach their ends.
Inputs may be any that keep to these rules, and one draw needn't show every extreme that they name: `vis_segment`: images take consecutive slots in order, each 1 to 256 slots, one exactly 256.
All inputs are finite; a program needn't handle non-finite values. No bound on the sum of `vis_valid` on one device may be relied on, other than what follows from the above.
Results may differ from the reference program's by a relative error of at most 0.008.
Values may be sent and summed in bfloat16 or wider, within the bound.
No kernel may reach another device: no remote copies, remote signals or barrier semaphores. Data moves between devices by JAX's collectives and lax.ppermute only.
A program may use at most 192 MiB of HBM per device.

```python
import math
import jax
import jax.numpy as jnp
import numpy as np
from jax import lax

D = 4096
HEADS = 32
HD = 128
MAXIMG = 256
PROMPT = 6144
VIS = 4096
IMAGES = 21


def rising_columns():
    columns = jnp.arange(D, dtype=jnp.float32)
    return 0.6 * jnp.exp(math.log(3.0) * columns / D)


def block_factors(key, count):
    factors = jnp.exp(jax.random.uniform(key, (count, 8), jnp.float32, -1.0, 1.0))
    return jnp.repeat(factors, D // 8, axis=1)


def drawn_rows(key, count, salt):
    own = jax.random.fold_in(key, salt)
    first, second = jax.random.split(own, 2)
    values = jax.random.normal(first, (count, D), jnp.float32) * rising_columns()
    return (values * block_factors(second, count)).astype(jnp.bfloat16)


def drawn_weight(key, salt):
    own = jax.random.normal(jax.random.fold_in(key, salt), (D, D), jnp.float32)
    return (own * D ** (-0.5)).astype(jnp.bfloat16)


def draw_text_embed(key, part):
    return drawn_rows(key, PROMPT, 11)


def draw_vis_embed(key, part):
    return drawn_rows(key, VIS, 12)


def draw_vis_wq(key, part):
    return drawn_weight(key, 31)


def draw_vis_wk(key, part):
    return drawn_weight(key, 32)


def draw_dec_wq(key, part):
    return drawn_weight(key, 41)


def draw_dec_wk(key, part):
    return drawn_weight(key, 42)


def set_ends(entries, own_key, low, largest):
    longest = entries.shape.index(max(entries.shape))
    spots = []
    for shift in (0, 1):
        where = [jax.random.randint(jax.random.fold_in(own_key, axis), (), 0, length) for axis, length in enumerate(entries.shape)]
        where[longest] = (where[longest] + shift) % entries.shape[longest]
        spots.append(tuple(where))
    return entries.at[spots[0]].set(low).at[spots[1]].set(largest)


def levels(stream_key, dims, cuts, low, top_value):
    def one(dim, shards_of):
        heights = jax.random.uniform(jax.random.fold_in(jax.random.fold_in(stream_key, 6), dim), (shards_of,), jnp.float32, low / len(cuts), top_value / len(cuts))
        return jnp.repeat(jnp.exp(heights), dims[dim] // shards_of).reshape((-1,) + (1,) * (len(dims) - dim - 1))

    factor_of = one(*cuts[0])
    for cut in cuts[1:]:
        factor_of = factor_of * one(*cut)
    return factor_of


def length_profile(amount, total, reach, slope):
    portions = [(1 << 20) // math.isqrt(standing ** slope) + 1 for standing in range(2, amount + 1)]
    rest, counts = total - reach - (amount - 1), [1] * (amount - 1)
    while rest > 0:
        free = [i for i in range(amount - 1) if counts[i] < reach]
        pool, left = sum([portions[i] for i in free]), rest
        for i in free:
            extra = min(reach - counts[i], max(1, left * portions[i] // pool), rest)
            counts[i] = counts[i] + extra
            rest = rest - extra
    return np.array([reach] + counts)


def ragged_sizes(own_key, count, total, most, lean):
    if count == 2:
        one = jax.random.randint(own_key, (), max(1, total - most), min(most, total - 1) + 1)
        return jnp.stack([one, total - one])
    sizes = jnp.asarray(length_profile(count, total, most, lean), jnp.int32)
    pairs = (count - 1) // 2
    donor, sink = sizes[1:1 + 2 * pairs:2], sizes[2:2 + 2 * pairs:2]
    slack = jnp.minimum(donor - 1, most - sink)
    moved = jax.random.randint(jax.random.fold_in(own_key, 1), (pairs,), 0, 1 << 20) % (slack + 1)
    sizes = sizes.at[1:1 + 2 * pairs:2].set(donor - moved).at[2:2 + 2 * pairs:2].set(sink + moved)
    return sizes[jax.random.permutation(jax.random.fold_in(own_key, 2), count)]


def centred(key, extent, spread, most, cuts=(), kind=jnp.bfloat16):
    array = jax.random.normal(key, extent, jnp.float32) * spread
    if len(cuts) > 0:
        array = levels(key, extent, cuts, -0.22, 0.18) * array
    return jnp.clip(array, min=-most, max=most).astype(kind)


def setup_inputs(seed: int = 0) -> dict:
    key_of = jax.random.split(jax.random.key(seed), 15)
    return {
        "text_embed": draw_text_embed(jax.random.fold_in(key_of[14], 71), 0),
        "vis_embed": draw_vis_embed(jax.random.fold_in(key_of[14], 71), 0),
        "vis_segment": jnp.searchsorted(jnp.cumsum(ragged_sizes(key_of[2], IMAGES, VIS, MAXIMG, 1)), jnp.arange(VIS), side="right").astype(jnp.int32),
        "vis_valid": set_ends((jax.random.randint(key_of[3], (VIS,), 0, 8) < 7).astype(jnp.int32), jax.random.fold_in(key_of[3], 1), 0, 1),
        "vis_gain": jnp.clip(1.0 + 0.15 * jax.random.normal(key_of[4], (D,), jnp.float32), 0.25, 1.75).astype(jnp.bfloat16),
        "vis_wq": draw_vis_wq(jax.random.fold_in(key_of[14], 71), 0),
        "vis_wk": draw_vis_wk(jax.random.fold_in(key_of[14], 71), 0),
        "vis_wv": centred(key_of[7], (D, D), D ** -0.5, 0.09375, ((0, 4), (1, 4))),
        "vis_wo": centred(key_of[8], (D, D), D ** -0.5, 0.09375, ((0, 4), (1, 4))),
        "dec_gain": jnp.clip(1.0 + 0.15 * jax.random.normal(key_of[9], (D,), jnp.float32), 0.25, 1.75).astype(jnp.bfloat16),
        "dec_wq": draw_dec_wq(jax.random.fold_in(key_of[14], 71), 0),
        "dec_wk": draw_dec_wk(jax.random.fold_in(key_of[14], 71), 0),
        "dec_wv": centred(key_of[12], (D, D), D ** -0.5, 0.09375, ((0, 4), (1, 4))),
        "dec_wo": centred(key_of[13], (D, D), D ** -0.5, 0.09375, ((0, 4), (1, 4))),
    }


def rms_norm(values, gain):
    floats = values.astype(jnp.float32)
    factor = lax.rsqrt(lax.optimization_barrier(jnp.mean(floats * floats, axis=-1, keepdims=True)) + 1e-05)
    return (floats * factor * gain.astype(jnp.float32)).astype(jnp.bfloat16)

def project(values, weight):
    return jnp.dot(values, weight, preferred_element_type=jnp.float32).astype(jnp.bfloat16)

def attend(queries, keys, values, allowed):
    count = queries.shape[0]
    shaped = [a.reshape(count, HEADS, HD).transpose(1, 0, 2) for a in (queries, keys, values)]

    def one_head(group):
        query_head, key_head, value_head = group
        scores = jnp.dot(query_head.astype(jnp.float32), key_head.astype(jnp.float32).T) * HD ** (-0.5)
        scores = jnp.where(allowed, scores, -1e+30)
        peak = lax.optimization_barrier(jnp.max(scores, axis=-1, keepdims=True))
        weights = jnp.where(allowed, jnp.exp(scores - peak), 0.0)
        mass = lax.optimization_barrier(jnp.sum(weights, axis=-1))
        rounded = weights.astype(jnp.bfloat16)
        summed = jnp.dot(rounded, value_head, preferred_element_type=jnp.float32)
        return (summed / mass[:, None]).astype(jnp.bfloat16)
    heads = lax.map(one_head, tuple(shaped))
    return heads.transpose(1, 0, 2).reshape(count, HEADS * HD)

def reference(text_embed, vis_embed, vis_segment, vis_valid, vis_gain, vis_wq, vis_wk, vis_wv, vis_wo, dec_gain, dec_wq, dec_wk, dec_wv, dec_wo):
    vis_norm = rms_norm(vis_embed, vis_gain)
    slots = jnp.arange(VIS, dtype=jnp.int32)
    seen = (vis_segment[:, None] == vis_segment[None, :]) & ((vis_valid[None, :] == 1) | (slots[:, None] == slots[None, :]))
    vis_att = attend(project(vis_norm, vis_wq), project(vis_norm, vis_wk), project(vis_norm, vis_wv), seen)
    vis_out = (vis_embed.astype(jnp.float32) + jnp.dot(vis_att, vis_wo, preferred_element_type=jnp.float32)).astype(jnp.bfloat16)
    begins = jnp.concatenate([jnp.ones((1,), jnp.bool_), vis_segment[1:] != vis_segment[:-1]])
    image_first = lax.cummax(jnp.where(begins, slots, 0).astype(jnp.int32), axis=0)
    patch_target = (image_first * PROMPT // VIS + slots - image_first).astype(jnp.int32)
    placed = vis_out.astype(jnp.float32) * (vis_valid == 1).astype(jnp.float32)[:, None]
    carried = jax.ops.segment_sum(placed, patch_target, num_segments=PROMPT)
    mixed = (text_embed.astype(jnp.float32) + carried).astype(jnp.bfloat16)
    dec_norm = rms_norm(mixed, dec_gain)
    places = jnp.arange(PROMPT, dtype=jnp.int32)
    causal = places[:, None] >= places[None, :]
    dec_att = attend(project(dec_norm, dec_wq), project(dec_norm, dec_wk), project(dec_norm, dec_wv), causal)
    return (mixed.astype(jnp.float32) + jnp.dot(dec_att, dec_wo, preferred_element_type=jnp.float32)).astype(jnp.bfloat16)
```

```python
import jax
import jax.numpy as jnp
from jax import lax
from jax.sharding import PartitionSpec as P

D = 4096
HD = 128
MAXIMG = 256


def with_halo(cells, sides, width):
    for axis, dim in sides:
        count = lax.axis_size(axis)
        ends = count - 1
        head = lax.slice_in_dim(cells, 0, width, axis=dim)
        tail = lax.slice_in_dim(cells, cells.shape[dim] - width, cells.shape[dim], axis=dim)
        cells = jnp.concatenate(
            [
                lax.ppermute(tail, axis, [(i, (i + 1) % count) for i in range(ends)]),
                cells,
                lax.ppermute(head, axis, [((i + 1) % count, i) for i in range(ends)]),
            ],
            axis=dim,
        )
    return cells


def passed_along(shard, axis, by):
    size = lax.axis_size(axis)
    pairs = [(i, i + by) for i in range(size) if 0 <= i + by < size]
    return lax.ppermute(shard, axis, pairs)


def norm_local(values, gain):
    floats = values.astype(jnp.float32)
    squares = jnp.sum(floats * floats, axis=-1)
    totals = lax.psum(squares, "row")
    factor = lax.rsqrt(totals / D + 1e-05)
    return (floats * factor[:, None] * gain.astype(jnp.float32)[None, :]).astype(jnp.bfloat16)


def gather_cols(values):
    return lax.all_gather(values, "col", axis=0, tiled=True)


def out_project(attended, weight):
    whole = lax.all_gather(attended, "row", axis=0, tiled=True)
    return lax.psum_scatter(
        jnp.dot(whole, weight, preferred_element_type=jnp.float32).astype(jnp.bfloat16),
        "col",
        scatter_dimension=0,
        tiled=True,
    ).astype(jnp.float32)


def split_heads(values):
    return values.reshape(values.shape[0], values.shape[1] // HD, HD)


def attend_block(queries, keys, values, allowed):
    query_heads = split_heads(queries)
    scores = jnp.einsum(
        "qhd,khd->hqk", query_heads, split_heads(keys), preferred_element_type=jnp.float32
    ) * HD ** (-0.5)
    scores = jnp.where(allowed[None], scores, -1e30)
    peak = jnp.max(scores, axis=-1, keepdims=True)
    weights = jnp.where(allowed[None], jnp.exp(scores - peak), 0.0)
    mass = jnp.sum(weights, axis=-1)
    summed = jnp.einsum(
        "hqk,khd->qhd",
        weights.astype(jnp.bfloat16),
        split_heads(values),
        preferred_element_type=jnp.float32,
    )
    result = summed / jnp.transpose(mass)[:, :, None]
    return result.reshape(queries.shape[0], queries.shape[1]).astype(jnp.bfloat16)


def fold_step(carry, query_heads, query_slots, key_heads, value_heads):
    peak, mass, accum = carry
    piece_slots = jnp.arange(key_heads.shape[0], dtype=jnp.int32)
    allowed = query_slots[:, None] >= piece_slots[None, :]
    scores = jnp.einsum(
        "qhd,khd->hqk", query_heads, key_heads, preferred_element_type=jnp.float32
    ) * HD ** (-0.5)
    scores = jnp.where(allowed[None], scores, -1e30)
    new_peak = jnp.maximum(peak, jnp.max(scores, axis=-1))
    weights = jnp.where(allowed[None], jnp.exp(scores - new_peak[:, :, None]), 0.0)
    summed = jnp.einsum(
        "hqk,khd->hqd",
        weights.astype(jnp.bfloat16),
        value_heads,
        preferred_element_type=jnp.float32,
    )
    return (new_peak, jnp.sum(weights, axis=-1), summed)


def start_state(head_count, query_count):
    return (
        jnp.full((head_count, query_count), -1e30, jnp.float32),
        jnp.zeros((head_count, query_count), jnp.float32),
        jnp.zeros((head_count, query_count, HD), jnp.float32),
    )


def head_project(values, weights):
    count = values.shape[0]
    row_count = lax.axis_size("row")
    width = weights[0].shape[1]
    parts = [
        jnp.dot(values, w, preferred_element_type=jnp.float32)
        .astype(jnp.bfloat16)
        .reshape(count, row_count, width // row_count)
        for w in weights
    ]
    stacked = jnp.stack(parts, axis=2).transpose(1, 0, 2, 3)
    stacked = stacked.reshape(row_count * count, len(weights) * (width // row_count))
    return lax.psum_scatter(stacked, "row", scatter_dimension=0, tiled=True)


def out_project_heads(attended, weight):
    row_count = lax.axis_size("row")
    whole = lax.all_gather(attended, "row", axis=0, tiled=False)
    shaped = weight.reshape(row_count, weight.shape[0] // row_count, weight.shape[1])
    summed = jnp.einsum("rtf,rfo->to", whole, shaped, preferred_element_type=jnp.float32)
    return lax.psum_scatter(
        summed.astype(jnp.bfloat16), "col", scatter_dimension=0, tiled=True
    ).astype(jnp.float32)


def per_device(
    text_embed,
    vis_embed,
    vis_segment,
    vis_valid,
    vis_gain,
    vis_wq,
    vis_wk,
    vis_wv,
    vis_wo,
    dec_gain,
    dec_wq,
    dec_wk,
    dec_wv,
    dec_wo,
):
    row_count = lax.axis_size("row")
    col_count = lax.axis_size("col")
    width = vis_wq.shape[1]
    local = width // row_count
    margin = MAXIMG - 1
    piece_ids = lax.all_gather(jnp.stack([vis_segment, vis_valid]), "col", axis=1, tiled=True)
    piece_len = piece_ids.shape[1]
    framed_ids = with_halo(piece_ids, (("req", 1),), margin)
    total_slots = piece_len * lax.axis_size("req")
    prompt_rows = text_embed.shape[0]
    prompt_total = prompt_rows * lax.axis_size("req") * col_count
    window_len = piece_len + 2 * margin
    window_start = lax.axis_index("req") * piece_len - margin
    window_index = jnp.arange(window_len, dtype=jnp.int32)
    key_slots = window_start + window_index
    inside = (key_slots >= 0) & (key_slots < total_slots)
    key_segment = framed_ids[0]
    key_valid = framed_ids[1]
    begins = jnp.concatenate([jnp.ones((1,), jnp.bool_), key_segment[1:] != key_segment[:-1]])
    begins = begins | (key_slots == 0)
    image_first = lax.cummax(jnp.where(begins, key_slots, window_start), axis=0)
    target_window = image_first * prompt_total // total_slots + key_slots - image_first
    vis_cols = gather_cols(norm_local(vis_embed, vis_gain))
    vis_proj = head_project(vis_cols, (vis_wq, vis_wk, vis_wv))
    vis_pairs = jnp.stack([vis_proj[:, local : 2 * local], vis_proj[:, 2 * local :]])
    framed = with_halo(vis_pairs, (("req", 1),), margin)
    query_local = margin + jnp.arange(piece_len, dtype=jnp.int32)
    query_slots = window_start + query_local
    query_segment = key_segment[query_local]
    seen = (
        inside[None, :]
        & (query_segment[:, None] == key_segment[None, :])
        & ((key_valid[None, :] == 1) | (query_slots[:, None] == key_slots[None, :]))
    )
    vis_att = attend_block(vis_proj[:, :local], framed[0], framed[1], seen)
    vis_out = (vis_embed.astype(jnp.float32) + out_project_heads(vis_att, vis_wo)).astype(
        jnp.bfloat16
    )
    device_place = lax.axis_index("req") * col_count + lax.axis_index("col")
    owned = device_place * prompt_rows + jnp.arange(prompt_rows, dtype=jnp.int32)
    slot_rows = vis_out.shape[0]
    following = passed_along(vis_out, ("req", "col"), -1)
    near_rows = jnp.concatenate([vis_out, following], axis=0)
    near_local = (
        margin + lax.axis_index("col") * slot_rows + jnp.arange(2 * slot_rows, dtype=jnp.int32)
    )
    near_slots = window_start + near_local
    present = near_slots < total_slots
    near_target = jnp.where(present, target_window[near_local], -1)
    near_valid = key_valid[near_local]
    onehot = ((owned[:, None] == near_target[None, :]) & (near_valid[None, :] == 1)).astype(
        jnp.bfloat16
    )
    carried = jnp.dot(onehot, near_rows, preferred_element_type=jnp.float32)
    mixed = (text_embed.astype(jnp.float32) + carried).astype(jnp.bfloat16)
    dec_cols = gather_cols(norm_local(mixed, dec_gain))
    dec_proj = head_project(dec_cols, (dec_wq, dec_wk, dec_wv))
    dec_rows = dec_cols.shape[0]
    dec_pairs = jnp.stack([dec_proj[:, local : 2 * local], dec_proj[:, 2 * local :]])
    piece = lax.all_gather(dec_pairs, "req", axis=1, tiled=True)
    token_slots = lax.axis_index("req") * dec_rows + jnp.arange(dec_rows, dtype=jnp.int32)
    all_slots = jnp.arange(piece.shape[1], dtype=jnp.int32)
    causal = token_slots[:, None] >= all_slots[None, :]
    dec_att = attend_block(dec_proj[:, :local], piece[0], piece[1], causal)
    return (mixed.astype(jnp.float32) + out_project_heads(dec_att, dec_wo)).astype(jnp.bfloat16)


def solution(mesh):
    return jax.shard_map(
        per_device,
        mesh=mesh,
        in_specs=(
            P(("req", "col"), "row"),
            P(("req", "col"), "row"),
            P(("req", "col")),
            P(("req", "col")),
            P("row"),
            P("row", "col"),
            P("row", "col"),
            P("row", "col"),
            P("col", "row"),
            P("row"),
            P("row", "col"),
            P("row", "col"),
            P("row", "col"),
            P("col", "row"),
        ),
        out_specs=P(("req", "col"), "row"),
        check_vma=False,
    )
```

```python
import jax
import jax.numpy as jnp
from jax import lax
from jax.sharding import PartitionSpec as P

D = 4096
HD = 128
MAXIMG = 256


def with_halo(cells, sides, width):
    for axis, dim in sides:
        count = lax.axis_size(axis)
        ends = count - 1
        head = lax.slice_in_dim(cells, 0, width, axis=dim)
        tail = lax.slice_in_dim(cells, cells.shape[dim] - width, cells.shape[dim], axis=dim)
        cells = jnp.concatenate(
            [
                lax.ppermute(tail, axis, [(i, (i + 1) % count) for i in range(ends)]),
                cells,
                lax.ppermute(head, axis, [((i + 1) % count, i) for i in range(ends)]),
            ],
            axis=dim,
        )
    return cells


def passed_along(shard, axis, by):
    size = lax.axis_size(axis)
    pairs = [(i, i + by) for i in range(size) if 0 <= i + by < size]
    return lax.ppermute(shard, axis, pairs)


def norm_local(values, gain):
    floats = values.astype(jnp.float32)
    squares = jnp.sum(floats * floats, axis=-1)
    totals = lax.psum(squares, "row")
    factor = lax.rsqrt(totals / D + 1e-05)
    return (floats * factor[:, None] * gain.astype(jnp.float32)[None, :]).astype(jnp.bfloat16)


def gather_cols(values):
    return lax.all_gather(values, "col", axis=0, tiled=True)


def out_project(attended, weight):
    whole = lax.all_gather(attended, "row", axis=0, tiled=True)
    return lax.psum_scatter(
        jnp.dot(whole, weight, preferred_element_type=jnp.float32).astype(jnp.bfloat16),
        "col",
        scatter_dimension=0,
        tiled=True,
    ).astype(jnp.float32)


def split_heads(values):
    return values.reshape(values.shape[0], values.shape[1] // HD, HD)


def attend_block(queries, keys, values, allowed):
    query_heads = split_heads(queries)
    scores = jnp.einsum(
        "qhd,khd->hqk", query_heads, split_heads(keys), preferred_element_type=jnp.float32
    ) * HD ** (-0.5)
    scores = jnp.where(allowed[None], scores, -1e30)
    peak = jnp.max(scores, axis=-1, keepdims=True)
    weights = jnp.where(allowed[None], jnp.exp(scores - peak), 0.0)
    mass = jnp.sum(weights, axis=-1)
    summed = jnp.einsum(
        "hqk,khd->qhd",
        weights.astype(jnp.bfloat16),
        split_heads(values),
        preferred_element_type=jnp.float32,
    )
    result = summed / jnp.transpose(mass)[:, :, None]
    return result.reshape(queries.shape[0], queries.shape[1]).astype(jnp.bfloat16)


def fold_step(carry, query_heads, query_slots, key_heads, value_heads):
    peak, mass, accum = carry
    piece_slots = jnp.arange(key_heads.shape[0], dtype=jnp.int32)
    allowed = query_slots[:, None] >= piece_slots[None, :]
    scores = jnp.einsum(
        "qhd,khd->hqk", query_heads, key_heads, preferred_element_type=jnp.float32
    ) * HD ** (-0.5)
    scores = jnp.where(allowed[None], scores, -1e30)
    new_peak = jnp.maximum(peak, jnp.max(scores, axis=-1))
    weights = jnp.where(allowed[None], jnp.exp(scores - new_peak[:, :, None]), 0.0)
    summed = jnp.einsum(
        "hqk,khd->hqd",
        weights.astype(jnp.bfloat16),
        value_heads,
        preferred_element_type=jnp.float32,
    )
    return (new_peak, jnp.sum(weights, axis=-1), summed)


def start_state(head_count, query_count):
    return (
        jnp.full((head_count, query_count), -1e30, jnp.float32),
        jnp.zeros((head_count, query_count), jnp.float32),
        jnp.zeros((head_count, query_count, HD), jnp.float32),
    )


def head_project(values, weights):
    row_count = lax.axis_size("row")
    width = weights[0].shape[1]
    depth = weights[0].shape[0]
    shaped = jnp.stack(
        [w.reshape(depth, row_count, width // row_count) for w in weights], axis=2
    ).reshape(depth, row_count, len(weights) * (width // row_count))
    summed = jnp.einsum("tf,frc->rtc", values, shaped, preferred_element_type=jnp.float32)
    summed = summed.astype(jnp.bfloat16).reshape(row_count * values.shape[0], -1)
    return lax.psum_scatter(summed, "row", scatter_dimension=0, tiled=True)


def out_project_heads(attended, weight):
    row_count = lax.axis_size("row")
    whole = lax.all_gather(attended, "row", axis=0, tiled=False)
    shaped = weight.reshape(row_count, weight.shape[0] // row_count, weight.shape[1])
    summed = jnp.einsum("rtf,rfo->to", whole, shaped, preferred_element_type=jnp.float32)
    return lax.psum_scatter(
        summed.astype(jnp.bfloat16), "col", scatter_dimension=0, tiled=True
    ).astype(jnp.float32)


def per_device(
    text_embed,
    vis_embed,
    vis_segment,
    vis_valid,
    vis_gain,
    vis_wq,
    vis_wk,
    vis_wv,
    vis_wo,
    dec_gain,
    dec_wq,
    dec_wk,
    dec_wv,
    dec_wo,
):
    row_count = lax.axis_size("row")
    col_count = lax.axis_size("col")
    width = vis_wq.shape[1]
    local = width // row_count
    margin = MAXIMG - 1
    piece_ids = lax.all_gather(jnp.stack([vis_segment, vis_valid]), "col", axis=1, tiled=True)
    piece_len = piece_ids.shape[1]
    framed_ids = with_halo(piece_ids, (("req", 1),), margin)
    total_slots = piece_len * lax.axis_size("req")
    prompt_rows = text_embed.shape[0]
    prompt_total = prompt_rows * lax.axis_size("req") * col_count
    window_len = piece_len + 2 * margin
    window_start = lax.axis_index("req") * piece_len - margin
    window_index = jnp.arange(window_len, dtype=jnp.int32)
    key_slots = window_start + window_index
    inside = (key_slots >= 0) & (key_slots < total_slots)
    key_segment = framed_ids[0]
    key_valid = framed_ids[1]
    begins = jnp.concatenate([jnp.ones((1,), jnp.bool_), key_segment[1:] != key_segment[:-1]])
    begins = begins | (key_slots == 0)
    image_first = lax.cummax(jnp.where(begins, key_slots, window_start), axis=0)
    target_window = image_first * prompt_total // total_slots + key_slots - image_first
    vis_cols = gather_cols(norm_local(vis_embed, vis_gain))
    vis_proj = head_project(vis_cols, (vis_wq, vis_wk, vis_wv))
    vis_pairs = jnp.stack([vis_proj[:, local : 2 * local], vis_proj[:, 2 * local :]])
    framed = with_halo(vis_pairs, (("req", 1),), margin)
    query_local = margin + jnp.arange(piece_len, dtype=jnp.int32)
    query_slots = window_start + query_local
    query_segment = key_segment[query_local]
    seen = (
        inside[None, :]
        & (query_segment[:, None] == key_segment[None, :])
        & ((key_valid[None, :] == 1) | (query_slots[:, None] == key_slots[None, :]))
    )
    vis_att = attend_block(vis_proj[:, :local], framed[0], framed[1], seen)
    vis_out = (vis_embed.astype(jnp.float32) + out_project_heads(vis_att, vis_wo)).astype(
        jnp.bfloat16
    )
    device_place = lax.axis_index("req") * col_count + lax.axis_index("col")
    owned = device_place * prompt_rows + jnp.arange(prompt_rows, dtype=jnp.int32)
    slot_rows = vis_out.shape[0]
    following = passed_along(vis_out, ("req", "col"), -1)
    near_rows = jnp.concatenate([vis_out, following], axis=0)
    near_local = (
        margin + lax.axis_index("col") * slot_rows + jnp.arange(2 * slot_rows, dtype=jnp.int32)
    )
    near_slots = window_start + near_local
    present = near_slots < total_slots
    near_target = jnp.where(present, target_window[near_local], -1)
    near_valid = key_valid[near_local]
    onehot = ((owned[:, None] == near_target[None, :]) & (near_valid[None, :] == 1)).astype(
        jnp.bfloat16
    )
    carried = jnp.dot(onehot, near_rows, preferred_element_type=jnp.float32)
    mixed = (text_embed.astype(jnp.float32) + carried).astype(jnp.bfloat16)
    dec_cols = gather_cols(norm_local(mixed, dec_gain))
    dec_proj = head_project(dec_cols, (dec_wq, dec_wk, dec_wv))
    dec_rows = dec_cols.shape[0]
    dec_pairs = jnp.stack([dec_proj[:, local : 2 * local], dec_proj[:, 2 * local :]])
    piece = lax.all_gather(dec_pairs, "req", axis=1, tiled=True)
    token_slots = lax.axis_index("req") * dec_rows + jnp.arange(dec_rows, dtype=jnp.int32)
    all_slots = jnp.arange(piece.shape[1], dtype=jnp.int32)
    causal = token_slots[:, None] >= all_slots[None, :]
    dec_att = attend_block(dec_proj[:, :local], piece[0], piece[1], causal)
    return (mixed.astype(jnp.float32) + out_project_heads(dec_att, dec_wo)).astype(jnp.bfloat16)


def solution(mesh):
    return jax.shard_map(
        per_device,
        mesh=mesh,
        in_specs=(
            P(("req", "col"), "row"),
            P(("req", "col"), "row"),
            P(("req", "col")),
            P(("req", "col")),
            P("row"),
            P("row", "col"),
            P("row", "col"),
            P("row", "col"),
            P("col", "row"),
            P("row"),
            P("row", "col"),
            P("row", "col"),
            P("row", "col"),
            P("col", "row"),
        ),
        out_specs=P(("req", "col"), "row"),
        check_vma=False,
    )
```

```python
import jax
import jax.numpy as jnp
from jax import lax
from jax.sharding import PartitionSpec as P
from jax.experimental import pallas as pl
from jax.experimental.pallas import tpu as pltpu

D = 4096
HD = 128
MAXIMG = 256


def with_halo(cells, sides, width):
    for axis, dim in sides:
        count = lax.axis_size(axis)
        ends = count - 1
        head = lax.slice_in_dim(cells, 0, width, axis=dim)
        tail = lax.slice_in_dim(cells, cells.shape[dim] - width, cells.shape[dim], axis=dim)
        cells = jnp.concatenate(
            [
                lax.ppermute(tail, axis, [(i, (i + 1) % count) for i in range(ends)]),
                cells,
                lax.ppermute(head, axis, [((i + 1) % count, i) for i in range(ends)]),
            ],
            axis=dim,
        )
    return cells


def passed_along(shard, axis, by):
    size = lax.axis_size(axis)
    pairs = [(i, i + by) for i in range(size) if 0 <= i + by < size]
    return lax.ppermute(shard, axis, pairs)


def norm_local(values, gain):
    floats = values.astype(jnp.float32)
    squares = jnp.sum(floats * floats, axis=-1)
    totals = lax.psum(squares, "row")
    factor = lax.rsqrt(totals / D + 1e-05)
    return (floats * factor[:, None] * gain.astype(jnp.float32)[None, :]).astype(jnp.bfloat16)


def gather_cols(values):
    return lax.all_gather(values, "col", axis=0, tiled=True)


def out_project(attended, weight):
    whole = lax.all_gather(attended, "row", axis=0, tiled=True)
    return lax.psum_scatter(
        jnp.dot(whole, weight, preferred_element_type=jnp.float32).astype(jnp.bfloat16),
        "col",
        scatter_dimension=0,
        tiled=True,
    ).astype(jnp.float32)


def split_heads(values):
    return values.reshape(values.shape[0], values.shape[1] // HD, HD)


def attend_block(queries, keys, values, allowed):
    query_heads = split_heads(queries)
    scores = jnp.einsum(
        "qhd,khd->hqk", query_heads, split_heads(keys), preferred_element_type=jnp.float32
    ) * HD ** (-0.5)
    scores = jnp.where(allowed[None], scores, -1e30)
    peak = jnp.max(scores, axis=-1, keepdims=True)
    weights = jnp.where(allowed[None], jnp.exp(scores - peak), 0.0)
    mass = jnp.sum(weights, axis=-1)
    summed = jnp.einsum(
        "hqk,khd->qhd",
        weights.astype(jnp.bfloat16),
        split_heads(values),
        preferred_element_type=jnp.float32,
    )
    result = summed / jnp.transpose(mass)[:, :, None]
    return result.reshape(queries.shape[0], queries.shape[1]).astype(jnp.bfloat16)


def fold_step(carry, query_heads, query_slots, key_heads, value_heads):
    peak, mass, accum = carry
    piece_slots = jnp.arange(key_heads.shape[0], dtype=jnp.int32)
    allowed = query_slots[:, None] >= piece_slots[None, :]
    scores = jnp.einsum(
        "qhd,khd->hqk", query_heads, key_heads, preferred_element_type=jnp.float32
    ) * HD ** (-0.5)
    scores = jnp.where(allowed[None], scores, -1e30)
    new_peak = jnp.maximum(peak, jnp.max(scores, axis=-1))
    weights = jnp.where(allowed[None], jnp.exp(scores - new_peak[:, :, None]), 0.0)
    summed = jnp.einsum(
        "hqk,khd->hqd",
        weights.astype(jnp.bfloat16),
        value_heads,
        preferred_element_type=jnp.float32,
    )
    return (new_peak, jnp.sum(weights, axis=-1), summed)


def start_state(head_count, query_count):
    return (
        jnp.full((head_count, query_count), -1e30, jnp.float32),
        jnp.zeros((head_count, query_count), jnp.float32),
        jnp.zeros((head_count, query_count, HD), jnp.float32),
    )


def head_project(values, weights):
    row_count = lax.axis_size("row")
    width = weights[0].shape[1]
    depth = weights[0].shape[0]
    shaped = jnp.stack(
        [w.reshape(depth, row_count, width // row_count) for w in weights], axis=2
    ).reshape(depth, row_count, len(weights) * (width // row_count))
    summed = jnp.einsum("tf,frc->rtc", values, shaped, preferred_element_type=jnp.float32)
    summed = summed.astype(jnp.bfloat16).reshape(row_count * values.shape[0], -1)
    return lax.psum_scatter(summed, "row", scatter_dimension=0, tiled=True)


def out_project_heads(attended, weight):
    row_count = lax.axis_size("row")
    whole = lax.all_gather(attended, "row", axis=0, tiled=False)
    shaped = weight.reshape(row_count, weight.shape[0] // row_count, weight.shape[1])
    summed = jnp.einsum("rtf,rfo->to", whole, shaped, preferred_element_type=jnp.float32)
    return lax.psum_scatter(
        summed.astype(jnp.bfloat16), "col", scatter_dimension=0, tiled=True
    ).astype(jnp.float32)


def causal_attend(proj, keyvals, base, key_tile=512):
    count = proj.shape[0]
    heads = proj.shape[1] // (3 * HD)
    total = keyvals.shape[0]
    steps = total // key_tile
    scale = HD ** (-0.5)

    def body(base_ref, q_ref, k_ref, v_ref, o_ref, peak_ref, mass_ref, acc_ref):
        step = pl.program_id(1)
        first = base_ref[0]

        @pl.when(step == 0)
        def _():
            peak_ref[...] = jnp.full(peak_ref.shape, -1e30, jnp.float32)
            mass_ref[...] = jnp.zeros(mass_ref.shape, jnp.float32)
            acc_ref[...] = jnp.zeros(acc_ref.shape, jnp.float32)

        def fold(masked):
            scores = lax.dot_general(
                q_ref[...], k_ref[...], (((1,), (1,)), ((), ())),
                preferred_element_type=jnp.float32) * scale
            if masked:
                rows = first + lax.broadcasted_iota(jnp.int32, scores.shape, 0)
                cols = step * key_tile + lax.broadcasted_iota(jnp.int32, scores.shape, 1)
                allowed = cols <= rows
                scores = jnp.where(allowed, scores, -1e30)
            old = peak_ref[...]
            new = jnp.maximum(old, jnp.max(scores, axis=1, keepdims=True))
            weights = jnp.exp(scores - new)
            if masked:
                weights = jnp.where(allowed, weights, 0.0)
            shrink = jnp.exp(old - new)
            mass_ref[...] = shrink * mass_ref[...] + jnp.sum(weights, axis=1, keepdims=True)
            acc_ref[...] = shrink * acc_ref[...] + jnp.dot(
                weights.astype(jnp.bfloat16), v_ref[...], preferred_element_type=jnp.float32)
            peak_ref[...] = new

        start = step * key_tile
        end = start + key_tile - 1

        @pl.when(end <= first)
        def _():
            fold(False)

        @pl.when((end > first) & (start <= first + count - 1))
        def _():
            fold(True)

        @pl.when(step == steps - 1)
        def _():
            o_ref[...] = (acc_ref[...] / mass_ref[...]).astype(o_ref.dtype)

    grid_spec = pltpu.PrefetchScalarGridSpec(
        num_scalar_prefetch=1,
        grid=(heads, steps),
        in_specs=[
            pl.BlockSpec((count, HD), lambda h, j, b: (0, h)),
            pl.BlockSpec((key_tile, HD), lambda h, j, b: (j, h)),
            pl.BlockSpec((key_tile, HD), lambda h, j, b: (j, heads + h)),
        ],
        out_specs=pl.BlockSpec((count, HD), lambda h, j, b: (0, h)),
        scratch_shapes=[
            pltpu.VMEM((count, 1), jnp.float32),
            pltpu.VMEM((count, 1), jnp.float32),
            pltpu.VMEM((count, HD), jnp.float32),
        ],
    )
    return pl.pallas_call(
        body,
        grid_spec=grid_spec,
        out_shape=jax.ShapeDtypeStruct((count, heads * HD), jnp.bfloat16),
    )(base, proj, keyvals, keyvals)


def per_device(
    text_embed,
    vis_embed,
    vis_segment,
    vis_valid,
    vis_gain,
    vis_wq,
    vis_wk,
    vis_wv,
    vis_wo,
    dec_gain,
    dec_wq,
    dec_wk,
    dec_wv,
    dec_wo,
):
    row_count = lax.axis_size("row")
    col_count = lax.axis_size("col")
    width = vis_wq.shape[1]
    local = width // row_count
    margin = MAXIMG - 1
    piece_ids = lax.all_gather(jnp.stack([vis_segment, vis_valid]), "col", axis=1, tiled=True)
    piece_len = piece_ids.shape[1]
    framed_ids = with_halo(piece_ids, (("req", 1),), margin)
    total_slots = piece_len * lax.axis_size("req")
    prompt_rows = text_embed.shape[0]
    prompt_total = prompt_rows * lax.axis_size("req") * col_count
    window_len = piece_len + 2 * margin
    window_start = lax.axis_index("req") * piece_len - margin
    window_index = jnp.arange(window_len, dtype=jnp.int32)
    key_slots = window_start + window_index
    inside = (key_slots >= 0) & (key_slots < total_slots)
    key_segment = framed_ids[0]
    key_valid = framed_ids[1]
    begins = jnp.concatenate([jnp.ones((1,), jnp.bool_), key_segment[1:] != key_segment[:-1]])
    begins = begins | (key_slots == 0)
    image_first = lax.cummax(jnp.where(begins, key_slots, window_start), axis=0)
    target_window = image_first * prompt_total // total_slots + key_slots - image_first
    vis_cols = gather_cols(norm_local(vis_embed, vis_gain))
    vis_proj = head_project(vis_cols, (vis_wq, vis_wk, vis_wv))
    vis_pairs = jnp.stack([vis_proj[:, local : 2 * local], vis_proj[:, 2 * local :]])
    framed = with_halo(vis_pairs, (("req", 1),), margin)
    query_local = margin + jnp.arange(piece_len, dtype=jnp.int32)
    query_slots = window_start + query_local
    query_segment = key_segment[query_local]
    seen = (
        inside[None, :]
        & (query_segment[:, None] == key_segment[None, :])
        & ((key_valid[None, :] == 1) | (query_slots[:, None] == key_slots[None, :]))
    )
    vis_att = attend_block(vis_proj[:, :local], framed[0], framed[1], seen)
    vis_out = (vis_embed.astype(jnp.float32) + out_project_heads(vis_att, vis_wo)).astype(
        jnp.bfloat16
    )
    device_place = lax.axis_index("req") * col_count + lax.axis_index("col")
    owned = device_place * prompt_rows + jnp.arange(prompt_rows, dtype=jnp.int32)
    slot_rows = vis_out.shape[0]
    following = passed_along(vis_out, ("req", "col"), -1)
    near_rows = jnp.concatenate([vis_out, following], axis=0)
    near_local = (
        margin + lax.axis_index("col") * slot_rows + jnp.arange(2 * slot_rows, dtype=jnp.int32)
    )
    near_slots = window_start + near_local
    present = near_slots < total_slots
    near_target = jnp.where(present, target_window[near_local], -1)
    near_valid = key_valid[near_local]
    onehot = ((owned[:, None] == near_target[None, :]) & (near_valid[None, :] == 1)).astype(
        jnp.bfloat16
    )
    carried = jnp.dot(onehot, near_rows, preferred_element_type=jnp.float32)
    mixed = (text_embed.astype(jnp.float32) + carried).astype(jnp.bfloat16)
    dec_cols = gather_cols(norm_local(mixed, dec_gain))
    dec_proj = head_project(dec_cols, (dec_wq, dec_wk, dec_wv))
    dec_rows = dec_cols.shape[0]
    piece = lax.all_gather(dec_proj[:, local:], "req", axis=0, tiled=True)
    base = (lax.axis_index("req") * dec_rows).astype(jnp.int32).reshape(1)
    dec_att = causal_attend(dec_proj, piece, base)
    return (mixed.astype(jnp.float32) + out_project_heads(dec_att, dec_wo)).astype(jnp.bfloat16)


def solution(mesh):
    return jax.shard_map(
        per_device,
        mesh=mesh,
        in_specs=(
            P(("req", "col"), "row"),
            P(("req", "col"), "row"),
            P(("req", "col")),
            P(("req", "col")),
            P("row"),
            P("row", "col"),
            P("row", "col"),
            P("row", "col"),
            P("col", "row"),
            P("row"),
            P("row", "col"),
            P("row", "col"),
            P("row", "col"),
            P("col", "row"),
        ),
        out_specs=P(("req", "col"), "row"),
        check_vma=False,
    )
```

```python
import jax
import jax.numpy as jnp
from jax import lax
from jax.sharding import PartitionSpec as P
from jax.experimental import pallas as pl
from jax.experimental.pallas import tpu as pltpu

D = 4096
HD = 128
MAXIMG = 256


def with_halo(cells, sides, width):
    for axis, dim in sides:
        count = lax.axis_size(axis)
        ends = count - 1
        head = lax.slice_in_dim(cells, 0, width, axis=dim)
        tail = lax.slice_in_dim(cells, cells.shape[dim] - width, cells.shape[dim], axis=dim)
        cells = jnp.concatenate(
            [
                lax.ppermute(tail, axis, [(i, (i + 1) % count) for i in range(ends)]),
                cells,
                lax.ppermute(head, axis, [((i + 1) % count, i) for i in range(ends)]),
            ],
            axis=dim,
        )
    return cells


def passed_along(shard, axis, by):
    size = lax.axis_size(axis)
    pairs = [(i, i + by) for i in range(size) if 0 <= i + by < size]
    return lax.ppermute(shard, axis, pairs)


def norm_local(values, gain):
    floats = values.astype(jnp.float32)
    squares = jnp.sum(floats * floats, axis=-1)
    totals = lax.psum(squares, "row")
    factor = lax.rsqrt(totals / D + 1e-05)
    return (floats * factor[:, None] * gain.astype(jnp.float32)[None, :]).astype(jnp.bfloat16)


def gather_cols(values):
    return lax.all_gather(values, "col", axis=0, tiled=True)


def out_project(attended, weight):
    whole = lax.all_gather(attended, "row", axis=0, tiled=True)
    return lax.psum_scatter(
        jnp.dot(whole, weight, preferred_element_type=jnp.float32).astype(jnp.bfloat16),
        "col",
        scatter_dimension=0,
        tiled=True,
    ).astype(jnp.float32)


def split_heads(values):
    return values.reshape(values.shape[0], values.shape[1] // HD, HD)


def attend_block(queries, keys, values, allowed):
    query_heads = split_heads(queries)
    scores = jnp.einsum(
        "qhd,khd->hqk", query_heads, split_heads(keys), preferred_element_type=jnp.float32
    ) * HD ** (-0.5)
    scores = jnp.where(allowed[None], scores, -1e30)
    peak = jnp.max(scores, axis=-1, keepdims=True)
    weights = jnp.where(allowed[None], jnp.exp(scores - peak), 0.0)
    mass = jnp.sum(weights, axis=-1)
    summed = jnp.einsum(
        "hqk,khd->qhd",
        weights.astype(jnp.bfloat16),
        split_heads(values),
        preferred_element_type=jnp.float32,
    )
    result = summed / jnp.transpose(mass)[:, :, None]
    return result.reshape(queries.shape[0], queries.shape[1]).astype(jnp.bfloat16)


def fold_step(carry, query_heads, query_slots, key_heads, value_heads):
    peak, mass, accum = carry
    piece_slots = jnp.arange(key_heads.shape[0], dtype=jnp.int32)
    allowed = query_slots[:, None] >= piece_slots[None, :]
    scores = jnp.einsum(
        "qhd,khd->hqk", query_heads, key_heads, preferred_element_type=jnp.float32
    ) * HD ** (-0.5)
    scores = jnp.where(allowed[None], scores, -1e30)
    new_peak = jnp.maximum(peak, jnp.max(scores, axis=-1))
    weights = jnp.where(allowed[None], jnp.exp(scores - new_peak[:, :, None]), 0.0)
    summed = jnp.einsum(
        "hqk,khd->hqd",
        weights.astype(jnp.bfloat16),
        value_heads,
        preferred_element_type=jnp.float32,
    )
    return (new_peak, jnp.sum(weights, axis=-1), summed)


def start_state(head_count, query_count):
    return (
        jnp.full((head_count, query_count), -1e30, jnp.float32),
        jnp.zeros((head_count, query_count), jnp.float32),
        jnp.zeros((head_count, query_count, HD), jnp.float32),
    )


def head_project(values, weights):
    row_count = lax.axis_size("row")
    count, depth = values.shape
    part = weights[0].shape[1] // row_count
    groups = len(weights)

    def body(x_ref, *refs):
        o_ref = refs[-1]
        for g in range(groups):
            o_ref[0, :, g * part : (g + 1) * part] = jnp.dot(
                x_ref[...], refs[g][...], preferred_element_type=jnp.float32
            ).astype(o_ref.dtype)

    summed = pl.pallas_call(
        body,
        grid=(row_count,),
        in_specs=[pl.BlockSpec((count, depth), lambda r: (0, 0))]
        + [pl.BlockSpec((depth, part), lambda r: (0, r)) for _ in weights],
        out_specs=pl.BlockSpec((1, count, groups * part), lambda r: (r, 0, 0)),
        out_shape=jax.ShapeDtypeStruct((row_count, count, groups * part), jnp.bfloat16),
    )(values, *weights)
    summed = summed.reshape(row_count * count, groups * part)
    return lax.psum_scatter(summed, "row", scatter_dimension=0, tiled=True)


def out_project_heads(attended, weight):
    row_count = lax.axis_size("row")
    whole = lax.all_gather(attended, "row", axis=0, tiled=False)
    shaped = weight.reshape(row_count, weight.shape[0] // row_count, weight.shape[1])
    summed = jnp.einsum("rtf,rfo->to", whole, shaped, preferred_element_type=jnp.float32)
    return lax.psum_scatter(
        summed.astype(jnp.bfloat16), "col", scatter_dimension=0, tiled=True
    ).astype(jnp.float32)


def causal_attend(proj, keyvals, base, key_tile=512):
    count = proj.shape[0]
    heads = proj.shape[1] // (3 * HD)
    total = keyvals.shape[0]
    steps = total // key_tile
    scale = HD ** (-0.5)

    def body(base_ref, q_ref, k_ref, v_ref, o_ref, peak_ref, mass_ref, acc_ref):
        step = pl.program_id(1)
        first = base_ref[0]

        @pl.when(step == 0)
        def _():
            peak_ref[...] = jnp.full(peak_ref.shape, -1e30, jnp.float32)
            mass_ref[...] = jnp.zeros(mass_ref.shape, jnp.float32)
            acc_ref[...] = jnp.zeros(acc_ref.shape, jnp.float32)

        def fold(masked):
            scores = lax.dot_general(
                q_ref[...], k_ref[...], (((1,), (1,)), ((), ())),
                preferred_element_type=jnp.float32) * scale
            if masked:
                rows = first + lax.broadcasted_iota(jnp.int32, scores.shape, 0)
                cols = step * key_tile + lax.broadcasted_iota(jnp.int32, scores.shape, 1)
                allowed = cols <= rows
                scores = jnp.where(allowed, scores, -1e30)
            old = peak_ref[...]
            new = jnp.maximum(old, jnp.max(scores, axis=1, keepdims=True))
            weights = jnp.exp(scores - new)
            if masked:
                weights = jnp.where(allowed, weights, 0.0)
            shrink = jnp.exp(old - new)
            mass_ref[...] = shrink * mass_ref[...] + jnp.sum(weights, axis=1, keepdims=True)
            acc_ref[...] = shrink * acc_ref[...] + jnp.dot(
                weights.astype(jnp.bfloat16), v_ref[...], preferred_element_type=jnp.float32)
            peak_ref[...] = new

        start = step * key_tile
        end = start + key_tile - 1

        @pl.when(end <= first)
        def _():
            fold(False)

        @pl.when((end > first) & (start <= first + count - 1))
        def _():
            fold(True)

        @pl.when(step == steps - 1)
        def _():
            o_ref[...] = (acc_ref[...] / mass_ref[...]).astype(o_ref.dtype)

    grid_spec = pltpu.PrefetchScalarGridSpec(
        num_scalar_prefetch=1,
        grid=(heads, steps),
        in_specs=[
            pl.BlockSpec((count, HD), lambda h, j, b: (0, h)),
            pl.BlockSpec((key_tile, HD), lambda h, j, b: (j, h)),
            pl.BlockSpec((key_tile, HD), lambda h, j, b: (j, heads + h)),
        ],
        out_specs=pl.BlockSpec((count, HD), lambda h, j, b: (0, h)),
        scratch_shapes=[
            pltpu.VMEM((count, 1), jnp.float32),
            pltpu.VMEM((count, 1), jnp.float32),
            pltpu.VMEM((count, HD), jnp.float32),
        ],
    )
    return pl.pallas_call(
        body,
        grid_spec=grid_spec,
        out_shape=jax.ShapeDtypeStruct((count, heads * HD), jnp.bfloat16),
    )(base, proj, keyvals, keyvals)


def per_device(
    text_embed,
    vis_embed,
    vis_segment,
    vis_valid,
    vis_gain,
    vis_wq,
    vis_wk,
    vis_wv,
    vis_wo,
    dec_gain,
    dec_wq,
    dec_wk,
    dec_wv,
    dec_wo,
):
    row_count = lax.axis_size("row")
    col_count = lax.axis_size("col")
    width = vis_wq.shape[1]
    local = width // row_count
    margin = MAXIMG - 1
    piece_ids = lax.all_gather(jnp.stack([vis_segment, vis_valid]), "col", axis=1, tiled=True)
    piece_len = piece_ids.shape[1]
    framed_ids = with_halo(piece_ids, (("req", 1),), margin)
    total_slots = piece_len * lax.axis_size("req")
    prompt_rows = text_embed.shape[0]
    prompt_total = prompt_rows * lax.axis_size("req") * col_count
    window_len = piece_len + 2 * margin
    window_start = lax.axis_index("req") * piece_len - margin
    window_index = jnp.arange(window_len, dtype=jnp.int32)
    key_slots = window_start + window_index
    inside = (key_slots >= 0) & (key_slots < total_slots)
    key_segment = framed_ids[0]
    key_valid = framed_ids[1]
    begins = jnp.concatenate([jnp.ones((1,), jnp.bool_), key_segment[1:] != key_segment[:-1]])
    begins = begins | (key_slots == 0)
    image_first = lax.cummax(jnp.where(begins, key_slots, window_start), axis=0)
    target_window = image_first * prompt_total // total_slots + key_slots - image_first
    vis_cols = gather_cols(norm_local(vis_embed, vis_gain))
    vis_proj = head_project(vis_cols, (vis_wq, vis_wk, vis_wv))
    vis_pairs = jnp.stack([vis_proj[:, local : 2 * local], vis_proj[:, 2 * local :]])
    framed = with_halo(vis_pairs, (("req", 1),), margin)
    query_local = margin + jnp.arange(piece_len, dtype=jnp.int32)
    query_slots = window_start + query_local
    query_segment = key_segment[query_local]
    seen = (
        inside[None, :]
        & (query_segment[:, None] == key_segment[None, :])
        & ((key_valid[None, :] == 1) | (query_slots[:, None] == key_slots[None, :]))
    )
    vis_att = attend_block(vis_proj[:, :local], framed[0], framed[1], seen)
    vis_out = (vis_embed.astype(jnp.float32) + out_project_heads(vis_att, vis_wo)).astype(
        jnp.bfloat16
    )
    device_place = lax.axis_index("req") * col_count + lax.axis_index("col")
    owned = device_place * prompt_rows + jnp.arange(prompt_rows, dtype=jnp.int32)
    slot_rows = vis_out.shape[0]
    following = passed_along(vis_out, ("req", "col"), -1)
    near_rows = jnp.concatenate([vis_out, following], axis=0)
    near_local = (
        margin + lax.axis_index("col") * slot_rows + jnp.arange(2 * slot_rows, dtype=jnp.int32)
    )
    near_slots = window_start + near_local
    present = near_slots < total_slots
    near_target = jnp.where(present, target_window[near_local], -1)
    near_valid = key_valid[near_local]
    onehot = ((owned[:, None] == near_target[None, :]) & (near_valid[None, :] == 1)).astype(
        jnp.bfloat16
    )
    carried = jnp.dot(onehot, near_rows, preferred_element_type=jnp.float32)
    mixed = (text_embed.astype(jnp.float32) + carried).astype(jnp.bfloat16)
    dec_cols = gather_cols(norm_local(mixed, dec_gain))
    dec_proj = head_project(dec_cols, (dec_wq, dec_wk, dec_wv))
    dec_rows = dec_cols.shape[0]
    piece = lax.all_gather(dec_proj[:, local:], "req", axis=0, tiled=True)
    base = (lax.axis_index("req") * dec_rows).astype(jnp.int32).reshape(1)
    dec_att = causal_attend(dec_proj, piece, base)
    return (mixed.astype(jnp.float32) + out_project_heads(dec_att, dec_wo)).astype(jnp.bfloat16)


def solution(mesh):
    return jax.shard_map(
        per_device,
        mesh=mesh,
        in_specs=(
            P(("req", "col"), "row"),
            P(("req", "col"), "row"),
            P(("req", "col")),
            P(("req", "col")),
            P("row"),
            P("row", "col"),
            P("row", "col"),
            P("row", "col"),
            P("col", "row"),
            P("row"),
            P("row", "col"),
            P("row", "col"),
            P("row", "col"),
            P("col", "row"),
        ),
        out_specs=P(("req", "col"), "row"),
        check_vma=False,
    )
```

```python
import jax
import jax.numpy as jnp
from jax import lax
from jax.sharding import PartitionSpec as P
from jax.experimental import pallas as pl
from jax.experimental.pallas import tpu as pltpu

D = 4096
HD = 128
MAXIMG = 256


def with_halo(cells, sides, width):
    for axis, dim in sides:
        count = lax.axis_size(axis)
        ends = count - 1
        head = lax.slice_in_dim(cells, 0, width, axis=dim)
        tail = lax.slice_in_dim(cells, cells.shape[dim] - width, cells.shape[dim], axis=dim)
        cells = jnp.concatenate(
            [
                lax.ppermute(tail, axis, [(i, (i + 1) % count) for i in range(ends)]),
                cells,
                lax.ppermute(head, axis, [((i + 1) % count, i) for i in range(ends)]),
            ],
            axis=dim,
        )
    return cells


def passed_along(shard, axis, by):
    size = lax.axis_size(axis)
    pairs = [(i, i + by) for i in range(size) if 0 <= i + by < size]
    return lax.ppermute(shard, axis, pairs)


def norm_local(values, gain):
    floats = values.astype(jnp.float32)
    squares = jnp.sum(floats * floats, axis=-1)
    totals = lax.psum(squares, "row")
    factor = lax.rsqrt(totals / D + 1e-05)
    return (floats * factor[:, None] * gain.astype(jnp.float32)[None, :]).astype(jnp.bfloat16)


def gather_permute(values, axis):
    count = lax.axis_size(axis)
    index = lax.axis_index(axis)
    rows = values.shape[0]
    got = [values] + [
        lax.ppermute(values, axis, [(j, (j + s) % count) for j in range(count)])
        for s in range(1, count)
    ]
    ahead = jnp.concatenate([got[0]] + got[:0:-1], axis=0)
    twice = jnp.concatenate([ahead, ahead], axis=0)
    start = ((count - index) % count) * rows
    return lax.dynamic_slice_in_dim(twice, start, count * rows, axis=0)


def scatter_permute(values, axis):
    count = lax.axis_size(axis)
    index = lax.axis_index(axis)
    rows = values.shape[0] // count
    total = lax.dynamic_slice_in_dim(values, index * rows, rows, axis=0).astype(jnp.float32)
    for s in range(1, count):
        chunk = lax.dynamic_slice_in_dim(values, ((index + s) % count) * rows, rows, axis=0)
        total = total + lax.ppermute(
            chunk, axis, [(j, (j + s) % count) for j in range(count)]
        ).astype(jnp.float32)
    return total


def gather_cols(values):
    return gather_permute(values, "col")


def out_project(attended, weight):
    whole = lax.all_gather(attended, "row", axis=0, tiled=True)
    return lax.psum_scatter(
        jnp.dot(whole, weight, preferred_element_type=jnp.float32).astype(jnp.bfloat16),
        "col",
        scatter_dimension=0,
        tiled=True,
    ).astype(jnp.float32)


def split_heads(values):
    return values.reshape(values.shape[0], values.shape[1] // HD, HD)


def attend_block(queries, keys, values, allowed):
    query_heads = split_heads(queries)
    scores = jnp.einsum(
        "qhd,khd->hqk", query_heads, split_heads(keys), preferred_element_type=jnp.float32
    ) * HD ** (-0.5)
    scores = jnp.where(allowed[None], scores, -1e30)
    peak = jnp.max(scores, axis=-1, keepdims=True)
    weights = jnp.where(allowed[None], jnp.exp(scores - peak), 0.0)
    mass = jnp.sum(weights, axis=-1)
    summed = jnp.einsum(
        "hqk,khd->qhd",
        weights.astype(jnp.bfloat16),
        split_heads(values),
        preferred_element_type=jnp.float32,
    )
    result = summed / jnp.transpose(mass)[:, :, None]
    return result.reshape(queries.shape[0], queries.shape[1]).astype(jnp.bfloat16)


def fold_step(carry, query_heads, query_slots, key_heads, value_heads):
    peak, mass, accum = carry
    piece_slots = jnp.arange(key_heads.shape[0], dtype=jnp.int32)
    allowed = query_slots[:, None] >= piece_slots[None, :]
    scores = jnp.einsum(
        "qhd,khd->hqk", query_heads, key_heads, preferred_element_type=jnp.float32
    ) * HD ** (-0.5)
    scores = jnp.where(allowed[None], scores, -1e30)
    new_peak = jnp.maximum(peak, jnp.max(scores, axis=-1))
    weights = jnp.where(allowed[None], jnp.exp(scores - new_peak[:, :, None]), 0.0)
    summed = jnp.einsum(
        "hqk,khd->hqd",
        weights.astype(jnp.bfloat16),
        value_heads,
        preferred_element_type=jnp.float32,
    )
    return (new_peak, jnp.sum(weights, axis=-1), summed)


def start_state(head_count, query_count):
    return (
        jnp.full((head_count, query_count), -1e30, jnp.float32),
        jnp.zeros((head_count, query_count), jnp.float32),
        jnp.zeros((head_count, query_count, HD), jnp.float32),
    )


def head_project(values, weights):
    row_count = lax.axis_size("row")
    count, depth = values.shape
    part = weights[0].shape[1] // row_count
    groups = len(weights)

    def body(x_ref, *refs):
        o_ref = refs[-1]
        for g in range(groups):
            o_ref[0, :, g * part : (g + 1) * part] = jnp.dot(
                x_ref[...], refs[g][...], preferred_element_type=jnp.float32
            ).astype(o_ref.dtype)

    summed = pl.pallas_call(
        body,
        grid=(row_count,),
        in_specs=[pl.BlockSpec((count, depth), lambda r: (0, 0))]
        + [pl.BlockSpec((depth, part), lambda r: (0, r)) for _ in weights],
        out_specs=pl.BlockSpec((1, count, groups * part), lambda r: (r, 0, 0)),
        out_shape=jax.ShapeDtypeStruct((row_count, count, groups * part), jnp.bfloat16),
    )(values, *weights)
    summed = summed.reshape(row_count * count, groups * part)
    return lax.psum_scatter(summed, "row", scatter_dimension=0, tiled=True)


def out_project_heads(attended, weight):
    row_count = lax.axis_size("row")
    whole = lax.all_gather(attended, "row", axis=0, tiled=False)
    shaped = weight.reshape(row_count, weight.shape[0] // row_count, weight.shape[1])
    summed = jnp.einsum("rtf,rfo->to", whole, shaped, preferred_element_type=jnp.float32)
    return scatter_permute(summed.astype(jnp.bfloat16), "col")


def causal_attend(proj, keyvals, base, key_tile=512):
    count = proj.shape[0]
    heads = proj.shape[1] // (3 * HD)
    total = keyvals.shape[0]
    steps = total // key_tile
    scale = HD ** (-0.5)

    def body(base_ref, q_ref, k_ref, v_ref, o_ref, peak_ref, mass_ref, acc_ref):
        step = pl.program_id(1)
        first = base_ref[0]

        @pl.when(step == 0)
        def _():
            peak_ref[...] = jnp.full(peak_ref.shape, -1e30, jnp.float32)
            mass_ref[...] = jnp.zeros(mass_ref.shape, jnp.float32)
            acc_ref[...] = jnp.zeros(acc_ref.shape, jnp.float32)

        def fold(masked):
            scores = lax.dot_general(
                q_ref[...], k_ref[...], (((1,), (1,)), ((), ())),
                preferred_element_type=jnp.float32) * scale
            if masked:
                rows = first + lax.broadcasted_iota(jnp.int32, scores.shape, 0)
                cols = step * key_tile + lax.broadcasted_iota(jnp.int32, scores.shape, 1)
                allowed = cols <= rows
                scores = jnp.where(allowed, scores, -1e30)
            old = peak_ref[...]
            new = jnp.maximum(old, jnp.max(scores, axis=1, keepdims=True))
            weights = jnp.exp(scores - new)
            if masked:
                weights = jnp.where(allowed, weights, 0.0)
            shrink = jnp.exp(old - new)
            mass_ref[...] = shrink * mass_ref[...] + jnp.sum(weights, axis=1, keepdims=True)
            acc_ref[...] = shrink * acc_ref[...] + jnp.dot(
                weights.astype(jnp.bfloat16), v_ref[...], preferred_element_type=jnp.float32)
            peak_ref[...] = new

        start = step * key_tile
        end = start + key_tile - 1

        @pl.when(end <= first)
        def _():
            fold(False)

        @pl.when((end > first) & (start <= first + count - 1))
        def _():
            fold(True)

        @pl.when(step == steps - 1)
        def _():
            o_ref[...] = (acc_ref[...] / mass_ref[...]).astype(o_ref.dtype)

    grid_spec = pltpu.PrefetchScalarGridSpec(
        num_scalar_prefetch=1,
        grid=(heads, steps),
        in_specs=[
            pl.BlockSpec((count, HD), lambda h, j, b: (0, h)),
            pl.BlockSpec((key_tile, HD), lambda h, j, b: (j, h)),
            pl.BlockSpec((key_tile, HD), lambda h, j, b: (j, heads + h)),
        ],
        out_specs=pl.BlockSpec((count, HD), lambda h, j, b: (0, h)),
        scratch_shapes=[
            pltpu.VMEM((count, 1), jnp.float32),
            pltpu.VMEM((count, 1), jnp.float32),
            pltpu.VMEM((count, HD), jnp.float32),
        ],
    )
    return pl.pallas_call(
        body,
        grid_spec=grid_spec,
        out_shape=jax.ShapeDtypeStruct((count, heads * HD), jnp.bfloat16),
    )(base, proj, keyvals, keyvals)


def per_device(
    text_embed,
    vis_embed,
    vis_segment,
    vis_valid,
    vis_gain,
    vis_wq,
    vis_wk,
    vis_wv,
    vis_wo,
    dec_gain,
    dec_wq,
    dec_wk,
    dec_wv,
    dec_wo,
):
    row_count = lax.axis_size("row")
    col_count = lax.axis_size("col")
    width = vis_wq.shape[1]
    local = width // row_count
    margin = MAXIMG - 1
    piece_ids = lax.all_gather(jnp.stack([vis_segment, vis_valid]), "col", axis=1, tiled=True)
    piece_len = piece_ids.shape[1]
    framed_ids = with_halo(piece_ids, (("req", 1),), margin)
    total_slots = piece_len * lax.axis_size("req")
    prompt_rows = text_embed.shape[0]
    prompt_total = prompt_rows * lax.axis_size("req") * col_count
    window_len = piece_len + 2 * margin
    window_start = lax.axis_index("req") * piece_len - margin
    window_index = jnp.arange(window_len, dtype=jnp.int32)
    key_slots = window_start + window_index
    inside = (key_slots >= 0) & (key_slots < total_slots)
    key_segment = framed_ids[0]
    key_valid = framed_ids[1]
    begins = jnp.concatenate([jnp.ones((1,), jnp.bool_), key_segment[1:] != key_segment[:-1]])
    begins = begins | (key_slots == 0)
    image_first = lax.cummax(jnp.where(begins, key_slots, window_start), axis=0)
    target_window = image_first * prompt_total // total_slots + key_slots - image_first
    vis_cols = gather_cols(norm_local(vis_embed, vis_gain))
    vis_proj = head_project(vis_cols, (vis_wq, vis_wk, vis_wv))
    vis_pairs = jnp.stack([vis_proj[:, local : 2 * local], vis_proj[:, 2 * local :]])
    framed = with_halo(vis_pairs, (("req", 1),), margin)
    query_local = margin + jnp.arange(piece_len, dtype=jnp.int32)
    query_slots = window_start + query_local
    query_segment = key_segment[query_local]
    seen = (
        inside[None, :]
        & (query_segment[:, None] == key_segment[None, :])
        & ((key_valid[None, :] == 1) | (query_slots[:, None] == key_slots[None, :]))
    )
    vis_att = attend_block(vis_proj[:, :local], framed[0], framed[1], seen)
    vis_out = (vis_embed.astype(jnp.float32) + out_project_heads(vis_att, vis_wo)).astype(
        jnp.bfloat16
    )
    device_place = lax.axis_index("req") * col_count + lax.axis_index("col")
    owned = device_place * prompt_rows + jnp.arange(prompt_rows, dtype=jnp.int32)
    slot_rows = vis_out.shape[0]
    following = passed_along(vis_out, ("req", "col"), -1)
    near_rows = jnp.concatenate([vis_out, following], axis=0)
    near_local = (
        margin + lax.axis_index("col") * slot_rows + jnp.arange(2 * slot_rows, dtype=jnp.int32)
    )
    near_slots = window_start + near_local
    present = near_slots < total_slots
    near_target = jnp.where(present, target_window[near_local], -1)
    near_valid = key_valid[near_local]
    onehot = ((owned[:, None] == near_target[None, :]) & (near_valid[None, :] == 1)).astype(
        jnp.bfloat16
    )
    carried = jnp.dot(onehot, near_rows, preferred_element_type=jnp.float32)
    mixed = (text_embed.astype(jnp.float32) + carried).astype(jnp.bfloat16)
    dec_cols = gather_cols(norm_local(mixed, dec_gain))
    dec_proj = head_project(dec_cols, (dec_wq, dec_wk, dec_wv))
    dec_rows = dec_cols.shape[0]
    piece = lax.all_gather(dec_proj[:, local:], "req", axis=0, tiled=True)
    base = (lax.axis_index("req") * dec_rows).astype(jnp.int32).reshape(1)
    dec_att = causal_attend(dec_proj, piece, base)
    return (mixed.astype(jnp.float32) + out_project_heads(dec_att, dec_wo)).astype(jnp.bfloat16)


def solution(mesh):
    return jax.shard_map(
        per_device,
        mesh=mesh,
        in_specs=(
            P(("req", "col"), "row"),
            P(("req", "col"), "row"),
            P(("req", "col")),
            P(("req", "col")),
            P("row"),
            P("row", "col"),
            P("row", "col"),
            P("row", "col"),
            P("col", "row"),
            P("row"),
            P("row", "col"),
            P("row", "col"),
            P("row", "col"),
            P("col", "row"),
        ),
        out_specs=P(("req", "col"), "row"),
        check_vma=False,
    )
```

```python
import jax
import jax.numpy as jnp
from jax import lax
from jax.sharding import PartitionSpec as P
from jax.experimental import pallas as pl
from jax.experimental.pallas import tpu as pltpu

D = 4096
HD = 128
MAXIMG = 256


def with_halo(cells, sides, width):
    for axis, dim in sides:
        count = lax.axis_size(axis)
        ends = count - 1
        head = lax.slice_in_dim(cells, 0, width, axis=dim)
        tail = lax.slice_in_dim(cells, cells.shape[dim] - width, cells.shape[dim], axis=dim)
        cells = jnp.concatenate(
            [
                lax.ppermute(tail, axis, [(i, (i + 1) % count) for i in range(ends)]),
                cells,
                lax.ppermute(head, axis, [((i + 1) % count, i) for i in range(ends)]),
            ],
            axis=dim,
        )
    return cells


def passed_along(shard, axis, by):
    size = lax.axis_size(axis)
    pairs = [(i, i + by) for i in range(size) if 0 <= i + by < size]
    return lax.ppermute(shard, axis, pairs)


def norm_local(values, gain):
    floats = values.astype(jnp.float32)
    squares = jnp.sum(floats * floats, axis=-1)
    totals = lax.psum(squares, "row")
    factor = lax.rsqrt(totals / D + 1e-05)
    return (floats * factor[:, None] * gain.astype(jnp.float32)[None, :]).astype(jnp.bfloat16)


def gather_permute(values, axis):
    count = lax.axis_size(axis)
    index = lax.axis_index(axis)
    rows = values.shape[0]
    got = [values] + [
        lax.ppermute(values, axis, [(j, (j + s) % count) for j in range(count)])
        for s in range(1, count)
    ]
    ahead = jnp.concatenate([got[0]] + got[:0:-1], axis=0)
    twice = jnp.concatenate([ahead, ahead], axis=0)
    start = ((count - index) % count) * rows
    return lax.dynamic_slice_in_dim(twice, start, count * rows, axis=0)


def scatter_permute(values, axis):
    count = lax.axis_size(axis)
    index = lax.axis_index(axis)
    rows = values.shape[0] // count
    total = lax.dynamic_slice_in_dim(values, index * rows, rows, axis=0).astype(jnp.float32)
    for s in range(1, count):
        chunk = lax.dynamic_slice_in_dim(values, ((index + s) % count) * rows, rows, axis=0)
        total = total + lax.ppermute(
            chunk, axis, [(j, (j + s) % count) for j in range(count)]
        ).astype(jnp.float32)
    return total


def gather_cols(values):
    return gather_permute(values, "col")


def out_project(attended, weight):
    whole = lax.all_gather(attended, "row", axis=0, tiled=True)
    return lax.psum_scatter(
        jnp.dot(whole, weight, preferred_element_type=jnp.float32).astype(jnp.bfloat16),
        "col",
        scatter_dimension=0,
        tiled=True,
    ).astype(jnp.float32)


def split_heads(values):
    return values.reshape(values.shape[0], values.shape[1] // HD, HD)


def attend_block(queries, keys, values, allowed):
    query_heads = split_heads(queries)
    scores = jnp.einsum(
        "qhd,khd->hqk", query_heads, split_heads(keys), preferred_element_type=jnp.float32
    ) * HD ** (-0.5)
    scores = jnp.where(allowed[None], scores, -1e30)
    peak = jnp.max(scores, axis=-1, keepdims=True)
    weights = jnp.where(allowed[None], jnp.exp(scores - peak), 0.0)
    mass = jnp.sum(weights, axis=-1)
    summed = jnp.einsum(
        "hqk,khd->qhd",
        weights.astype(jnp.bfloat16),
        split_heads(values),
        preferred_element_type=jnp.float32,
    )
    result = summed / jnp.transpose(mass)[:, :, None]
    return result.reshape(queries.shape[0], queries.shape[1]).astype(jnp.bfloat16)


def fold_step(carry, query_heads, query_slots, key_heads, value_heads):
    peak, mass, accum = carry
    piece_slots = jnp.arange(key_heads.shape[0], dtype=jnp.int32)
    allowed = query_slots[:, None] >= piece_slots[None, :]
    scores = jnp.einsum(
        "qhd,khd->hqk", query_heads, key_heads, preferred_element_type=jnp.float32
    ) * HD ** (-0.5)
    scores = jnp.where(allowed[None], scores, -1e30)
    new_peak = jnp.maximum(peak, jnp.max(scores, axis=-1))
    weights = jnp.where(allowed[None], jnp.exp(scores - new_peak[:, :, None]), 0.0)
    summed = jnp.einsum(
        "hqk,khd->hqd",
        weights.astype(jnp.bfloat16),
        value_heads,
        preferred_element_type=jnp.float32,
    )
    return (new_peak, jnp.sum(weights, axis=-1), summed)


def start_state(head_count, query_count):
    return (
        jnp.full((head_count, query_count), -1e30, jnp.float32),
        jnp.zeros((head_count, query_count), jnp.float32),
        jnp.zeros((head_count, query_count, HD), jnp.float32),
    )


def flip(values, axis, bit):
    count = lax.axis_size(axis)
    return lax.ppermute(values, axis, [(j, j ^ bit) for j in range(count)])


def scatter_row(values):
    count = lax.axis_size("row")
    index = lax.axis_index("row")
    rows = values.shape[0] // count
    chunks = values.reshape(count // 2, 2, rows, values.shape[1])
    mine = lax.dynamic_index_in_dim(chunks, index % 2, axis=1, keepdims=False)
    theirs = lax.dynamic_index_in_dim(chunks, 1 - index % 2, axis=1, keepdims=False)
    paired = (mine.astype(jnp.float32) + flip(theirs, "row", 1).astype(jnp.float32))
    paired = paired.astype(jnp.bfloat16)
    keep = lax.dynamic_index_in_dim(paired, index // 2, axis=0, keepdims=False)
    send = lax.dynamic_index_in_dim(paired, 1 - index // 2, axis=0, keepdims=False)
    return (keep.astype(jnp.float32) + flip(send, "row", 2).astype(jnp.float32)).astype(
        jnp.bfloat16
    )


def gather_row(values):
    count = lax.axis_size("row")
    index = lax.axis_index("row")
    got = [values] + [flip(values, "row", b) for b in range(1, count)]
    stacked = jnp.stack(got)
    order = jnp.arange(count, dtype=jnp.int32) ^ index
    return jnp.take(stacked, order, axis=0)


def head_project(values, weights):
    row_count = lax.axis_size("row")
    count, depth = values.shape
    part = weights[0].shape[1] // row_count
    groups = len(weights)

    def body(x_ref, *refs):
        o_ref = refs[-1]
        for g in range(groups):
            o_ref[0, :, g * part : (g + 1) * part] = jnp.dot(
                x_ref[...], refs[g][...], preferred_element_type=jnp.float32
            ).astype(o_ref.dtype)

    summed = pl.pallas_call(
        body,
        grid=(row_count,),
        in_specs=[pl.BlockSpec((count, depth), lambda r: (0, 0))]
        + [pl.BlockSpec((depth, part), lambda r: (0, r)) for _ in weights],
        out_specs=pl.BlockSpec((1, count, groups * part), lambda r: (r, 0, 0)),
        out_shape=jax.ShapeDtypeStruct((row_count, count, groups * part), jnp.bfloat16),
    )(values, *weights)
    summed = summed.reshape(row_count * count, groups * part)
    return scatter_row(summed)


def out_project_heads(attended, weight):
    row_count = lax.axis_size("row")
    whole = gather_row(attended)
    shaped = weight.reshape(row_count, weight.shape[0] // row_count, weight.shape[1])
    summed = jnp.einsum("rtf,rfo->to", whole, shaped, preferred_element_type=jnp.float32)
    return scatter_permute(summed.astype(jnp.bfloat16), "col")


def causal_attend(proj, keyvals, base, key_tile=512):
    count = proj.shape[0]
    heads = proj.shape[1] // (3 * HD)
    total = keyvals.shape[0]
    steps = total // key_tile
    scale = HD ** (-0.5)

    def body(base_ref, q_ref, k_ref, v_ref, o_ref, peak_ref, mass_ref, acc_ref):
        step = pl.program_id(1)
        first = base_ref[0]

        @pl.when(step == 0)
        def _():
            peak_ref[...] = jnp.full(peak_ref.shape, -1e30, jnp.float32)
            mass_ref[...] = jnp.zeros(mass_ref.shape, jnp.float32)
            acc_ref[...] = jnp.zeros(acc_ref.shape, jnp.float32)

        def fold(masked):
            scores = lax.dot_general(
                q_ref[...], k_ref[...], (((1,), (1,)), ((), ())),
                preferred_element_type=jnp.float32) * scale
            if masked:
                rows = first + lax.broadcasted_iota(jnp.int32, scores.shape, 0)
                cols = step * key_tile + lax.broadcasted_iota(jnp.int32, scores.shape, 1)
                allowed = cols <= rows
                scores = jnp.where(allowed, scores, -1e30)
            old = peak_ref[...]
            new = jnp.maximum(old, jnp.max(scores, axis=1, keepdims=True))
            weights = jnp.exp(scores - new)
            if masked:
                weights = jnp.where(allowed, weights, 0.0)
            shrink = jnp.exp(old - new)
            mass_ref[...] = shrink * mass_ref[...] + jnp.sum(weights, axis=1, keepdims=True)
            acc_ref[...] = shrink * acc_ref[...] + jnp.dot(
                weights.astype(jnp.bfloat16), v_ref[...], preferred_element_type=jnp.float32)
            peak_ref[...] = new

        start = step * key_tile
        end = start + key_tile - 1

        @pl.when(end <= first)
        def _():
            fold(False)

        @pl.when((end > first) & (start <= first + count - 1))
        def _():
            fold(True)

        @pl.when(step == steps - 1)
        def _():
            o_ref[...] = (acc_ref[...] / mass_ref[...]).astype(o_ref.dtype)

    grid_spec = pltpu.PrefetchScalarGridSpec(
        num_scalar_prefetch=1,
        grid=(heads, steps),
        in_specs=[
            pl.BlockSpec((count, HD), lambda h, j, b: (0, h)),
            pl.BlockSpec((key_tile, HD), lambda h, j, b: (j, h)),
            pl.BlockSpec((key_tile, HD), lambda h, j, b: (j, heads + h)),
        ],
        out_specs=pl.BlockSpec((count, HD), lambda h, j, b: (0, h)),
        scratch_shapes=[
            pltpu.VMEM((count, 1), jnp.float32),
            pltpu.VMEM((count, 1), jnp.float32),
            pltpu.VMEM((count, HD), jnp.float32),
        ],
    )
    return pl.pallas_call(
        body,
        grid_spec=grid_spec,
        out_shape=jax.ShapeDtypeStruct((count, heads * HD), jnp.bfloat16),
    )(base, proj, keyvals, keyvals)


def per_device(
    text_embed,
    vis_embed,
    vis_segment,
    vis_valid,
    vis_gain,
    vis_wq,
    vis_wk,
    vis_wv,
    vis_wo,
    dec_gain,
    dec_wq,
    dec_wk,
    dec_wv,
    dec_wo,
):
    row_count = lax.axis_size("row")
    col_count = lax.axis_size("col")
    width = vis_wq.shape[1]
    local = width // row_count
    margin = MAXIMG - 1
    piece_ids = lax.all_gather(jnp.stack([vis_segment, vis_valid]), "col", axis=1, tiled=True)
    piece_len = piece_ids.shape[1]
    framed_ids = with_halo(piece_ids, (("req", 1),), margin)
    total_slots = piece_len * lax.axis_size("req")
    prompt_rows = text_embed.shape[0]
    prompt_total = prompt_rows * lax.axis_size("req") * col_count
    window_len = piece_len + 2 * margin
    window_start = lax.axis_index("req") * piece_len - margin
    window_index = jnp.arange(window_len, dtype=jnp.int32)
    key_slots = window_start + window_index
    inside = (key_slots >= 0) & (key_slots < total_slots)
    key_segment = framed_ids[0]
    key_valid = framed_ids[1]
    begins = jnp.concatenate([jnp.ones((1,), jnp.bool_), key_segment[1:] != key_segment[:-1]])
    begins = begins | (key_slots == 0)
    image_first = lax.cummax(jnp.where(begins, key_slots, window_start), axis=0)
    target_window = image_first * prompt_total // total_slots + key_slots - image_first
    vis_cols = gather_cols(norm_local(vis_embed, vis_gain))
    vis_proj = head_project(vis_cols, (vis_wq, vis_wk, vis_wv))
    vis_pairs = jnp.stack([vis_proj[:, local : 2 * local], vis_proj[:, 2 * local :]])
    framed = with_halo(vis_pairs, (("req", 1),), margin)
    query_local = margin + jnp.arange(piece_len, dtype=jnp.int32)
    query_slots = window_start + query_local
    query_segment = key_segment[query_local]
    seen = (
        inside[None, :]
        & (query_segment[:, None] == key_segment[None, :])
        & ((key_valid[None, :] == 1) | (query_slots[:, None] == key_slots[None, :]))
    )
    vis_att = attend_block(vis_proj[:, :local], framed[0], framed[1], seen)
    vis_out = (vis_embed.astype(jnp.float32) + out_project_heads(vis_att, vis_wo)).astype(
        jnp.bfloat16
    )
    device_place = lax.axis_index("req") * col_count + lax.axis_index("col")
    owned = device_place * prompt_rows + jnp.arange(prompt_rows, dtype=jnp.int32)
    slot_rows = vis_out.shape[0]
    following = passed_along(vis_out, ("req", "col"), -1)
    near_rows = jnp.concatenate([vis_out, following], axis=0)
    near_local = (
        margin + lax.axis_index("col") * slot_rows + jnp.arange(2 * slot_rows, dtype=jnp.int32)
    )
    near_slots = window_start + near_local
    present = near_slots < total_slots
    near_target = jnp.where(present, target_window[near_local], -1)
    near_valid = key_valid[near_local]
    onehot = ((owned[:, None] == near_target[None, :]) & (near_valid[None, :] == 1)).astype(
        jnp.bfloat16
    )
    carried = jnp.dot(onehot, near_rows, preferred_element_type=jnp.float32)
    mixed = (text_embed.astype(jnp.float32) + carried).astype(jnp.bfloat16)
    dec_cols = gather_cols(norm_local(mixed, dec_gain))
    dec_proj = head_project(dec_cols, (dec_wq, dec_wk, dec_wv))
    dec_rows = dec_cols.shape[0]
    piece = lax.all_gather(dec_proj[:, local:], "req", axis=0, tiled=True)
    base = (lax.axis_index("req") * dec_rows).astype(jnp.int32).reshape(1)
    dec_att = causal_attend(dec_proj, piece, base)
    return (mixed.astype(jnp.float32) + out_project_heads(dec_att, dec_wo)).astype(jnp.bfloat16)


def solution(mesh):
    return jax.shard_map(
        per_device,
        mesh=mesh,
        in_specs=(
            P(("req", "col"), "row"),
            P(("req", "col"), "row"),
            P(("req", "col")),
            P(("req", "col")),
            P("row"),
            P("row", "col"),
            P("row", "col"),
            P("row", "col"),
            P("col", "row"),
            P("row"),
            P("row", "col"),
            P("row", "col"),
            P("row", "col"),
            P("col", "row"),
        ),
        out_specs=P(("req", "col"), "row"),
        check_vma=False,
    )
```

```python
import jax
import jax.numpy as jnp
from jax import lax
from jax.sharding import PartitionSpec as P
from jax.experimental import pallas as pl
from jax.experimental.pallas import tpu as pltpu

D = 4096
HD = 128
MAXIMG = 256


def with_halo(cells, sides, width):
    for axis, dim in sides:
        count = lax.axis_size(axis)
        ends = count - 1
        head = lax.slice_in_dim(cells, 0, width, axis=dim)
        tail = lax.slice_in_dim(cells, cells.shape[dim] - width, cells.shape[dim], axis=dim)
        cells = jnp.concatenate(
            [
                lax.ppermute(tail, axis, [(i, (i + 1) % count) for i in range(ends)]),
                cells,
                lax.ppermute(head, axis, [((i + 1) % count, i) for i in range(ends)]),
            ],
            axis=dim,
        )
    return cells


def passed_along(shard, axis, by):
    size = lax.axis_size(axis)
    pairs = [(i, i + by) for i in range(size) if 0 <= i + by < size]
    return lax.ppermute(shard, axis, pairs)


def norm_local(values, gain):
    floats = values.astype(jnp.float32)
    squares = jnp.sum(floats * floats, axis=-1)
    totals = lax.psum(squares, "row")
    factor = lax.rsqrt(totals / D + 1e-05)
    return (floats * factor[:, None] * gain.astype(jnp.float32)[None, :]).astype(jnp.bfloat16)


def gather_permute(values, axis):
    count = lax.axis_size(axis)
    index = lax.axis_index(axis)
    rows = values.shape[0]
    got = [values] + [
        lax.ppermute(values, axis, [(j, (j + s) % count) for j in range(count)])
        for s in range(1, count)
    ]
    ahead = jnp.concatenate([got[0]] + got[:0:-1], axis=0)
    twice = jnp.concatenate([ahead, ahead], axis=0)
    start = ((count - index) % count) * rows
    return lax.dynamic_slice_in_dim(twice, start, count * rows, axis=0)


def scatter_permute(values, axis):
    count = lax.axis_size(axis)
    index = lax.axis_index(axis)
    rows = values.shape[0] // count
    total = lax.dynamic_slice_in_dim(values, index * rows, rows, axis=0).astype(jnp.float32)
    for s in range(1, count):
        chunk = lax.dynamic_slice_in_dim(values, ((index + s) % count) * rows, rows, axis=0)
        total = total + lax.ppermute(
            chunk, axis, [(j, (j + s) % count) for j in range(count)]
        ).astype(jnp.float32)
    return total


def gather_cols(values):
    return gather_permute(values, "col")


def out_project(attended, weight):
    whole = lax.all_gather(attended, "row", axis=0, tiled=True)
    return lax.psum_scatter(
        jnp.dot(whole, weight, preferred_element_type=jnp.float32).astype(jnp.bfloat16),
        "col",
        scatter_dimension=0,
        tiled=True,
    ).astype(jnp.float32)


def split_heads(values):
    return values.reshape(values.shape[0], values.shape[1] // HD, HD)


def attend_block(queries, keys, values, allowed):
    query_heads = split_heads(queries)
    scores = jnp.einsum(
        "qhd,khd->hqk", query_heads, split_heads(keys), preferred_element_type=jnp.float32
    ) * HD ** (-0.5)
    scores = jnp.where(allowed[None], scores, -1e30)
    peak = jnp.max(scores, axis=-1, keepdims=True)
    weights = jnp.where(allowed[None], jnp.exp(scores - peak), 0.0)
    mass = jnp.sum(weights, axis=-1)
    summed = jnp.einsum(
        "hqk,khd->qhd",
        weights.astype(jnp.bfloat16),
        split_heads(values),
        preferred_element_type=jnp.float32,
    )
    result = summed / jnp.transpose(mass)[:, :, None]
    return result.reshape(queries.shape[0], queries.shape[1]).astype(jnp.bfloat16)


def fold_step(carry, query_heads, query_slots, key_heads, value_heads):
    peak, mass, accum = carry
    piece_slots = jnp.arange(key_heads.shape[0], dtype=jnp.int32)
    allowed = query_slots[:, None] >= piece_slots[None, :]
    scores = jnp.einsum(
        "qhd,khd->hqk", query_heads, key_heads, preferred_element_type=jnp.float32
    ) * HD ** (-0.5)
    scores = jnp.where(allowed[None], scores, -1e30)
    new_peak = jnp.maximum(peak, jnp.max(scores, axis=-1))
    weights = jnp.where(allowed[None], jnp.exp(scores - new_peak[:, :, None]), 0.0)
    summed = jnp.einsum(
        "hqk,khd->hqd",
        weights.astype(jnp.bfloat16),
        value_heads,
        preferred_element_type=jnp.float32,
    )
    return (new_peak, jnp.sum(weights, axis=-1), summed)


def start_state(head_count, query_count):
    return (
        jnp.full((head_count, query_count), -1e30, jnp.float32),
        jnp.zeros((head_count, query_count), jnp.float32),
        jnp.zeros((head_count, query_count, HD), jnp.float32),
    )


def flip(values, axis, bit):
    count = lax.axis_size(axis)
    return lax.ppermute(values, axis, [(j, j ^ bit) for j in range(count)])


def scatter_row(values):
    count = lax.axis_size("row")
    index = lax.axis_index("row")
    rows = values.shape[0] // count
    chunks = values.reshape(count // 2, 2, rows, values.shape[1])
    mine = lax.dynamic_index_in_dim(chunks, index % 2, axis=1, keepdims=False)
    theirs = lax.dynamic_index_in_dim(chunks, 1 - index % 2, axis=1, keepdims=False)
    paired = (mine.astype(jnp.float32) + flip(theirs, "row", 1).astype(jnp.float32))
    paired = paired.astype(jnp.bfloat16)
    keep = lax.dynamic_index_in_dim(paired, index // 2, axis=0, keepdims=False)
    send = lax.dynamic_index_in_dim(paired, 1 - index // 2, axis=0, keepdims=False)
    return (keep.astype(jnp.float32) + flip(send, "row", 2).astype(jnp.float32)).astype(
        jnp.bfloat16
    )


def gather_row(values):
    count = lax.axis_size("row")
    index = lax.axis_index("row")
    got = [values] + [flip(values, "row", b) for b in range(1, count)]
    stacked = jnp.stack(got)
    order = jnp.arange(count, dtype=jnp.int32) ^ index
    return jnp.take(stacked, order, axis=0)


def head_project(values, weights):
    row_count = lax.axis_size("row")
    count, depth = values.shape
    part = weights[0].shape[1] // row_count
    groups = len(weights)

    def body(x_ref, *refs):
        o_ref = refs[-1]
        for g in range(groups):
            o_ref[0, :, g * part : (g + 1) * part] = jnp.dot(
                x_ref[...], refs[g][...], preferred_element_type=jnp.float32
            ).astype(o_ref.dtype)

    summed = pl.pallas_call(
        body,
        grid=(row_count,),
        in_specs=[pl.BlockSpec((count, depth), lambda r: (0, 0))]
        + [pl.BlockSpec((depth, part), lambda r: (0, r)) for _ in weights],
        out_specs=pl.BlockSpec((1, count, groups * part), lambda r: (r, 0, 0)),
        out_shape=jax.ShapeDtypeStruct((row_count, count, groups * part), jnp.bfloat16),
    )(values, *weights)
    summed = summed.reshape(row_count * count, groups * part)
    return scatter_row(summed)


def out_project_heads(attended, weight):
    row_count = lax.axis_size("row")
    whole = gather_row(attended)
    shaped = weight.reshape(row_count, weight.shape[0] // row_count, weight.shape[1])
    summed = jnp.einsum("rtf,rfo->to", whole, shaped, preferred_element_type=jnp.float32)
    return scatter_permute(summed.astype(jnp.bfloat16), "col")


def causal_attend(proj, blocks, place):
    count = proj.shape[0]
    heads = proj.shape[1] // (3 * HD)
    steps = blocks.shape[0]
    scale = HD ** (-0.5)

    def body(place_ref, q_ref, k_ref, v_ref, o_ref, peak_ref, mass_ref, acc_ref):
        step = pl.program_id(1)
        own = place_ref[0]

        @pl.when(step == 0)
        def _():
            peak_ref[...] = jnp.full(peak_ref.shape, -1e30, jnp.float32)
            mass_ref[...] = jnp.zeros(mass_ref.shape, jnp.float32)
            acc_ref[...] = jnp.zeros(acc_ref.shape, jnp.float32)

        def fold(masked):
            scores = lax.dot_general(
                q_ref[...], k_ref[...], (((1,), (1,)), ((), ())),
                preferred_element_type=jnp.float32) * scale
            if masked:
                rows = lax.broadcasted_iota(jnp.int32, scores.shape, 0)
                cols = lax.broadcasted_iota(jnp.int32, scores.shape, 1)
                allowed = cols <= rows
                scores = jnp.where(allowed, scores, -1e30)
            old = peak_ref[...]
            new = jnp.maximum(old, jnp.max(scores, axis=1, keepdims=True))
            weights = jnp.exp(scores - new)
            if masked:
                weights = jnp.where(allowed, weights, 0.0)
            shrink = jnp.exp(old - new)
            mass_ref[...] = shrink * mass_ref[...] + jnp.sum(weights, axis=1, keepdims=True)
            acc_ref[...] = shrink * acc_ref[...] + jnp.dot(
                weights.astype(jnp.bfloat16), v_ref[...], preferred_element_type=jnp.float32)
            peak_ref[...] = new

        @pl.when(step < own)
        def _():
            fold(False)

        @pl.when(step == own)
        def _():
            fold(True)

        @pl.when(step == steps - 1)
        def _():
            o_ref[...] = (acc_ref[...] / mass_ref[...]).astype(o_ref.dtype)

    grid_spec = pltpu.PrefetchScalarGridSpec(
        num_scalar_prefetch=1,
        grid=(heads, steps),
        in_specs=[
            pl.BlockSpec((count, HD), lambda h, j, p: (0, h)),
            pl.BlockSpec((None, count, HD), lambda h, j, p: (p[0] - jnp.minimum(j, p[0]), 0, h)),
            pl.BlockSpec(
                (None, count, HD), lambda h, j, p: (p[0] - jnp.minimum(j, p[0]), 0, heads + h)
            ),
        ],
        out_specs=pl.BlockSpec((count, HD), lambda h, j, p: (0, h)),
        scratch_shapes=[
            pltpu.VMEM((count, 1), jnp.float32),
            pltpu.VMEM((count, 1), jnp.float32),
            pltpu.VMEM((count, HD), jnp.float32),
        ],
    )
    return pl.pallas_call(
        body,
        grid_spec=grid_spec,
        out_shape=jax.ShapeDtypeStruct((count, heads * HD), jnp.bfloat16),
    )(place, proj, blocks, blocks)


def per_device(
    text_embed,
    vis_embed,
    vis_segment,
    vis_valid,
    vis_gain,
    vis_wq,
    vis_wk,
    vis_wv,
    vis_wo,
    dec_gain,
    dec_wq,
    dec_wk,
    dec_wv,
    dec_wo,
):
    row_count = lax.axis_size("row")
    col_count = lax.axis_size("col")
    width = vis_wq.shape[1]
    local = width // row_count
    margin = MAXIMG - 1
    piece_ids = lax.all_gather(jnp.stack([vis_segment, vis_valid]), "col", axis=1, tiled=True)
    piece_len = piece_ids.shape[1]
    framed_ids = with_halo(piece_ids, (("req", 1),), margin)
    total_slots = piece_len * lax.axis_size("req")
    prompt_rows = text_embed.shape[0]
    prompt_total = prompt_rows * lax.axis_size("req") * col_count
    window_len = piece_len + 2 * margin
    window_start = lax.axis_index("req") * piece_len - margin
    window_index = jnp.arange(window_len, dtype=jnp.int32)
    key_slots = window_start + window_index
    inside = (key_slots >= 0) & (key_slots < total_slots)
    key_segment = framed_ids[0]
    key_valid = framed_ids[1]
    begins = jnp.concatenate([jnp.ones((1,), jnp.bool_), key_segment[1:] != key_segment[:-1]])
    begins = begins | (key_slots == 0)
    image_first = lax.cummax(jnp.where(begins, key_slots, window_start), axis=0)
    target_window = image_first * prompt_total // total_slots + key_slots - image_first
    vis_cols = gather_cols(norm_local(vis_embed, vis_gain))
    vis_proj = head_project(vis_cols, (vis_wq, vis_wk, vis_wv))
    vis_pairs = jnp.stack([vis_proj[:, local : 2 * local], vis_proj[:, 2 * local :]])
    framed = with_halo(vis_pairs, (("req", 1),), margin)
    query_local = margin + jnp.arange(piece_len, dtype=jnp.int32)
    query_slots = window_start + query_local
    query_segment = key_segment[query_local]
    seen = (
        inside[None, :]
        & (query_segment[:, None] == key_segment[None, :])
        & ((key_valid[None, :] == 1) | (query_slots[:, None] == key_slots[None, :]))
    )
    vis_att = attend_block(vis_proj[:, :local], framed[0], framed[1], seen)
    vis_out = (vis_embed.astype(jnp.float32) + out_project_heads(vis_att, vis_wo)).astype(
        jnp.bfloat16
    )
    device_place = lax.axis_index("req") * col_count + lax.axis_index("col")
    owned = device_place * prompt_rows + jnp.arange(prompt_rows, dtype=jnp.int32)
    slot_rows = vis_out.shape[0]
    following = passed_along(vis_out, ("req", "col"), -1)
    near_rows = jnp.concatenate([vis_out, following], axis=0)
    near_local = (
        margin + lax.axis_index("col") * slot_rows + jnp.arange(2 * slot_rows, dtype=jnp.int32)
    )
    near_slots = window_start + near_local
    present = near_slots < total_slots
    near_target = jnp.where(present, target_window[near_local], -1)
    near_valid = key_valid[near_local]
    onehot = ((owned[:, None] == near_target[None, :]) & (near_valid[None, :] == 1)).astype(
        jnp.bfloat16
    )
    carried = jnp.dot(onehot, near_rows, preferred_element_type=jnp.float32)
    mixed = (text_embed.astype(jnp.float32) + carried).astype(jnp.bfloat16)
    dec_cols = gather_cols(norm_local(mixed, dec_gain))
    dec_proj = head_project(dec_cols, (dec_wq, dec_wk, dec_wv))
    dec_rows = dec_cols.shape[0]
    keyvals = dec_proj[:, local:]
    req_count = lax.axis_size("req")
    earlier = [keyvals] + [
        lax.ppermute(keyvals, "req", [(j, j + s) for j in range(req_count - s)])
        for s in range(1, req_count)
    ]
    place = lax.axis_index("req").astype(jnp.int32).reshape(1)
    dec_att = causal_attend(dec_proj, jnp.stack(earlier), place)
    return (mixed.astype(jnp.float32) + out_project_heads(dec_att, dec_wo)).astype(jnp.bfloat16)


def solution(mesh):
    return jax.shard_map(
        per_device,
        mesh=mesh,
        in_specs=(
            P(("req", "col"), "row"),
            P(("req", "col"), "row"),
            P(("req", "col")),
            P(("req", "col")),
            P("row"),
            P("row", "col"),
            P("row", "col"),
            P("row", "col"),
            P("col", "row"),
            P("row"),
            P("row", "col"),
            P("row", "col"),
            P("row", "col"),
            P("col", "row"),
        ),
        out_specs=P(("req", "col"), "row"),
        check_vma=False,
    )
```

```python
import jax
import jax.numpy as jnp
from jax import lax
from jax.sharding import PartitionSpec as P
from jax.experimental import pallas as pl
from jax.experimental.pallas import tpu as pltpu

D = 4096
HD = 128
MAXIMG = 256


def with_halo(cells, sides, width):
    for axis, dim in sides:
        count = lax.axis_size(axis)
        ends = count - 1
        head = lax.slice_in_dim(cells, 0, width, axis=dim)
        tail = lax.slice_in_dim(cells, cells.shape[dim] - width, cells.shape[dim], axis=dim)
        cells = jnp.concatenate(
            [
                lax.ppermute(tail, axis, [(i, (i + 1) % count) for i in range(ends)]),
                cells,
                lax.ppermute(head, axis, [((i + 1) % count, i) for i in range(ends)]),
            ],
            axis=dim,
        )
    return cells


def passed_along(shard, axis, by):
    size = lax.axis_size(axis)
    pairs = [(i, i + by) for i in range(size) if 0 <= i + by < size]
    return lax.ppermute(shard, axis, pairs)


def norm_local(values, gain):
    floats = values.astype(jnp.float32)
    squares = jnp.sum(floats * floats, axis=-1)
    totals = lax.psum(squares, "row")
    factor = lax.rsqrt(totals / D + 1e-05)
    return (floats * factor[:, None] * gain.astype(jnp.float32)[None, :]).astype(jnp.bfloat16)


def gather_permute(values, axis):
    count = lax.axis_size(axis)
    index = lax.axis_index(axis)
    rows = values.shape[0]
    got = [values] + [
        lax.ppermute(values, axis, [(j, (j + s) % count) for j in range(count)])
        for s in range(1, count)
    ]
    ahead = jnp.concatenate([got[0]] + got[:0:-1], axis=0)
    twice = jnp.concatenate([ahead, ahead], axis=0)
    start = ((count - index) % count) * rows
    return lax.dynamic_slice_in_dim(twice, start, count * rows, axis=0)


def scatter_permute(values, axis):
    count = lax.axis_size(axis)
    index = lax.axis_index(axis)
    rows = values.shape[0] // count
    total = lax.dynamic_slice_in_dim(values, index * rows, rows, axis=0).astype(jnp.float32)
    for s in range(1, count):
        chunk = lax.dynamic_slice_in_dim(values, ((index + s) % count) * rows, rows, axis=0)
        total = total + lax.ppermute(
            chunk, axis, [(j, (j + s) % count) for j in range(count)]
        ).astype(jnp.float32)
    return total


def gather_cols(values):
    return gather_permute(values, "col")


def out_project(attended, weight):
    whole = lax.all_gather(attended, "row", axis=0, tiled=True)
    return lax.psum_scatter(
        jnp.dot(whole, weight, preferred_element_type=jnp.float32).astype(jnp.bfloat16),
        "col",
        scatter_dimension=0,
        tiled=True,
    ).astype(jnp.float32)


def split_heads(values):
    return values.reshape(values.shape[0], values.shape[1] // HD, HD)


def attend_block(queries, keys, values, allowed):
    query_heads = split_heads(queries)
    scores = jnp.einsum(
        "qhd,khd->hqk", query_heads, split_heads(keys), preferred_element_type=jnp.float32
    ) * HD ** (-0.5)
    scores = jnp.where(allowed[None], scores, -1e30)
    peak = jnp.max(scores, axis=-1, keepdims=True)
    weights = jnp.where(allowed[None], jnp.exp(scores - peak), 0.0)
    mass = jnp.sum(weights, axis=-1)
    summed = jnp.einsum(
        "hqk,khd->qhd",
        weights.astype(jnp.bfloat16),
        split_heads(values),
        preferred_element_type=jnp.float32,
    )
    result = summed / jnp.transpose(mass)[:, :, None]
    return result.reshape(queries.shape[0], queries.shape[1]).astype(jnp.bfloat16)


def fold_step(carry, query_heads, query_slots, key_heads, value_heads):
    peak, mass, accum = carry
    piece_slots = jnp.arange(key_heads.shape[0], dtype=jnp.int32)
    allowed = query_slots[:, None] >= piece_slots[None, :]
    scores = jnp.einsum(
        "qhd,khd->hqk", query_heads, key_heads, preferred_element_type=jnp.float32
    ) * HD ** (-0.5)
    scores = jnp.where(allowed[None], scores, -1e30)
    new_peak = jnp.maximum(peak, jnp.max(scores, axis=-1))
    weights = jnp.where(allowed[None], jnp.exp(scores - new_peak[:, :, None]), 0.0)
    summed = jnp.einsum(
        "hqk,khd->hqd",
        weights.astype(jnp.bfloat16),
        value_heads,
        preferred_element_type=jnp.float32,
    )
    return (new_peak, jnp.sum(weights, axis=-1), summed)


def start_state(head_count, query_count):
    return (
        jnp.full((head_count, query_count), -1e30, jnp.float32),
        jnp.zeros((head_count, query_count), jnp.float32),
        jnp.zeros((head_count, query_count, HD), jnp.float32),
    )


def flip(values, axis, bit):
    count = lax.axis_size(axis)
    return lax.ppermute(values, axis, [(j, j ^ bit) for j in range(count)])


def scatter_row(values):
    count = lax.axis_size("row")
    index = lax.axis_index("row")
    rows = values.shape[0] // count
    chunks = values.reshape(count // 2, 2, rows, values.shape[1])
    mine = lax.dynamic_index_in_dim(chunks, index % 2, axis=1, keepdims=False)
    theirs = lax.dynamic_index_in_dim(chunks, 1 - index % 2, axis=1, keepdims=False)
    paired = (mine.astype(jnp.float32) + flip(theirs, "row", 1).astype(jnp.float32))
    paired = paired.astype(jnp.bfloat16)
    keep = lax.dynamic_index_in_dim(paired, index // 2, axis=0, keepdims=False)
    send = lax.dynamic_index_in_dim(paired, 1 - index // 2, axis=0, keepdims=False)
    return (keep.astype(jnp.float32) + flip(send, "row", 2).astype(jnp.float32)).astype(
        jnp.bfloat16
    )


def gather_row(values):
    count = lax.axis_size("row")
    index = lax.axis_index("row")
    got = [values] + [flip(values, "row", b) for b in range(1, count)]
    stacked = jnp.stack(got)
    order = jnp.arange(count, dtype=jnp.int32) ^ index
    return jnp.take(stacked, order, axis=0)


def head_project(values, weights):
    row_count = lax.axis_size("row")
    count, depth = values.shape
    part = weights[0].shape[1] // row_count
    groups = len(weights)

    def body(x_ref, *refs):
        o_ref = refs[-1]
        for g in range(groups):
            o_ref[0, :, g * part : (g + 1) * part] = jnp.dot(
                x_ref[...], refs[g][...], preferred_element_type=jnp.float32
            ).astype(o_ref.dtype)

    summed = pl.pallas_call(
        body,
        grid=(row_count,),
        in_specs=[pl.BlockSpec((count, depth), lambda r: (0, 0))]
        + [pl.BlockSpec((depth, part), lambda r: (0, r)) for _ in weights],
        out_specs=pl.BlockSpec((1, count, groups * part), lambda r: (r, 0, 0)),
        out_shape=jax.ShapeDtypeStruct((row_count, count, groups * part), jnp.bfloat16),
    )(values, *weights)
    summed = summed.reshape(row_count * count, groups * part)
    return scatter_row(summed)


def out_project_heads(attended, weight):
    row_count = lax.axis_size("row")
    whole = gather_row(attended)
    shaped = weight.reshape(row_count, weight.shape[0] // row_count, weight.shape[1])
    summed = jnp.einsum("rtf,rfo->to", whole, shaped, preferred_element_type=jnp.float32)
    return scatter_permute(summed.astype(jnp.bfloat16), "col")


def causal_attend(proj, blocks, shifts, place, carry=None, last=True):
    count = proj.shape[0]
    heads = proj.shape[1] // (3 * HD)
    steps = blocks.shape[0]
    scale = HD ** (-0.5)
    shift_table = jnp.asarray(shifts, jnp.int32)

    def body(place_ref, shift_ref, q_ref, k_ref, v_ref, *refs):
        if carry is None:
            outs = refs[:-3]
        else:
            peak_in, mass_in, acc_in = refs[:3]
            outs = refs[3:-3]
        peak_ref, mass_ref, acc_ref = refs[-3:]
        step = pl.program_id(1)
        shift = shift_ref[step]
        own = place_ref[0]

        @pl.when(step == 0)
        def _():
            if carry is None:
                peak_ref[...] = jnp.full(peak_ref.shape, -1e30, jnp.float32)
                mass_ref[...] = jnp.zeros(mass_ref.shape, jnp.float32)
                acc_ref[...] = jnp.zeros(acc_ref.shape, jnp.float32)
            else:
                peak_ref[...] = peak_in[...]
                mass_ref[...] = mass_in[...]
                acc_ref[...] = acc_in[...]

        def fold(masked):
            scores = lax.dot_general(
                q_ref[...], k_ref[...], (((1,), (1,)), ((), ())),
                preferred_element_type=jnp.float32) * scale
            if masked:
                rows = lax.broadcasted_iota(jnp.int32, scores.shape, 0)
                cols = lax.broadcasted_iota(jnp.int32, scores.shape, 1)
                allowed = cols <= rows
                scores = jnp.where(allowed, scores, -1e30)
            old = peak_ref[...]
            new = jnp.maximum(old, jnp.max(scores, axis=1, keepdims=True))
            weights = jnp.exp(scores - new)
            if masked:
                weights = jnp.where(allowed, weights, 0.0)
            shrink = jnp.exp(old - new)
            mass_ref[...] = shrink * mass_ref[...] + jnp.sum(weights, axis=1, keepdims=True)
            acc_ref[...] = shrink * acc_ref[...] + jnp.dot(
                weights.astype(jnp.bfloat16), v_ref[...], preferred_element_type=jnp.float32)
            peak_ref[...] = new

        @pl.when((shift > 0) & (shift <= own))
        def _():
            fold(False)

        @pl.when(shift == 0)
        def _():
            fold(True)

        @pl.when(step == steps - 1)
        def _():
            if last:
                outs[0][...] = (acc_ref[...] / mass_ref[...]).astype(outs[0].dtype)
            else:
                outs[0][...] = peak_ref[...]
                outs[1][...] = mass_ref[...]
                outs[2][...] = acc_ref[...]

    state_specs = [
        pl.BlockSpec((None, count, 1), lambda h, j, p, s: (h, 0, 0)),
        pl.BlockSpec((None, count, 1), lambda h, j, p, s: (h, 0, 0)),
        pl.BlockSpec((None, count, HD), lambda h, j, p, s: (h, 0, 0)),
    ]
    state_shapes = [
        jax.ShapeDtypeStruct((heads, count, 1), jnp.float32),
        jax.ShapeDtypeStruct((heads, count, 1), jnp.float32),
        jax.ShapeDtypeStruct((heads, count, HD), jnp.float32),
    ]
    in_specs = [
        pl.BlockSpec((count, HD), lambda h, j, p, s: (0, h)),
        pl.BlockSpec((None, count, HD), lambda h, j, p, s: (j, 0, h)),
        pl.BlockSpec((None, count, HD), lambda h, j, p, s: (j, 0, heads + h)),
    ]
    if carry is not None:
        in_specs = in_specs + state_specs
    if last:
        out_specs = pl.BlockSpec((count, HD), lambda h, j, p, s: (0, h))
        out_shape = jax.ShapeDtypeStruct((count, heads * HD), jnp.bfloat16)
    else:
        out_specs = state_specs
        out_shape = state_shapes
    grid_spec = pltpu.PrefetchScalarGridSpec(
        num_scalar_prefetch=2,
        grid=(heads, steps),
        in_specs=in_specs,
        out_specs=out_specs,
        scratch_shapes=[
            pltpu.VMEM((count, 1), jnp.float32),
            pltpu.VMEM((count, 1), jnp.float32),
            pltpu.VMEM((count, HD), jnp.float32),
        ],
    )
    extra = () if carry is None else tuple(carry)
    return pl.pallas_call(
        body,
        grid_spec=grid_spec,
        out_shape=out_shape,
    )(place, shift_table, proj, blocks, blocks, *extra)


def per_device(
    text_embed,
    vis_embed,
    vis_segment,
    vis_valid,
    vis_gain,
    vis_wq,
    vis_wk,
    vis_wv,
    vis_wo,
    dec_gain,
    dec_wq,
    dec_wk,
    dec_wv,
    dec_wo,
):
    row_count = lax.axis_size("row")
    col_count = lax.axis_size("col")
    width = vis_wq.shape[1]
    local = width // row_count
    margin = MAXIMG - 1
    piece_ids = gather_permute(jnp.stack([vis_segment, vis_valid], axis=1), "col").T
    piece_len = piece_ids.shape[1]
    framed_ids = with_halo(piece_ids, (("req", 1),), margin)
    total_slots = piece_len * lax.axis_size("req")
    prompt_rows = text_embed.shape[0]
    prompt_total = prompt_rows * lax.axis_size("req") * col_count
    window_len = piece_len + 2 * margin
    window_start = lax.axis_index("req") * piece_len - margin
    window_index = jnp.arange(window_len, dtype=jnp.int32)
    key_slots = window_start + window_index
    inside = (key_slots >= 0) & (key_slots < total_slots)
    key_segment = framed_ids[0]
    key_valid = framed_ids[1]
    begins = jnp.concatenate([jnp.ones((1,), jnp.bool_), key_segment[1:] != key_segment[:-1]])
    begins = begins | (key_slots == 0)
    image_first = lax.cummax(jnp.where(begins, key_slots, window_start), axis=0)
    target_window = image_first * prompt_total // total_slots + key_slots - image_first
    vis_cols = gather_cols(norm_local(vis_embed, vis_gain))
    vis_proj = head_project(vis_cols, (vis_wq, vis_wk, vis_wv))
    vis_pairs = jnp.stack([vis_proj[:, local : 2 * local], vis_proj[:, 2 * local :]])
    framed = with_halo(vis_pairs, (("req", 1),), margin)
    query_local = margin + jnp.arange(piece_len, dtype=jnp.int32)
    query_slots = window_start + query_local
    query_segment = key_segment[query_local]
    seen = (
        inside[None, :]
        & (query_segment[:, None] == key_segment[None, :])
        & ((key_valid[None, :] == 1) | (query_slots[:, None] == key_slots[None, :]))
    )
    vis_att = attend_block(vis_proj[:, :local], framed[0], framed[1], seen)
    vis_out = (vis_embed.astype(jnp.float32) + out_project_heads(vis_att, vis_wo)).astype(
        jnp.bfloat16
    )
    device_place = lax.axis_index("req") * col_count + lax.axis_index("col")
    owned = device_place * prompt_rows + jnp.arange(prompt_rows, dtype=jnp.int32)
    slot_rows = vis_out.shape[0]
    following = passed_along(vis_out, ("req", "col"), -1)
    near_rows = jnp.concatenate([vis_out, following], axis=0)
    near_local = (
        margin + lax.axis_index("col") * slot_rows + jnp.arange(2 * slot_rows, dtype=jnp.int32)
    )
    near_slots = window_start + near_local
    present = near_slots < total_slots
    near_target = jnp.where(present, target_window[near_local], -1)
    near_valid = key_valid[near_local]
    onehot = ((owned[:, None] == near_target[None, :]) & (near_valid[None, :] == 1)).astype(
        jnp.bfloat16
    )
    carried = jnp.dot(onehot, near_rows, preferred_element_type=jnp.float32)
    mixed = (text_embed.astype(jnp.float32) + carried).astype(jnp.bfloat16)
    dec_cols = gather_cols(norm_local(mixed, dec_gain))
    dec_proj = head_project(dec_cols, (dec_wq, dec_wk, dec_wv))
    dec_rows = dec_cols.shape[0]
    keyvals = dec_proj[:, local:]
    req_count = lax.axis_size("req")
    earlier = [keyvals] + [
        lax.ppermute(keyvals, "req", [(j, j + s) for j in range(req_count - s)])
        for s in range(1, req_count)
    ]
    place = lax.axis_index("req").astype(jnp.int32).reshape(1)
    near = [s for s in range(0, req_count, 2)]
    far = [s for s in range(1, req_count, 2)]
    state = causal_attend(
        dec_proj, jnp.stack([earlier[s] for s in near]), near, place, last=False
    )
    dec_att = causal_attend(
        dec_proj, jnp.stack([earlier[s] for s in far]), far, place, carry=state
    )
    return (mixed.astype(jnp.float32) + out_project_heads(dec_att, dec_wo)).astype(jnp.bfloat16)


def solution(mesh):
    return jax.shard_map(
        per_device,
        mesh=mesh,
        in_specs=(
            P(("req", "col"), "row"),
            P(("req", "col"), "row"),
            P(("req", "col")),
            P(("req", "col")),
            P("row"),
            P("row", "col"),
            P("row", "col"),
            P("row", "col"),
            P("col", "row"),
            P("row"),
            P("row", "col"),
            P("row", "col"),
            P("row", "col"),
            P("col", "row"),
        ),
        out_specs=P(("req", "col"), "row"),
        check_vma=False,
    )
```

```python
import jax
import jax.numpy as jnp
from jax import lax
from jax.sharding import PartitionSpec as P
from jax.experimental import pallas as pl
from jax.experimental.pallas import tpu as pltpu

D = 4096
HD = 128
MAXIMG = 256


def with_halo(cells, sides, width):
    for axis, dim in sides:
        count = lax.axis_size(axis)
        ends = count - 1
        head = lax.slice_in_dim(cells, 0, width, axis=dim)
        tail = lax.slice_in_dim(cells, cells.shape[dim] - width, cells.shape[dim], axis=dim)
        cells = jnp.concatenate(
            [
                lax.ppermute(tail, axis, [(i, (i + 1) % count) for i in range(ends)]),
                cells,
                lax.ppermute(head, axis, [((i + 1) % count, i) for i in range(ends)]),
            ],
            axis=dim,
        )
    return cells


def passed_along(shard, axis, by):
    size = lax.axis_size(axis)
    pairs = [(i, i + by) for i in range(size) if 0 <= i + by < size]
    return lax.ppermute(shard, axis, pairs)


def norm_local(values, gain):
    floats = values.astype(jnp.float32)
    squares = jnp.sum(floats * floats, axis=-1)
    totals = squares + flip(squares, "row", 1)
    totals = totals + flip(totals, "row", 2)
    factor = lax.rsqrt(totals / D + 1e-05)
    return (floats * factor[:, None] * gain.astype(jnp.float32)[None, :]).astype(jnp.bfloat16)


def gather_permute(values, axis):
    count = lax.axis_size(axis)
    index = lax.axis_index(axis)
    rows = values.shape[0]
    got = [values] + [
        lax.ppermute(values, axis, [(j, (j + s) % count) for j in range(count)])
        for s in range(1, count)
    ]
    ahead = jnp.concatenate([got[0]] + got[:0:-1], axis=0)
    twice = jnp.concatenate([ahead, ahead], axis=0)
    start = ((count - index) % count) * rows
    return lax.dynamic_slice_in_dim(twice, start, count * rows, axis=0)


def scatter_permute(values, axis):
    count = lax.axis_size(axis)
    index = lax.axis_index(axis)
    rows = values.shape[0] // count
    total = lax.dynamic_slice_in_dim(values, index * rows, rows, axis=0).astype(jnp.float32)
    for s in range(1, count):
        chunk = lax.dynamic_slice_in_dim(values, ((index + s) % count) * rows, rows, axis=0)
        total = total + lax.ppermute(
            chunk, axis, [(j, (j + s) % count) for j in range(count)]
        ).astype(jnp.float32)
    return total


def gather_cols(values):
    return gather_permute(values, "col")


def out_project(attended, weight):
    whole = lax.all_gather(attended, "row", axis=0, tiled=True)
    return lax.psum_scatter(
        jnp.dot(whole, weight, preferred_element_type=jnp.float32).astype(jnp.bfloat16),
        "col",
        scatter_dimension=0,
        tiled=True,
    ).astype(jnp.float32)


def split_heads(values):
    return values.reshape(values.shape[0], values.shape[1] // HD, HD)


def attend_block(queries, keys, values, allowed):
    query_heads = split_heads(queries)
    scores = jnp.einsum(
        "qhd,khd->hqk", query_heads, split_heads(keys), preferred_element_type=jnp.float32
    ) * HD ** (-0.5)
    scores = jnp.where(allowed[None], scores, -1e30)
    peak = jnp.max(scores, axis=-1, keepdims=True)
    weights = jnp.where(allowed[None], jnp.exp(scores - peak), 0.0)
    mass = jnp.sum(weights, axis=-1)
    summed = jnp.einsum(
        "hqk,khd->qhd",
        weights.astype(jnp.bfloat16),
        split_heads(values),
        preferred_element_type=jnp.float32,
    )
    result = summed / jnp.transpose(mass)[:, :, None]
    return result.reshape(queries.shape[0], queries.shape[1]).astype(jnp.bfloat16)


def fold_step(carry, query_heads, query_slots, key_heads, value_heads):
    peak, mass, accum = carry
    piece_slots = jnp.arange(key_heads.shape[0], dtype=jnp.int32)
    allowed = query_slots[:, None] >= piece_slots[None, :]
    scores = jnp.einsum(
        "qhd,khd->hqk", query_heads, key_heads, preferred_element_type=jnp.float32
    ) * HD ** (-0.5)
    scores = jnp.where(allowed[None], scores, -1e30)
    new_peak = jnp.maximum(peak, jnp.max(scores, axis=-1))
    weights = jnp.where(allowed[None], jnp.exp(scores - new_peak[:, :, None]), 0.0)
    summed = jnp.einsum(
        "hqk,khd->hqd",
        weights.astype(jnp.bfloat16),
        value_heads,
        preferred_element_type=jnp.float32,
    )
    return (new_peak, jnp.sum(weights, axis=-1), summed)


def start_state(head_count, query_count):
    return (
        jnp.full((head_count, query_count), -1e30, jnp.float32),
        jnp.zeros((head_count, query_count), jnp.float32),
        jnp.zeros((head_count, query_count, HD), jnp.float32),
    )


def flip(values, axis, bit):
    count = lax.axis_size(axis)
    return lax.ppermute(values, axis, [(j, j ^ bit) for j in range(count)])


def scatter_row(values):
    count = lax.axis_size("row")
    index = lax.axis_index("row")
    rows = values.shape[0] // count
    chunks = values.reshape(count // 2, 2, rows, values.shape[1])
    mine = lax.dynamic_index_in_dim(chunks, index % 2, axis=1, keepdims=False)
    theirs = lax.dynamic_index_in_dim(chunks, 1 - index % 2, axis=1, keepdims=False)
    paired = (mine.astype(jnp.float32) + flip(theirs, "row", 1).astype(jnp.float32))
    paired = paired.astype(jnp.bfloat16)
    keep = lax.dynamic_index_in_dim(paired, index // 2, axis=0, keepdims=False)
    send = lax.dynamic_index_in_dim(paired, 1 - index // 2, axis=0, keepdims=False)
    return (keep.astype(jnp.float32) + flip(send, "row", 2).astype(jnp.float32)).astype(
        jnp.bfloat16
    )


def gather_row(values):
    count = lax.axis_size("row")
    index = lax.axis_index("row")
    got = [values] + [flip(values, "row", b) for b in range(1, count)]
    stacked = jnp.stack(got)
    order = jnp.arange(count, dtype=jnp.int32) ^ index
    return jnp.take(stacked, order, axis=0)


def received(values, axis):
    count = lax.axis_size(axis)
    return [values] + [
        lax.ppermute(values, axis, [(j, (j + s) % count) for j in range(count)])
        for s in range(1, count)
    ]


def head_project(pieces, weights, axis):
    row_count = lax.axis_size("row")
    count = len(pieces)
    rows, depth = pieces[0].shape
    part = weights[0].shape[1] // row_count
    groups = len(weights)
    index = lax.axis_index(axis).astype(jnp.int32).reshape(1)

    def body(index_ref, *refs):
        x_refs = refs[:count]
        w_refs = refs[count : count + groups]
        o_ref = refs[-1]
        own = index_ref[0]
        for s in range(count):
            start = pl.multiple_of(((own - s + count) % count) * rows, 8)
            for g in range(groups):
                o_ref[0, pl.ds(start, rows), g * part : (g + 1) * part] = jnp.dot(
                    x_refs[s][...], w_refs[g][...], preferred_element_type=jnp.float32
                ).astype(o_ref.dtype)

    grid_spec = pltpu.PrefetchScalarGridSpec(
        num_scalar_prefetch=1,
        grid=(row_count,),
        in_specs=[pl.BlockSpec((rows, depth), lambda r, i: (0, 0)) for _ in pieces]
        + [pl.BlockSpec((depth, part), lambda r, i: (0, r)) for _ in weights],
        out_specs=pl.BlockSpec((1, count * rows, groups * part), lambda r, i: (r, 0, 0)),
    )
    summed = pl.pallas_call(
        body,
        grid_spec=grid_spec,
        out_shape=jax.ShapeDtypeStruct((row_count, count * rows, groups * part), jnp.bfloat16),
    )(index, *pieces, *weights)
    summed = summed.reshape(row_count * count * rows, groups * part)
    return scatter_row(summed)


def out_project_heads(attended, weight):
    row_count = lax.axis_size("row")
    whole = gather_row(attended)
    shaped = weight.reshape(row_count, weight.shape[0] // row_count, weight.shape[1])
    summed = jnp.einsum("rtf,rfo->to", whole, shaped, preferred_element_type=jnp.float32)
    return scatter_permute(summed.astype(jnp.bfloat16), "col")


def causal_attend(proj, blocks, shifts, place, carry=None, last=True):
    count = proj.shape[0]
    heads = proj.shape[1] // (3 * HD)
    steps = blocks.shape[0]
    scale = HD ** (-0.5)
    shift_table = jnp.asarray(shifts, jnp.int32)

    def body(place_ref, shift_ref, q_ref, k_ref, v_ref, *refs):
        if carry is None:
            outs = refs[:-3]
        else:
            peak_in, mass_in, acc_in = refs[:3]
            outs = refs[3:-3]
        peak_ref, mass_ref, acc_ref = refs[-3:]
        step = pl.program_id(1)
        shift = shift_ref[step]
        own = place_ref[0]

        @pl.when(step == 0)
        def _():
            if carry is None:
                peak_ref[...] = jnp.full(peak_ref.shape, -1e30, jnp.float32)
                mass_ref[...] = jnp.zeros(mass_ref.shape, jnp.float32)
                acc_ref[...] = jnp.zeros(acc_ref.shape, jnp.float32)
            else:
                peak_ref[...] = peak_in[...]
                mass_ref[...] = mass_in[...]
                acc_ref[...] = acc_in[...]

        def fold(masked):
            scores = lax.dot_general(
                q_ref[...], k_ref[...], (((1,), (1,)), ((), ())),
                preferred_element_type=jnp.float32) * scale
            if masked:
                rows = lax.broadcasted_iota(jnp.int32, scores.shape, 0)
                cols = lax.broadcasted_iota(jnp.int32, scores.shape, 1)
                allowed = cols <= rows
                scores = jnp.where(allowed, scores, -1e30)
            old = peak_ref[...]
            new = jnp.maximum(old, jnp.max(scores, axis=1, keepdims=True))
            weights = jnp.exp(scores - new)
            if masked:
                weights = jnp.where(allowed, weights, 0.0)
            shrink = jnp.exp(old - new)
            mass_ref[...] = shrink * mass_ref[...] + jnp.sum(weights, axis=1, keepdims=True)
            acc_ref[...] = shrink * acc_ref[...] + jnp.dot(
                weights.astype(jnp.bfloat16), v_ref[...], preferred_element_type=jnp.float32)
            peak_ref[...] = new

        @pl.when((shift > 0) & (shift <= own))
        def _():
            fold(False)

        @pl.when(shift == 0)
        def _():
            fold(True)

        @pl.when(step == steps - 1)
        def _():
            if last:
                outs[0][...] = (acc_ref[...] / mass_ref[...]).astype(outs[0].dtype)
            else:
                outs[0][...] = peak_ref[...]
                outs[1][...] = mass_ref[...]
                outs[2][...] = acc_ref[...]

    state_specs = [
        pl.BlockSpec((None, count, 1), lambda h, j, p, s: (h, 0, 0)),
        pl.BlockSpec((None, count, 1), lambda h, j, p, s: (h, 0, 0)),
        pl.BlockSpec((None, count, HD), lambda h, j, p, s: (h, 0, 0)),
    ]
    state_shapes = [
        jax.ShapeDtypeStruct((heads, count, 1), jnp.float32),
        jax.ShapeDtypeStruct((heads, count, 1), jnp.float32),
        jax.ShapeDtypeStruct((heads, count, HD), jnp.float32),
    ]
    in_specs = [
        pl.BlockSpec((count, HD), lambda h, j, p, s: (0, h)),
        pl.BlockSpec((None, count, HD), lambda h, j, p, s: (j, 0, h)),
        pl.BlockSpec((None, count, HD), lambda h, j, p, s: (j, 0, heads + h)),
    ]
    if carry is not None:
        in_specs = in_specs + state_specs
    if last:
        out_specs = pl.BlockSpec((count, HD), lambda h, j, p, s: (0, h))
        out_shape = jax.ShapeDtypeStruct((count, heads * HD), jnp.bfloat16)
    else:
        out_specs = state_specs
        out_shape = state_shapes
    grid_spec = pltpu.PrefetchScalarGridSpec(
        num_scalar_prefetch=2,
        grid=(heads, steps),
        in_specs=in_specs,
        out_specs=out_specs,
        scratch_shapes=[
            pltpu.VMEM((count, 1), jnp.float32),
            pltpu.VMEM((count, 1), jnp.float32),
            pltpu.VMEM((count, HD), jnp.float32),
        ],
    )
    extra = () if carry is None else tuple(carry)
    return pl.pallas_call(
        body,
        grid_spec=grid_spec,
        out_shape=out_shape,
    )(place, shift_table, proj, blocks, blocks, *extra)


def per_device(
    text_embed,
    vis_embed,
    vis_segment,
    vis_valid,
    vis_gain,
    vis_wq,
    vis_wk,
    vis_wv,
    vis_wo,
    dec_gain,
    dec_wq,
    dec_wk,
    dec_wv,
    dec_wo,
):
    row_count = lax.axis_size("row")
    col_count = lax.axis_size("col")
    width = vis_wq.shape[1]
    local = width // row_count
    margin = MAXIMG - 1
    piece_ids = gather_permute(jnp.stack([vis_segment, vis_valid], axis=1), "col").T
    piece_len = piece_ids.shape[1]
    framed_ids = with_halo(piece_ids, (("req", 1),), margin)
    total_slots = piece_len * lax.axis_size("req")
    prompt_rows = text_embed.shape[0]
    prompt_total = prompt_rows * lax.axis_size("req") * col_count
    window_len = piece_len + 2 * margin
    window_start = lax.axis_index("req") * piece_len - margin
    window_index = jnp.arange(window_len, dtype=jnp.int32)
    key_slots = window_start + window_index
    inside = (key_slots >= 0) & (key_slots < total_slots)
    key_segment = framed_ids[0]
    key_valid = framed_ids[1]
    begins = jnp.concatenate([jnp.ones((1,), jnp.bool_), key_segment[1:] != key_segment[:-1]])
    begins = begins | (key_slots == 0)
    image_first = lax.cummax(jnp.where(begins, key_slots, window_start), axis=0)
    target_window = image_first * prompt_total // total_slots + key_slots - image_first
    vis_cols = received(norm_local(vis_embed, vis_gain), "col")
    vis_proj = head_project(vis_cols, (vis_wq, vis_wk, vis_wv), "col")
    vis_pairs = jnp.stack([vis_proj[:, local : 2 * local], vis_proj[:, 2 * local :]])
    framed = with_halo(vis_pairs, (("req", 1),), margin)
    query_local = margin + jnp.arange(piece_len, dtype=jnp.int32)
    query_slots = window_start + query_local
    query_segment = key_segment[query_local]
    seen = (
        inside[None, :]
        & (query_segment[:, None] == key_segment[None, :])
        & ((key_valid[None, :] == 1) | (query_slots[:, None] == key_slots[None, :]))
    )
    vis_att = attend_block(vis_proj[:, :local], framed[0], framed[1], seen)
    vis_out = (vis_embed.astype(jnp.float32) + out_project_heads(vis_att, vis_wo)).astype(
        jnp.bfloat16
    )
    device_place = lax.axis_index("req") * col_count + lax.axis_index("col")
    owned = device_place * prompt_rows + jnp.arange(prompt_rows, dtype=jnp.int32)
    slot_rows = vis_out.shape[0]
    following = passed_along(vis_out, ("req", "col"), -1)
    near_rows = jnp.concatenate([vis_out, following], axis=0)
    near_local = (
        margin + lax.axis_index("col") * slot_rows + jnp.arange(2 * slot_rows, dtype=jnp.int32)
    )
    near_slots = window_start + near_local
    present = near_slots < total_slots
    near_target = jnp.where(present, target_window[near_local], -1)
    near_valid = key_valid[near_local]
    onehot = ((owned[:, None] == near_target[None, :]) & (near_valid[None, :] == 1)).astype(
        jnp.bfloat16
    )
    carried = jnp.dot(onehot, near_rows, preferred_element_type=jnp.float32)
    mixed = (text_embed.astype(jnp.float32) + carried).astype(jnp.bfloat16)
    dec_cols = received(norm_local(mixed, dec_gain), "col")
    dec_proj = head_project(dec_cols, (dec_wq, dec_wk, dec_wv), "col")
    dec_rows = dec_proj.shape[0]
    keyvals = dec_proj[:, local:]
    req_count = lax.axis_size("req")
    earlier = [keyvals] + [
        lax.ppermute(keyvals, "req", [(j, j + s) for j in range(req_count - s)])
        for s in range(1, req_count)
    ]
    place = lax.axis_index("req").astype(jnp.int32).reshape(1)
    near = [s for s in range(0, req_count, 2)]
    far = [s for s in range(1, req_count, 2)]
    state = causal_attend(
        dec_proj, jnp.stack([earlier[s] for s in near]), near, place, last=False
    )
    dec_att = causal_attend(
        dec_proj, jnp.stack([earlier[s] for s in far]), far, place, carry=state
    )
    return (mixed.astype(jnp.float32) + out_project_heads(dec_att, dec_wo)).astype(jnp.bfloat16)


def solution(mesh):
    return jax.shard_map(
        per_device,
        mesh=mesh,
        in_specs=(
            P(("req", "col"), "row"),
            P(("req", "col"), "row"),
            P(("req", "col")),
            P(("req", "col")),
            P("row"),
            P("row", "col"),
            P("row", "col"),
            P("row", "col"),
            P("col", "row"),
            P("row"),
            P("row", "col"),
            P("row", "col"),
            P("row", "col"),
            P("col", "row"),
        ),
        out_specs=P(("req", "col"), "row"),
        check_vma=False,
    )
```

```python
import jax
import jax.numpy as jnp
from jax import lax
from jax.sharding import PartitionSpec as P
from jax.experimental import pallas as pl
from jax.experimental.pallas import tpu as pltpu

D = 4096
HD = 128
MAXIMG = 256


def with_halo(cells, sides, width):
    for axis, dim in sides:
        count = lax.axis_size(axis)
        ends = count - 1
        head = lax.slice_in_dim(cells, 0, width, axis=dim)
        tail = lax.slice_in_dim(cells, cells.shape[dim] - width, cells.shape[dim], axis=dim)
        cells = jnp.concatenate(
            [
                lax.ppermute(tail, axis, [(i, (i + 1) % count) for i in range(ends)]),
                cells,
                lax.ppermute(head, axis, [((i + 1) % count, i) for i in range(ends)]),
            ],
            axis=dim,
        )
    return cells


def passed_along(shard, axis, by):
    size = lax.axis_size(axis)
    pairs = [(i, i + by) for i in range(size) if 0 <= i + by < size]
    return lax.ppermute(shard, axis, pairs)


def norm_local(values, gain):
    floats = values.astype(jnp.float32)
    squares = jnp.sum(floats * floats, axis=-1)
    totals = squares + flip(squares, "row", 1)
    totals = totals + flip(totals, "row", 2)
    factor = lax.rsqrt(totals / D + 1e-05)
    return (floats * factor[:, None] * gain.astype(jnp.float32)[None, :]).astype(jnp.bfloat16)


def gather_permute(values, axis):
    count = lax.axis_size(axis)
    index = lax.axis_index(axis)
    rows = values.shape[0]
    got = [values] + [
        lax.ppermute(values, axis, [(j, (j + s) % count) for j in range(count)])
        for s in range(1, count)
    ]
    ahead = jnp.concatenate([got[0]] + got[:0:-1], axis=0)
    twice = jnp.concatenate([ahead, ahead], axis=0)
    start = ((count - index) % count) * rows
    return lax.dynamic_slice_in_dim(twice, start, count * rows, axis=0)


def scatter_permute(values, axis):
    count = lax.axis_size(axis)
    index = lax.axis_index(axis)
    rows = values.shape[0] // count
    total = lax.dynamic_slice_in_dim(values, index * rows, rows, axis=0).astype(jnp.float32)
    for s in range(1, count):
        chunk = lax.dynamic_slice_in_dim(values, ((index + s) % count) * rows, rows, axis=0)
        total = total + lax.ppermute(
            chunk, axis, [(j, (j + s) % count) for j in range(count)]
        ).astype(jnp.float32)
    return total


def gather_cols(values):
    return gather_permute(values, "col")


def out_project(attended, weight):
    whole = lax.all_gather(attended, "row", axis=0, tiled=True)
    return lax.psum_scatter(
        jnp.dot(whole, weight, preferred_element_type=jnp.float32).astype(jnp.bfloat16),
        "col",
        scatter_dimension=0,
        tiled=True,
    ).astype(jnp.float32)


def split_heads(values):
    return values.reshape(values.shape[0], values.shape[1] // HD, HD)


def attend_block(queries, keys, values, allowed):
    query_heads = split_heads(queries)
    scores = jnp.einsum(
        "qhd,khd->hqk", query_heads, split_heads(keys), preferred_element_type=jnp.float32
    ) * HD ** (-0.5)
    scores = jnp.where(allowed[None], scores, -1e30)
    peak = jnp.max(scores, axis=-1, keepdims=True)
    weights = jnp.where(allowed[None], jnp.exp(scores - peak), 0.0)
    mass = jnp.sum(weights, axis=-1)
    summed = jnp.einsum(
        "hqk,khd->qhd",
        weights.astype(jnp.bfloat16),
        split_heads(values),
        preferred_element_type=jnp.float32,
    )
    result = summed / jnp.transpose(mass)[:, :, None]
    return result.reshape(queries.shape[0], queries.shape[1]).astype(jnp.bfloat16)


def fold_step(carry, query_heads, query_slots, key_heads, value_heads):
    peak, mass, accum = carry
    piece_slots = jnp.arange(key_heads.shape[0], dtype=jnp.int32)
    allowed = query_slots[:, None] >= piece_slots[None, :]
    scores = jnp.einsum(
        "qhd,khd->hqk", query_heads, key_heads, preferred_element_type=jnp.float32
    ) * HD ** (-0.5)
    scores = jnp.where(allowed[None], scores, -1e30)
    new_peak = jnp.maximum(peak, jnp.max(scores, axis=-1))
    weights = jnp.where(allowed[None], jnp.exp(scores - new_peak[:, :, None]), 0.0)
    summed = jnp.einsum(
        "hqk,khd->hqd",
        weights.astype(jnp.bfloat16),
        value_heads,
        preferred_element_type=jnp.float32,
    )
    return (new_peak, jnp.sum(weights, axis=-1), summed)


def start_state(head_count, query_count):
    return (
        jnp.full((head_count, query_count), -1e30, jnp.float32),
        jnp.zeros((head_count, query_count), jnp.float32),
        jnp.zeros((head_count, query_count, HD), jnp.float32),
    )


def flip(values, axis, bit):
    count = lax.axis_size(axis)
    return lax.ppermute(values, axis, [(j, j ^ bit) for j in range(count)])


def scatter_row(values):
    rows = values.shape[0] // 4
    chunk = [values[k * rows : (k + 1) * rows] for k in range(4)]
    sent = flip(jnp.concatenate([chunk[1], chunk[3]], axis=0), "row", 1)
    near = chunk[0].astype(jnp.float32) + sent[:rows].astype(jnp.float32)
    far = (chunk[2].astype(jnp.float32) + sent[rows:].astype(jnp.float32)).astype(jnp.bfloat16)
    return (near + flip(far, "row", 2).astype(jnp.float32)).astype(jnp.bfloat16)


def gather_row(values):
    count = lax.axis_size("row")
    index = lax.axis_index("row")
    got = [values] + [flip(values, "row", b) for b in range(1, count)]
    stacked = jnp.stack(got)
    order = jnp.arange(count, dtype=jnp.int32) ^ index
    return jnp.take(stacked, order, axis=0)


def received(values, axis):
    count = lax.axis_size(axis)
    return [values] + [
        lax.ppermute(values, axis, [(j, (j + s) % count) for j in range(count)])
        for s in range(1, count)
    ]


def head_project(pieces, weights, axis):
    row_count = lax.axis_size("row")
    count = len(pieces)
    rows, depth = pieces[0].shape
    part = weights[0].shape[1] // row_count
    groups = len(weights)
    index = jnp.stack([lax.axis_index(axis), lax.axis_index("row")]).astype(jnp.int32)

    def body(index_ref, *refs):
        x_refs = refs[:count]
        w_refs = refs[count : count + groups]
        o_ref = refs[-1]
        own = index_ref[0]
        for s in range(count):
            start = pl.multiple_of(((own - s + count) % count) * rows, 8)
            for g in range(groups):
                o_ref[0, pl.ds(start, rows), g * part : (g + 1) * part] = jnp.dot(
                    x_refs[s][...], w_refs[g][...], preferred_element_type=jnp.float32
                ).astype(o_ref.dtype)

    grid_spec = pltpu.PrefetchScalarGridSpec(
        num_scalar_prefetch=1,
        grid=(row_count,),
        in_specs=[pl.BlockSpec((rows, depth), lambda r, i: (0, 0)) for _ in pieces]
        + [pl.BlockSpec((depth, part), lambda r, i: (0, r)) for _ in weights],
        out_specs=pl.BlockSpec(
            (1, count * rows, groups * part),
            lambda r, i: ((r % 2 + i[1] % 2) % 2 + 2 * ((r // 2 + i[1] // 2) % 2), 0, 0),
        ),
    )
    summed = pl.pallas_call(
        body,
        grid_spec=grid_spec,
        out_shape=jax.ShapeDtypeStruct((row_count, count * rows, groups * part), jnp.bfloat16),
    )(index, *pieces, *weights)
    summed = summed.reshape(row_count * count * rows, groups * part)
    return scatter_row(summed)


def out_project_heads(attended, weight):
    row_count = lax.axis_size("row")
    whole = gather_row(attended)
    shaped = weight.reshape(row_count, weight.shape[0] // row_count, weight.shape[1])
    summed = jnp.einsum("rtf,rfo->to", whole, shaped, preferred_element_type=jnp.float32)
    return scatter_permute(summed.astype(jnp.bfloat16), "col")


def causal_attend(proj, blocks, shifts, place, carry=None, last=True):
    count = proj.shape[0]
    heads = proj.shape[1] // (3 * HD)
    steps = blocks.shape[0]
    scale = HD ** (-0.5)
    shift_table = jnp.asarray(shifts, jnp.int32)

    def body(place_ref, shift_ref, q_ref, kv_ref, *refs):
        if carry is None:
            outs = refs[:-3]
        else:
            peak_in, mass_in, acc_in = refs[:3]
            outs = refs[3:-3]
        peak_ref, mass_ref, acc_ref = refs[-3:]
        step = pl.program_id(0)
        shift = shift_ref[step]
        own = place_ref[0]

        @pl.when(step == 0)
        def _():
            if carry is None:
                peak_ref[...] = jnp.full(peak_ref.shape, -1e30, jnp.float32)
                mass_ref[...] = jnp.zeros(mass_ref.shape, jnp.float32)
                acc_ref[...] = jnp.zeros(acc_ref.shape, jnp.float32)
            else:
                peak_ref[...] = peak_in[...]
                mass_ref[...] = mass_in[...]
                acc_ref[...] = acc_in[...]

        def fold(masked):
            for h in range(heads):
                scores = lax.dot_general(
                    q_ref[:, h * HD : (h + 1) * HD],
                    kv_ref[:, h * HD : (h + 1) * HD],
                    (((1,), (1,)), ((), ())),
                    preferred_element_type=jnp.float32,
                ) * scale
                if masked:
                    rows = lax.broadcasted_iota(jnp.int32, scores.shape, 0)
                    cols = lax.broadcasted_iota(jnp.int32, scores.shape, 1)
                    allowed = cols <= rows
                    scores = jnp.where(allowed, scores, -1e30)
                old = peak_ref[h]
                new = jnp.maximum(old, jnp.max(scores, axis=1, keepdims=True))
                weights = jnp.exp(scores - new)
                if masked:
                    weights = jnp.where(allowed, weights, 0.0)
                shrink = jnp.exp(old - new)
                mass_ref[h] = shrink * mass_ref[h] + jnp.sum(weights, axis=1, keepdims=True)
                acc_ref[h] = shrink * acc_ref[h] + jnp.dot(
                    weights.astype(jnp.bfloat16),
                    kv_ref[:, (heads + h) * HD : (heads + h + 1) * HD],
                    preferred_element_type=jnp.float32,
                )
                peak_ref[h] = new

        @pl.when((shift > 0) & (shift <= own))
        def _():
            fold(False)

        @pl.when(shift == 0)
        def _():
            fold(True)

        @pl.when(step == steps - 1)
        def _():
            if last:
                for h in range(heads):
                    outs[0][:, h * HD : (h + 1) * HD] = (acc_ref[h] / mass_ref[h]).astype(
                        outs[0].dtype
                    )
            else:
                outs[0][...] = peak_ref[...]
                outs[1][...] = mass_ref[...]
                outs[2][...] = acc_ref[...]

    state_specs = [
        pl.BlockSpec((heads, count, 1), lambda j, p, s: (0, 0, 0)),
        pl.BlockSpec((heads, count, 1), lambda j, p, s: (0, 0, 0)),
        pl.BlockSpec((heads, count, HD), lambda j, p, s: (0, 0, 0)),
    ]
    state_shapes = [
        jax.ShapeDtypeStruct((heads, count, 1), jnp.float32),
        jax.ShapeDtypeStruct((heads, count, 1), jnp.float32),
        jax.ShapeDtypeStruct((heads, count, HD), jnp.float32),
    ]
    in_specs = [
        pl.BlockSpec((count, heads * HD), lambda j, p, s: (0, 0)),
        pl.BlockSpec((None, count, 2 * heads * HD), lambda j, p, s: (j, 0, 0)),
    ]
    if carry is not None:
        in_specs = in_specs + state_specs
    if last:
        out_specs = pl.BlockSpec((count, heads * HD), lambda j, p, s: (0, 0))
        out_shape = jax.ShapeDtypeStruct((count, heads * HD), jnp.bfloat16)
    else:
        out_specs = state_specs
        out_shape = state_shapes
    grid_spec = pltpu.PrefetchScalarGridSpec(
        num_scalar_prefetch=2,
        grid=(steps,),
        in_specs=in_specs,
        out_specs=out_specs,
        scratch_shapes=[
            pltpu.VMEM((heads, count, 1), jnp.float32),
            pltpu.VMEM((heads, count, 1), jnp.float32),
            pltpu.VMEM((heads, count, HD), jnp.float32),
        ],
    )
    extra = () if carry is None else tuple(carry)
    return pl.pallas_call(
        body,
        grid_spec=grid_spec,
        out_shape=out_shape,
    )(place, shift_table, proj, blocks, *extra)


def per_device(
    text_embed,
    vis_embed,
    vis_segment,
    vis_valid,
    vis_gain,
    vis_wq,
    vis_wk,
    vis_wv,
    vis_wo,
    dec_gain,
    dec_wq,
    dec_wk,
    dec_wv,
    dec_wo,
):
    row_count = lax.axis_size("row")
    col_count = lax.axis_size("col")
    width = vis_wq.shape[1]
    local = width // row_count
    margin = MAXIMG - 1
    piece_ids = gather_permute(jnp.stack([vis_segment, vis_valid], axis=1), "col").T
    piece_len = piece_ids.shape[1]
    framed_ids = with_halo(piece_ids, (("req", 1),), margin)
    total_slots = piece_len * lax.axis_size("req")
    prompt_rows = text_embed.shape[0]
    prompt_total = prompt_rows * lax.axis_size("req") * col_count
    window_len = piece_len + 2 * margin
    window_start = lax.axis_index("req") * piece_len - margin
    window_index = jnp.arange(window_len, dtype=jnp.int32)
    key_slots = window_start + window_index
    inside = (key_slots >= 0) & (key_slots < total_slots)
    key_segment = framed_ids[0]
    key_valid = framed_ids[1]
    begins = jnp.concatenate([jnp.ones((1,), jnp.bool_), key_segment[1:] != key_segment[:-1]])
    begins = begins | (key_slots == 0)
    image_first = lax.cummax(jnp.where(begins, key_slots, window_start), axis=0)
    target_window = image_first * prompt_total // total_slots + key_slots - image_first
    vis_cols = received(norm_local(vis_embed, vis_gain), "col")
    vis_proj = head_project(vis_cols, (vis_wq, vis_wk, vis_wv), "col")
    vis_pairs = jnp.stack([vis_proj[:, local : 2 * local], vis_proj[:, 2 * local :]])
    framed = with_halo(vis_pairs, (("req", 1),), margin)
    query_local = margin + jnp.arange(piece_len, dtype=jnp.int32)
    query_slots = window_start + query_local
    query_segment = key_segment[query_local]
    seen = (
        inside[None, :]
        & (query_segment[:, None] == key_segment[None, :])
        & ((key_valid[None, :] == 1) | (query_slots[:, None] == key_slots[None, :]))
    )
    vis_att = attend_block(vis_proj[:, :local], framed[0], framed[1], seen)
    vis_out = (vis_embed.astype(jnp.float32) + out_project_heads(vis_att, vis_wo)).astype(
        jnp.bfloat16
    )
    device_place = lax.axis_index("req") * col_count + lax.axis_index("col")
    owned = device_place * prompt_rows + jnp.arange(prompt_rows, dtype=jnp.int32)
    slot_rows = vis_out.shape[0]
    following = passed_along(vis_out, ("req", "col"), -1)
    near_rows = jnp.concatenate([vis_out, following], axis=0)
    near_local = (
        margin + lax.axis_index("col") * slot_rows + jnp.arange(2 * slot_rows, dtype=jnp.int32)
    )
    near_slots = window_start + near_local
    present = near_slots < total_slots
    near_target = jnp.where(present, target_window[near_local], -1)
    near_valid = key_valid[near_local]
    onehot = ((owned[:, None] == near_target[None, :]) & (near_valid[None, :] == 1)).astype(
        jnp.bfloat16
    )
    carried = jnp.dot(onehot, near_rows, preferred_element_type=jnp.float32)
    mixed = (text_embed.astype(jnp.float32) + carried).astype(jnp.bfloat16)
    dec_cols = received(norm_local(mixed, dec_gain), "col")
    dec_proj = head_project(dec_cols, (dec_wq, dec_wk, dec_wv), "col")
    dec_rows = dec_proj.shape[0]
    keyvals = dec_proj[:, local:]
    req_count = lax.axis_size("req")
    earlier = [keyvals] + [
        lax.ppermute(keyvals, "req", [(j, j + s) for j in range(req_count - s)])
        for s in range(1, req_count)
    ]
    place = lax.axis_index("req").astype(jnp.int32).reshape(1)
    near = [s for s in range(0, req_count, 2)]
    far = [s for s in range(1, req_count, 2)]
    state = causal_attend(
        dec_proj, jnp.stack([earlier[s] for s in near]), near, place, last=False
    )
    dec_att = causal_attend(
        dec_proj, jnp.stack([earlier[s] for s in far]), far, place, carry=state
    )
    return (mixed.astype(jnp.float32) + out_project_heads(dec_att, dec_wo)).astype(jnp.bfloat16)


def solution(mesh):
    return jax.shard_map(
        per_device,
        mesh=mesh,
        in_specs=(
            P(("req", "col"), "row"),
            P(("req", "col"), "row"),
            P(("req", "col")),
            P(("req", "col")),
            P("row"),
            P("row", "col"),
            P("row", "col"),
            P("row", "col"),
            P("col", "row"),
            P("row"),
            P("row", "col"),
            P("row", "col"),
            P("row", "col"),
            P("col", "row"),
        ),
        out_specs=P(("req", "col"), "row"),
        check_vma=False,
    )
```

```python
import jax
import jax.numpy as jnp
from jax import lax
from jax.sharding import PartitionSpec as P
from jax.experimental import pallas as pl
from jax.experimental.pallas import tpu as pltpu

D = 4096
HD = 128
MAXIMG = 256


def with_halo(cells, sides, width):
    for axis, dim in sides:
        count = lax.axis_size(axis)
        ends = count - 1
        head = lax.slice_in_dim(cells, 0, width, axis=dim)
        tail = lax.slice_in_dim(cells, cells.shape[dim] - width, cells.shape[dim], axis=dim)
        cells = jnp.concatenate(
            [
                lax.ppermute(tail, axis, [(i, (i + 1) % count) for i in range(ends)]),
                cells,
                lax.ppermute(head, axis, [((i + 1) % count, i) for i in range(ends)]),
            ],
            axis=dim,
        )
    return cells


def passed_along(shard, axis, by):
    size = lax.axis_size(axis)
    pairs = [(i, i + by) for i in range(size) if 0 <= i + by < size]
    return lax.ppermute(shard, axis, pairs)


def norm_local(values, gain):
    floats = values.astype(jnp.float32)
    squares = jnp.sum(floats * floats, axis=-1)
    totals = squares + flip(squares, "row", 1)
    totals = totals + flip(totals, "row", 2)
    factor = lax.rsqrt(totals / D + 1e-05)
    return (floats * factor[:, None] * gain.astype(jnp.float32)[None, :]).astype(jnp.bfloat16)


def gather_permute(values, axis):
    count = lax.axis_size(axis)
    index = lax.axis_index(axis)
    rows = values.shape[0]
    got = [values] + [
        lax.ppermute(values, axis, [(j, (j + s) % count) for j in range(count)])
        for s in range(1, count)
    ]
    ahead = jnp.concatenate([got[0]] + got[:0:-1], axis=0)
    twice = jnp.concatenate([ahead, ahead], axis=0)
    start = ((count - index) % count) * rows
    return lax.dynamic_slice_in_dim(twice, start, count * rows, axis=0)


def scatter_permute(values, axis):
    count = lax.axis_size(axis)
    index = lax.axis_index(axis)
    rows = values.shape[0] // count
    total = lax.dynamic_slice_in_dim(values, index * rows, rows, axis=0).astype(jnp.float32)
    for s in range(1, count):
        chunk = lax.dynamic_slice_in_dim(values, ((index + s) % count) * rows, rows, axis=0)
        total = total + lax.ppermute(
            chunk, axis, [(j, (j + s) % count) for j in range(count)]
        ).astype(jnp.float32)
    return total


def gather_cols(values):
    return gather_permute(values, "col")


def out_project(attended, weight):
    whole = lax.all_gather(attended, "row", axis=0, tiled=True)
    return lax.psum_scatter(
        jnp.dot(whole, weight, preferred_element_type=jnp.float32).astype(jnp.bfloat16),
        "col",
        scatter_dimension=0,
        tiled=True,
    ).astype(jnp.float32)


def split_heads(values):
    return values.reshape(values.shape[0], values.shape[1] // HD, HD)


def attend_block(queries, keys, values, allowed):
    query_heads = split_heads(queries)
    scores = jnp.einsum(
        "qhd,khd->hqk", query_heads, split_heads(keys), preferred_element_type=jnp.float32
    ) * HD ** (-0.5)
    scores = jnp.where(allowed[None], scores, -1e30)
    peak = jnp.max(scores, axis=-1, keepdims=True)
    weights = jnp.where(allowed[None], jnp.exp(scores - peak), 0.0)
    mass = jnp.sum(weights, axis=-1)
    summed = jnp.einsum(
        "hqk,khd->qhd",
        weights.astype(jnp.bfloat16),
        split_heads(values),
        preferred_element_type=jnp.float32,
    )
    result = summed / jnp.transpose(mass)[:, :, None]
    return result.reshape(queries.shape[0], queries.shape[1]).astype(jnp.bfloat16)


def fold_step(carry, query_heads, query_slots, key_heads, value_heads):
    peak, mass, accum = carry
    piece_slots = jnp.arange(key_heads.shape[0], dtype=jnp.int32)
    allowed = query_slots[:, None] >= piece_slots[None, :]
    scores = jnp.einsum(
        "qhd,khd->hqk", query_heads, key_heads, preferred_element_type=jnp.float32
    ) * HD ** (-0.5)
    scores = jnp.where(allowed[None], scores, -1e30)
    new_peak = jnp.maximum(peak, jnp.max(scores, axis=-1))
    weights = jnp.where(allowed[None], jnp.exp(scores - new_peak[:, :, None]), 0.0)
    summed = jnp.einsum(
        "hqk,khd->hqd",
        weights.astype(jnp.bfloat16),
        value_heads,
        preferred_element_type=jnp.float32,
    )
    return (new_peak, jnp.sum(weights, axis=-1), summed)


def start_state(head_count, query_count):
    return (
        jnp.full((head_count, query_count), -1e30, jnp.float32),
        jnp.zeros((head_count, query_count), jnp.float32),
        jnp.zeros((head_count, query_count, HD), jnp.float32),
    )


def flip(values, axis, bit):
    count = lax.axis_size(axis)
    return lax.ppermute(values, axis, [(j, j ^ bit) for j in range(count)])


def scatter_row(values):
    rows = values.shape[0] // 4
    chunk = [values[k * rows : (k + 1) * rows] for k in range(4)]
    sent = flip(jnp.concatenate([chunk[1], chunk[3]], axis=0), "row", 1)
    near = chunk[0].astype(jnp.float32) + sent[:rows].astype(jnp.float32)
    far = (chunk[2].astype(jnp.float32) + sent[rows:].astype(jnp.float32)).astype(jnp.bfloat16)
    return (near + flip(far, "row", 2).astype(jnp.float32)).astype(jnp.bfloat16)


def gather_row(values):
    count = lax.axis_size("row")
    index = lax.axis_index("row")
    got = [values] + [flip(values, "row", b) for b in range(1, count)]
    stacked = jnp.stack(got)
    order = jnp.arange(count, dtype=jnp.int32) ^ index
    return jnp.take(stacked, order, axis=0)


def received(values, axis):
    count = lax.axis_size(axis)
    return [values] + [
        lax.ppermute(values, axis, [(j, (j + s) % count) for j in range(count)])
        for s in range(1, count)
    ]


def head_project(pieces, weights, axis):
    row_count = lax.axis_size("row")
    count = len(pieces)
    rows, depth = pieces[0].shape
    part = weights[0].shape[1] // row_count
    groups = len(weights)
    index = jnp.stack([lax.axis_index(axis), lax.axis_index("row")]).astype(jnp.int32)

    def body(index_ref, *refs):
        x_refs = refs[:count]
        w_refs = refs[count : count + groups]
        o_ref = refs[-1]
        own = index_ref[0]
        for s in range(count):
            start = pl.multiple_of(((own - s + count) % count) * rows, 8)
            for g in range(groups):
                o_ref[0, pl.ds(start, rows), g * part : (g + 1) * part] = jnp.dot(
                    x_refs[s][...], w_refs[g][...], preferred_element_type=jnp.float32
                ).astype(o_ref.dtype)

    grid_spec = pltpu.PrefetchScalarGridSpec(
        num_scalar_prefetch=1,
        grid=(row_count,),
        in_specs=[pl.BlockSpec((rows, depth), lambda r, i: (0, 0)) for _ in pieces]
        + [pl.BlockSpec((depth, part), lambda r, i: (0, r)) for _ in weights],
        out_specs=pl.BlockSpec(
            (1, count * rows, groups * part),
            lambda r, i: ((r % 2 + i[1] % 2) % 2 + 2 * ((r // 2 + i[1] // 2) % 2), 0, 0),
        ),
    )
    summed = pl.pallas_call(
        body,
        grid_spec=grid_spec,
        out_shape=jax.ShapeDtypeStruct((row_count, count * rows, groups * part), jnp.bfloat16),
    )(index, *pieces, *weights)
    summed = summed.reshape(row_count * count * rows, groups * part)
    return scatter_row(summed)


def out_project_heads(attended, weight):
    row_count = lax.axis_size("row")
    whole = gather_row(attended)
    shaped = weight.reshape(row_count, weight.shape[0] // row_count, weight.shape[1])
    summed = jnp.einsum("rtf,rfo->to", whole, shaped, preferred_element_type=jnp.float32)
    return scatter_permute(summed.astype(jnp.bfloat16), "col")


def causal_attend(proj, blocks, shifts, place, carry=None, last=True):
    count = proj.shape[0]
    heads = proj.shape[1] // (3 * HD)
    steps = blocks.shape[0]
    scale = HD ** (-0.5)
    shift_table = jnp.asarray(shifts, jnp.int32)

    def body(place_ref, shift_ref, q_ref, kv_ref, *refs):
        if carry is None:
            outs = refs[:-3]
        else:
            peak_in, mass_in, acc_in = refs[:3]
            outs = refs[3:-3]
        peak_ref, mass_ref, acc_ref = refs[-3:]
        step = pl.program_id(0)
        shift = shift_ref[step]
        own = place_ref[0]

        @pl.when(step == 0)
        def _():
            if carry is None:
                peak_ref[...] = jnp.full(peak_ref.shape, -1e30, jnp.float32)
                mass_ref[...] = jnp.zeros(mass_ref.shape, jnp.float32)
                acc_ref[...] = jnp.zeros(acc_ref.shape, jnp.float32)
            else:
                peak_ref[...] = peak_in[...]
                mass_ref[...] = mass_in[...]
                acc_ref[...] = acc_in[...]

        def fold(masked):
            def one(h, unused):
                lane = pl.multiple_of(h * HD, HD)
                scores = lax.dot_general(
                    q_ref[:, pl.ds(lane, HD)],
                    kv_ref[:, pl.ds(lane, HD)],
                    (((1,), (1,)), ((), ())),
                    preferred_element_type=jnp.float32,
                ) * scale
                if masked:
                    rows = lax.broadcasted_iota(jnp.int32, scores.shape, 0)
                    cols = lax.broadcasted_iota(jnp.int32, scores.shape, 1)
                    allowed = cols <= rows
                    scores = jnp.where(allowed, scores, -1e30)
                old = peak_ref[h]
                new = jnp.maximum(old, jnp.max(scores, axis=1, keepdims=True))
                weights = jnp.exp(scores - new)
                if masked:
                    weights = jnp.where(allowed, weights, 0.0)
                shrink = jnp.exp(old - new)
                mass_ref[h] = shrink * mass_ref[h] + jnp.sum(weights, axis=1, keepdims=True)
                acc_ref[h] = shrink * acc_ref[h] + jnp.dot(
                    weights.astype(jnp.bfloat16),
                    kv_ref[:, pl.ds(lane + heads * HD, HD)],
                    preferred_element_type=jnp.float32,
                )
                peak_ref[h] = new
                return unused

            lax.fori_loop(0, heads, one, 0)

        @pl.when((shift > 0) & (shift <= own))
        def _():
            fold(False)

        @pl.when(shift == 0)
        def _():
            fold(True)

        @pl.when(step == steps - 1)
        def _():
            if last:
                for h in range(heads):
                    outs[0][:, h * HD : (h + 1) * HD] = (acc_ref[h] / mass_ref[h]).astype(
                        outs[0].dtype
                    )
            else:
                outs[0][...] = peak_ref[...]
                outs[1][...] = mass_ref[...]
                outs[2][...] = acc_ref[...]

    state_specs = [
        pl.BlockSpec((heads, count, 1), lambda j, p, s: (0, 0, 0)),
        pl.BlockSpec((heads, count, 1), lambda j, p, s: (0, 0, 0)),
        pl.BlockSpec((heads, count, HD), lambda j, p, s: (0, 0, 0)),
    ]
    state_shapes = [
        jax.ShapeDtypeStruct((heads, count, 1), jnp.float32),
        jax.ShapeDtypeStruct((heads, count, 1), jnp.float32),
        jax.ShapeDtypeStruct((heads, count, HD), jnp.float32),
    ]
    in_specs = [
        pl.BlockSpec((count, heads * HD), lambda j, p, s: (0, 0)),
        pl.BlockSpec((None, count, 2 * heads * HD), lambda j, p, s: (j, 0, 0)),
    ]
    if carry is not None:
        in_specs = in_specs + state_specs
    if last:
        out_specs = pl.BlockSpec((count, heads * HD), lambda j, p, s: (0, 0))
        out_shape = jax.ShapeDtypeStruct((count, heads * HD), jnp.bfloat16)
    else:
        out_specs = state_specs
        out_shape = state_shapes
    grid_spec = pltpu.PrefetchScalarGridSpec(
        num_scalar_prefetch=2,
        grid=(steps,),
        in_specs=in_specs,
        out_specs=out_specs,
        scratch_shapes=[
            pltpu.VMEM((heads, count, 1), jnp.float32),
            pltpu.VMEM((heads, count, 1), jnp.float32),
            pltpu.VMEM((heads, count, HD), jnp.float32),
        ],
    )
    extra = () if carry is None else tuple(carry)
    return pl.pallas_call(
        body,
        grid_spec=grid_spec,
        out_shape=out_shape,
    )(place, shift_table, proj, blocks, *extra)


def per_device(
    text_embed,
    vis_embed,
    vis_segment,
    vis_valid,
    vis_gain,
    vis_wq,
    vis_wk,
    vis_wv,
    vis_wo,
    dec_gain,
    dec_wq,
    dec_wk,
    dec_wv,
    dec_wo,
):
    row_count = lax.axis_size("row")
    col_count = lax.axis_size("col")
    width = vis_wq.shape[1]
    local = width // row_count
    margin = MAXIMG - 1
    piece_ids = gather_permute(jnp.stack([vis_segment, vis_valid], axis=1), "col").T
    piece_len = piece_ids.shape[1]
    framed_ids = with_halo(piece_ids, (("req", 1),), margin)
    total_slots = piece_len * lax.axis_size("req")
    prompt_rows = text_embed.shape[0]
    prompt_total = prompt_rows * lax.axis_size("req") * col_count
    window_len = piece_len + 2 * margin
    window_start = lax.axis_index("req") * piece_len - margin
    window_index = jnp.arange(window_len, dtype=jnp.int32)
    key_slots = window_start + window_index
    inside = (key_slots >= 0) & (key_slots < total_slots)
    key_segment = framed_ids[0]
    key_valid = framed_ids[1]
    begins = jnp.concatenate([jnp.ones((1,), jnp.bool_), key_segment[1:] != key_segment[:-1]])
    begins = begins | (key_slots == 0)
    image_first = lax.cummax(jnp.where(begins, key_slots, window_start), axis=0)
    target_window = image_first * prompt_total // total_slots + key_slots - image_first
    vis_cols = received(norm_local(vis_embed, vis_gain), "col")
    vis_proj = head_project(vis_cols, (vis_wq, vis_wk, vis_wv), "col")
    vis_pairs = jnp.stack([vis_proj[:, local : 2 * local], vis_proj[:, 2 * local :]])
    framed = with_halo(vis_pairs, (("req", 1),), margin)
    query_local = margin + jnp.arange(piece_len, dtype=jnp.int32)
    query_slots = window_start + query_local
    query_segment = key_segment[query_local]
    seen = (
        inside[None, :]
        & (query_segment[:, None] == key_segment[None, :])
        & ((key_valid[None, :] == 1) | (query_slots[:, None] == key_slots[None, :]))
    )
    vis_att = attend_block(vis_proj[:, :local], framed[0], framed[1], seen)
    vis_out = (vis_embed.astype(jnp.float32) + out_project_heads(vis_att, vis_wo)).astype(
        jnp.bfloat16
    )
    device_place = lax.axis_index("req") * col_count + lax.axis_index("col")
    owned = device_place * prompt_rows + jnp.arange(prompt_rows, dtype=jnp.int32)
    slot_rows = vis_out.shape[0]
    following = passed_along(vis_out, ("req", "col"), -1)
    near_rows = jnp.concatenate([vis_out, following], axis=0)
    near_local = (
        margin + lax.axis_index("col") * slot_rows + jnp.arange(2 * slot_rows, dtype=jnp.int32)
    )
    near_slots = window_start + near_local
    present = near_slots < total_slots
    near_target = jnp.where(present, target_window[near_local], -1)
    near_valid = key_valid[near_local]
    onehot = ((owned[:, None] == near_target[None, :]) & (near_valid[None, :] == 1)).astype(
        jnp.bfloat16
    )
    carried = jnp.dot(onehot, near_rows, preferred_element_type=jnp.float32)
    mixed = (text_embed.astype(jnp.float32) + carried).astype(jnp.bfloat16)
    dec_cols = received(norm_local(mixed, dec_gain), "col")
    dec_proj = head_project(dec_cols, (dec_wq, dec_wk, dec_wv), "col")
    dec_rows = dec_proj.shape[0]
    keyvals = dec_proj[:, local:]
    req_count = lax.axis_size("req")
    earlier = [keyvals] + [
        lax.ppermute(keyvals, "req", [(j, j + s) for j in range(req_count - s)])
        for s in range(1, req_count)
    ]
    place = lax.axis_index("req").astype(jnp.int32).reshape(1)
    near = [s for s in range(0, req_count, 2)]
    far = [s for s in range(1, req_count, 2)]
    state = causal_attend(
        dec_proj, jnp.stack([earlier[s] for s in near]), near, place, last=False
    )
    dec_att = causal_attend(
        dec_proj, jnp.stack([earlier[s] for s in far]), far, place, carry=state
    )
    return (mixed.astype(jnp.float32) + out_project_heads(dec_att, dec_wo)).astype(jnp.bfloat16)


def solution(mesh):
    return jax.shard_map(
        per_device,
        mesh=mesh,
        in_specs=(
            P(("req", "col"), "row"),
            P(("req", "col"), "row"),
            P(("req", "col")),
            P(("req", "col")),
            P("row"),
            P("row", "col"),
            P("row", "col"),
            P("row", "col"),
            P("col", "row"),
            P("row"),
            P("row", "col"),
            P("row", "col"),
            P("row", "col"),
            P("col", "row"),
        ),
        out_specs=P(("req", "col"), "row"),
        check_vma=False,
    )
```

```python
import jax
import jax.numpy as jnp
from jax import lax
from jax.sharding import PartitionSpec as P
from jax.experimental import pallas as pl
from jax.experimental.pallas import tpu as pltpu

D = 4096
HD = 128
MAXIMG = 256


def with_halo(cells, sides, width):
    for axis, dim in sides:
        count = lax.axis_size(axis)
        ends = count - 1
        head = lax.slice_in_dim(cells, 0, width, axis=dim)
        tail = lax.slice_in_dim(cells, cells.shape[dim] - width, cells.shape[dim], axis=dim)
        cells = jnp.concatenate(
            [
                lax.ppermute(tail, axis, [(i, (i + 1) % count) for i in range(ends)]),
                cells,
                lax.ppermute(head, axis, [((i + 1) % count, i) for i in range(ends)]),
            ],
            axis=dim,
        )
    return cells


def passed_along(shard, axis, by):
    size = lax.axis_size(axis)
    pairs = [(i, i + by) for i in range(size) if 0 <= i + by < size]
    return lax.ppermute(shard, axis, pairs)


def norm_local(values, gain):
    floats = values.astype(jnp.float32)
    squares = jnp.sum(floats * floats, axis=-1)
    totals = squares + flip(squares, "row", 1)
    totals = totals + flip(totals, "row", 2)
    factor = lax.rsqrt(totals / D + 1e-05)
    return (floats * factor[:, None] * gain.astype(jnp.float32)[None, :]).astype(jnp.bfloat16)


def gather_permute(values, axis):
    count = lax.axis_size(axis)
    index = lax.axis_index(axis)
    rows = values.shape[0]
    got = [values] + [
        lax.ppermute(values, axis, [(j, (j + s) % count) for j in range(count)])
        for s in range(1, count)
    ]
    ahead = jnp.concatenate([got[0]] + got[:0:-1], axis=0)
    twice = jnp.concatenate([ahead, ahead], axis=0)
    start = ((count - index) % count) * rows
    return lax.dynamic_slice_in_dim(twice, start, count * rows, axis=0)


def scatter_permute(values, axis):
    count = lax.axis_size(axis)
    index = lax.axis_index(axis)
    rows = values.shape[0] // count
    total = lax.dynamic_slice_in_dim(values, index * rows, rows, axis=0).astype(jnp.float32)
    for s in range(1, count):
        chunk = lax.dynamic_slice_in_dim(values, ((index + s) % count) * rows, rows, axis=0)
        total = total + lax.ppermute(
            chunk, axis, [(j, (j + s) % count) for j in range(count)]
        ).astype(jnp.float32)
    return total


def gather_cols(values):
    return gather_permute(values, "col")


def out_project(attended, weight):
    whole = lax.all_gather(attended, "row", axis=0, tiled=True)
    return lax.psum_scatter(
        jnp.dot(whole, weight, preferred_element_type=jnp.float32).astype(jnp.bfloat16),
        "col",
        scatter_dimension=0,
        tiled=True,
    ).astype(jnp.float32)


def split_heads(values):
    return values.reshape(values.shape[0], values.shape[1] // HD, HD)


def attend_block(queries, keys, values, allowed):
    query_heads = split_heads(queries)
    scores = jnp.einsum(
        "qhd,khd->hqk", query_heads, split_heads(keys), preferred_element_type=jnp.float32
    ) * HD ** (-0.5)
    scores = jnp.where(allowed[None], scores, -1e30)
    peak = jnp.max(scores, axis=-1, keepdims=True)
    weights = jnp.where(allowed[None], jnp.exp(scores - peak), 0.0)
    mass = jnp.sum(weights, axis=-1)
    summed = jnp.einsum(
        "hqk,khd->qhd",
        weights.astype(jnp.bfloat16),
        split_heads(values),
        preferred_element_type=jnp.float32,
    )
    result = summed / jnp.transpose(mass)[:, :, None]
    return result.reshape(queries.shape[0], queries.shape[1]).astype(jnp.bfloat16)


def fold_step(carry, query_heads, query_slots, key_heads, value_heads):
    peak, mass, accum = carry
    piece_slots = jnp.arange(key_heads.shape[0], dtype=jnp.int32)
    allowed = query_slots[:, None] >= piece_slots[None, :]
    scores = jnp.einsum(
        "qhd,khd->hqk", query_heads, key_heads, preferred_element_type=jnp.float32
    ) * HD ** (-0.5)
    scores = jnp.where(allowed[None], scores, -1e30)
    new_peak = jnp.maximum(peak, jnp.max(scores, axis=-1))
    weights = jnp.where(allowed[None], jnp.exp(scores - new_peak[:, :, None]), 0.0)
    summed = jnp.einsum(
        "hqk,khd->hqd",
        weights.astype(jnp.bfloat16),
        value_heads,
        preferred_element_type=jnp.float32,
    )
    return (new_peak, jnp.sum(weights, axis=-1), summed)


def start_state(head_count, query_count):
    return (
        jnp.full((head_count, query_count), -1e30, jnp.float32),
        jnp.zeros((head_count, query_count), jnp.float32),
        jnp.zeros((head_count, query_count, HD), jnp.float32),
    )


def flip(values, axis, bit):
    count = lax.axis_size(axis)
    return lax.ppermute(values, axis, [(j, j ^ bit) for j in range(count)])


def scatter_row(values):
    rows = values.shape[0] // 4
    chunk = [values[k * rows : (k + 1) * rows] for k in range(4)]
    sent = flip(jnp.concatenate([chunk[1], chunk[3]], axis=0), "row", 1)
    near = chunk[0].astype(jnp.float32) + sent[:rows].astype(jnp.float32)
    far = (chunk[2].astype(jnp.float32) + sent[rows:].astype(jnp.float32)).astype(jnp.bfloat16)
    return (near + flip(far, "row", 2).astype(jnp.float32)).astype(jnp.bfloat16)


def gather_row(values):
    count = lax.axis_size("row")
    index = lax.axis_index("row")
    got = [values] + [flip(values, "row", b) for b in range(1, count)]
    stacked = jnp.stack(got)
    order = jnp.arange(count, dtype=jnp.int32) ^ index
    return jnp.take(stacked, order, axis=0)


def received(values, axis):
    count = lax.axis_size(axis)
    return [values] + [
        lax.ppermute(values, axis, [(j, (j + s) % count) for j in range(count)])
        for s in range(1, count)
    ]


def head_project(pieces, weights, axis):
    row_count = lax.axis_size("row")
    count = len(pieces)
    rows, depth = pieces[0].shape
    part = weights[0].shape[1] // row_count
    groups = len(weights)
    index = jnp.stack([lax.axis_index(axis), lax.axis_index("row")]).astype(jnp.int32)

    def body(index_ref, *refs):
        x_refs = refs[:count]
        w_refs = refs[count : count + groups]
        o_ref = refs[-1]
        own = index_ref[0]
        for s in range(count):
            start = pl.multiple_of(((own - s + count) % count) * rows, 8)
            for g in range(groups):
                o_ref[0, pl.ds(start, rows), g * part : (g + 1) * part] = jnp.dot(
                    x_refs[s][...], w_refs[g][...], preferred_element_type=jnp.float32
                ).astype(o_ref.dtype)

    grid_spec = pltpu.PrefetchScalarGridSpec(
        num_scalar_prefetch=1,
        grid=(row_count,),
        in_specs=[pl.BlockSpec((rows, depth), lambda r, i: (0, 0)) for _ in pieces]
        + [pl.BlockSpec((depth, part), lambda r, i: (0, r)) for _ in weights],
        out_specs=pl.BlockSpec(
            (1, count * rows, groups * part),
            lambda r, i: ((r % 2 + i[1] % 2) % 2 + 2 * ((r // 2 + i[1] // 2) % 2), 0, 0),
        ),
    )
    summed = pl.pallas_call(
        body,
        grid_spec=grid_spec,
        out_shape=jax.ShapeDtypeStruct((row_count, count * rows, groups * part), jnp.bfloat16),
    )(index, *pieces, *weights)
    summed = summed.reshape(row_count * count * rows, groups * part)
    return scatter_row(summed)


def out_project_heads(attended, weight):
    row_count = lax.axis_size("row")
    whole = gather_row(attended)
    shaped = weight.reshape(row_count, weight.shape[0] // row_count, weight.shape[1])
    summed = jnp.einsum("rtf,rfo->to", whole, shaped, preferred_element_type=jnp.float32)
    return scatter_permute(summed.astype(jnp.bfloat16), "col")


def causal_attend(proj, blocks, shifts, place, carry=None, last=True):
    diagonal = 0 in shifts
    count = proj.shape[0]
    heads = proj.shape[1] // (3 * HD)
    steps = blocks.shape[0]
    scale = HD ** (-0.5)
    shift_table = jnp.asarray(shifts, jnp.int32)

    def body(place_ref, shift_ref, q_ref, kv_ref, *refs):
        if carry is None:
            outs = refs[:-3]
        else:
            peak_in, mass_in, acc_in = refs[:3]
            outs = refs[3:-3]
        peak_ref, mass_ref, acc_ref = refs[-3:]
        step = pl.program_id(0)
        shift = shift_ref[step]
        own = place_ref[0]

        @pl.when(step == 0)
        def _():
            if carry is None:
                peak_ref[...] = jnp.full(peak_ref.shape, -1e30, jnp.float32)
                mass_ref[...] = jnp.zeros(mass_ref.shape, jnp.float32)
                acc_ref[...] = jnp.zeros(acc_ref.shape, jnp.float32)
            else:
                peak_ref[...] = peak_in[...]
                mass_ref[...] = mass_in[...]
                acc_ref[...] = acc_in[...]

        def fold(masked):
            def one(h, unused):
                lane = pl.multiple_of(h * HD, HD)
                scores = lax.dot_general(
                    q_ref[:, pl.ds(lane, HD)],
                    kv_ref[:, pl.ds(lane, HD)],
                    (((1,), (1,)), ((), ())),
                    preferred_element_type=jnp.float32,
                ) * scale
                if masked:
                    rows = lax.broadcasted_iota(jnp.int32, scores.shape, 0)
                    cols = lax.broadcasted_iota(jnp.int32, scores.shape, 1)
                    allowed = cols <= rows
                    scores = jnp.where(allowed, scores, -1e30)
                old = peak_ref[h]
                new = jnp.maximum(old, jnp.max(scores, axis=1, keepdims=True))
                weights = jnp.exp(scores - new)
                if masked:
                    weights = jnp.where(allowed, weights, 0.0)
                shrink = jnp.exp(old - new)
                mass_ref[h] = shrink * mass_ref[h] + jnp.sum(weights, axis=1, keepdims=True)
                acc_ref[h] = shrink * acc_ref[h] + jnp.dot(
                    weights.astype(jnp.bfloat16),
                    kv_ref[:, pl.ds(lane + heads * HD, HD)],
                    preferred_element_type=jnp.float32,
                )
                peak_ref[h] = new
                return unused

            if diagonal:
                lax.fori_loop(0, heads, one, 0)
            else:
                for h in range(heads):
                    one(h, 0)

        @pl.when((shift > 0) & (shift <= own))
        def _():
            fold(False)

        if diagonal:

            @pl.when(shift == 0)
            def _():
                fold(True)

        @pl.when(step == steps - 1)
        def _():
            if last:
                for h in range(heads):
                    outs[0][:, h * HD : (h + 1) * HD] = (acc_ref[h] / mass_ref[h]).astype(
                        outs[0].dtype
                    )
            else:
                outs[0][...] = peak_ref[...]
                outs[1][...] = mass_ref[...]
                outs[2][...] = acc_ref[...]

    state_specs = [
        pl.BlockSpec((heads, count, 1), lambda j, p, s: (0, 0, 0)),
        pl.BlockSpec((heads, count, 1), lambda j, p, s: (0, 0, 0)),
        pl.BlockSpec((heads, count, HD), lambda j, p, s: (0, 0, 0)),
    ]
    state_shapes = [
        jax.ShapeDtypeStruct((heads, count, 1), jnp.float32),
        jax.ShapeDtypeStruct((heads, count, 1), jnp.float32),
        jax.ShapeDtypeStruct((heads, count, HD), jnp.float32),
    ]
    in_specs = [
        pl.BlockSpec((count, heads * HD), lambda j, p, s: (0, 0)),
        pl.BlockSpec((None, count, 2 * heads * HD), lambda j, p, s: (j, 0, 0)),
    ]
    if carry is not None:
        in_specs = in_specs + state_specs
    if last:
        out_specs = pl.BlockSpec((count, heads * HD), lambda j, p, s: (0, 0))
        out_shape = jax.ShapeDtypeStruct((count, heads * HD), jnp.bfloat16)
    else:
        out_specs = state_specs
        out_shape = state_shapes
    grid_spec = pltpu.PrefetchScalarGridSpec(
        num_scalar_prefetch=2,
        grid=(steps,),
        in_specs=in_specs,
        out_specs=out_specs,
        scratch_shapes=[
            pltpu.VMEM((heads, count, 1), jnp.float32),
            pltpu.VMEM((heads, count, 1), jnp.float32),
            pltpu.VMEM((heads, count, HD), jnp.float32),
        ],
    )
    extra = () if carry is None else tuple(carry)
    return pl.pallas_call(
        body,
        grid_spec=grid_spec,
        out_shape=out_shape,
    )(place, shift_table, proj, blocks, *extra)


def per_device(
    text_embed,
    vis_embed,
    vis_segment,
    vis_valid,
    vis_gain,
    vis_wq,
    vis_wk,
    vis_wv,
    vis_wo,
    dec_gain,
    dec_wq,
    dec_wk,
    dec_wv,
    dec_wo,
):
    row_count = lax.axis_size("row")
    col_count = lax.axis_size("col")
    width = vis_wq.shape[1]
    local = width // row_count
    margin = MAXIMG - 1
    piece_ids = gather_permute(jnp.stack([vis_segment, vis_valid], axis=1), "col").T
    piece_len = piece_ids.shape[1]
    framed_ids = with_halo(piece_ids, (("req", 1),), margin)
    total_slots = piece_len * lax.axis_size("req")
    prompt_rows = text_embed.shape[0]
    prompt_total = prompt_rows * lax.axis_size("req") * col_count
    window_len = piece_len + 2 * margin
    window_start = lax.axis_index("req") * piece_len - margin
    window_index = jnp.arange(window_len, dtype=jnp.int32)
    key_slots = window_start + window_index
    inside = (key_slots >= 0) & (key_slots < total_slots)
    key_segment = framed_ids[0]
    key_valid = framed_ids[1]
    begins = jnp.concatenate([jnp.ones((1,), jnp.bool_), key_segment[1:] != key_segment[:-1]])
    begins = begins | (key_slots == 0)
    image_first = lax.cummax(jnp.where(begins, key_slots, window_start), axis=0)
    target_window = image_first * prompt_total // total_slots + key_slots - image_first
    vis_cols = received(norm_local(vis_embed, vis_gain), "col")
    vis_proj = head_project(vis_cols, (vis_wq, vis_wk, vis_wv), "col")
    vis_pairs = jnp.stack([vis_proj[:, local : 2 * local], vis_proj[:, 2 * local :]])
    framed = with_halo(vis_pairs, (("req", 1),), margin)
    query_local = margin + jnp.arange(piece_len, dtype=jnp.int32)
    query_slots = window_start + query_local
    query_segment = key_segment[query_local]
    seen = (
        inside[None, :]
        & (query_segment[:, None] == key_segment[None, :])
        & ((key_valid[None, :] == 1) | (query_slots[:, None] == key_slots[None, :]))
    )
    vis_att = attend_block(vis_proj[:, :local], framed[0], framed[1], seen)
    vis_out = (vis_embed.astype(jnp.float32) + out_project_heads(vis_att, vis_wo)).astype(
        jnp.bfloat16
    )
    device_place = lax.axis_index("req") * col_count + lax.axis_index("col")
    owned = device_place * prompt_rows + jnp.arange(prompt_rows, dtype=jnp.int32)
    slot_rows = vis_out.shape[0]
    following = passed_along(vis_out, ("req", "col"), -1)
    near_rows = jnp.concatenate([vis_out, following], axis=0)
    near_local = (
        margin + lax.axis_index("col") * slot_rows + jnp.arange(2 * slot_rows, dtype=jnp.int32)
    )
    near_slots = window_start + near_local
    present = near_slots < total_slots
    near_target = jnp.where(present, target_window[near_local], -1)
    near_valid = key_valid[near_local]
    onehot = ((owned[:, None] == near_target[None, :]) & (near_valid[None, :] == 1)).astype(
        jnp.bfloat16
    )
    carried = jnp.dot(onehot, near_rows, preferred_element_type=jnp.float32)
    mixed = (text_embed.astype(jnp.float32) + carried).astype(jnp.bfloat16)
    dec_cols = received(norm_local(mixed, dec_gain), "col")
    dec_proj = head_project(dec_cols, (dec_wq, dec_wk, dec_wv), "col")
    dec_rows = dec_proj.shape[0]
    keyvals = dec_proj[:, local:]
    req_count = lax.axis_size("req")
    earlier = [keyvals] + [
        lax.ppermute(keyvals, "req", [(j, j + s) for j in range(req_count - s)])
        for s in range(1, req_count)
    ]
    place = lax.axis_index("req").astype(jnp.int32).reshape(1)
    near = [s for s in range(0, req_count, 2)]
    far = [s for s in range(1, req_count, 2)]
    state = causal_attend(
        dec_proj, jnp.stack([earlier[s] for s in near]), near, place, last=False
    )
    dec_att = causal_attend(
        dec_proj, jnp.stack([earlier[s] for s in far]), far, place, carry=state
    )
    return (mixed.astype(jnp.float32) + out_project_heads(dec_att, dec_wo)).astype(jnp.bfloat16)


def solution(mesh):
    return jax.shard_map(
        per_device,
        mesh=mesh,
        in_specs=(
            P(("req", "col"), "row"),
            P(("req", "col"), "row"),
            P(("req", "col")),
            P(("req", "col")),
            P("row"),
            P("row", "col"),
            P("row", "col"),
            P("row", "col"),
            P("col", "row"),
            P("row"),
            P("row", "col"),
            P("row", "col"),
            P("row", "col"),
            P("col", "row"),
        ),
        out_specs=P(("req", "col"), "row"),
        check_vma=False,
    )
```

```python
import jax
import jax.numpy as jnp
from jax import lax
from jax.sharding import PartitionSpec as P
from jax.experimental import pallas as pl
from jax.experimental.pallas import tpu as pltpu

D = 4096
HD = 128
MAXIMG = 256


def with_halo(cells, sides, width):
    for axis, dim in sides:
        count = lax.axis_size(axis)
        ends = count - 1
        head = lax.slice_in_dim(cells, 0, width, axis=dim)
        tail = lax.slice_in_dim(cells, cells.shape[dim] - width, cells.shape[dim], axis=dim)
        cells = jnp.concatenate(
            [
                lax.ppermute(tail, axis, [(i, (i + 1) % count) for i in range(ends)]),
                cells,
                lax.ppermute(head, axis, [((i + 1) % count, i) for i in range(ends)]),
            ],
            axis=dim,
        )
    return cells


def passed_along(shard, axis, by):
    size = lax.axis_size(axis)
    pairs = [(i, i + by) for i in range(size) if 0 <= i + by < size]
    return lax.ppermute(shard, axis, pairs)


def norm_local(values, gain):
    floats = values.astype(jnp.float32)
    squares = jnp.sum(floats * floats, axis=-1)
    totals = squares + flip(squares, "row", 1)
    totals = totals + flip(totals, "row", 2)
    factor = lax.rsqrt(totals / D + 1e-05)
    return (floats * factor[:, None] * gain.astype(jnp.float32)[None, :]).astype(jnp.bfloat16)


def gather_permute(values, axis):
    count = lax.axis_size(axis)
    index = lax.axis_index(axis)
    rows = values.shape[0]
    got = [values] + [
        lax.ppermute(values, axis, [(j, (j + s) % count) for j in range(count)])
        for s in range(1, count)
    ]
    ahead = jnp.concatenate([got[0]] + got[:0:-1], axis=0)
    twice = jnp.concatenate([ahead, ahead], axis=0)
    start = ((count - index) % count) * rows
    return lax.dynamic_slice_in_dim(twice, start, count * rows, axis=0)


def scatter_permute(values, axis):
    count = lax.axis_size(axis)
    index = lax.axis_index(axis)
    rows = values.shape[0] // count
    total = lax.dynamic_slice_in_dim(values, index * rows, rows, axis=0).astype(jnp.float32)
    for s in range(1, count):
        chunk = lax.dynamic_slice_in_dim(values, ((index + s) % count) * rows, rows, axis=0)
        total = total + lax.ppermute(
            chunk, axis, [(j, (j + s) % count) for j in range(count)]
        ).astype(jnp.float32)
    return total


def gather_cols(values):
    return gather_permute(values, "col")


def out_project(attended, weight):
    whole = lax.all_gather(attended, "row", axis=0, tiled=True)
    return lax.psum_scatter(
        jnp.dot(whole, weight, preferred_element_type=jnp.float32).astype(jnp.bfloat16),
        "col",
        scatter_dimension=0,
        tiled=True,
    ).astype(jnp.float32)


def split_heads(values):
    return values.reshape(values.shape[0], values.shape[1] // HD, HD)


def attend_block(queries, keys, values, allowed):
    query_heads = split_heads(queries)
    scores = jnp.einsum(
        "qhd,khd->hqk", query_heads, split_heads(keys), preferred_element_type=jnp.float32
    ) * HD ** (-0.5)
    scores = jnp.where(allowed[None], scores, -1e30)
    peak = jnp.max(scores, axis=-1, keepdims=True)
    weights = jnp.where(allowed[None], jnp.exp(scores - peak), 0.0)
    mass = jnp.sum(weights, axis=-1)
    summed = jnp.einsum(
        "hqk,khd->qhd",
        weights.astype(jnp.bfloat16),
        split_heads(values),
        preferred_element_type=jnp.float32,
    )
    result = summed / jnp.transpose(mass)[:, :, None]
    return result.reshape(queries.shape[0], queries.shape[1]).astype(jnp.bfloat16)


def fold_step(carry, query_heads, query_slots, key_heads, value_heads):
    peak, mass, accum = carry
    piece_slots = jnp.arange(key_heads.shape[0], dtype=jnp.int32)
    allowed = query_slots[:, None] >= piece_slots[None, :]
    scores = jnp.einsum(
        "qhd,khd->hqk", query_heads, key_heads, preferred_element_type=jnp.float32
    ) * HD ** (-0.5)
    scores = jnp.where(allowed[None], scores, -1e30)
    new_peak = jnp.maximum(peak, jnp.max(scores, axis=-1))
    weights = jnp.where(allowed[None], jnp.exp(scores - new_peak[:, :, None]), 0.0)
    summed = jnp.einsum(
        "hqk,khd->hqd",
        weights.astype(jnp.bfloat16),
        value_heads,
        preferred_element_type=jnp.float32,
    )
    return (new_peak, jnp.sum(weights, axis=-1), summed)


def start_state(head_count, query_count):
    return (
        jnp.full((head_count, query_count), -1e30, jnp.float32),
        jnp.zeros((head_count, query_count), jnp.float32),
        jnp.zeros((head_count, query_count, HD), jnp.float32),
    )


def flip(values, axis, bit):
    count = lax.axis_size(axis)
    return lax.ppermute(values, axis, [(j, j ^ bit) for j in range(count)])


def scatter_row(values):
    rows = values.shape[0] // 4
    chunk = [values[k * rows : (k + 1) * rows] for k in range(4)]
    sent = flip(jnp.concatenate([chunk[1], chunk[3]], axis=0), "row", 1)
    near = chunk[0].astype(jnp.float32) + sent[:rows].astype(jnp.float32)
    far = (chunk[2].astype(jnp.float32) + sent[rows:].astype(jnp.float32)).astype(jnp.bfloat16)
    return (near + flip(far, "row", 2).astype(jnp.float32)).astype(jnp.bfloat16)


def gather_row(values):
    count = lax.axis_size("row")
    index = lax.axis_index("row")
    got = [values] + [flip(values, "row", b) for b in range(1, count)]
    stacked = jnp.stack(got)
    order = jnp.arange(count, dtype=jnp.int32) ^ index
    return jnp.take(stacked, order, axis=0)


def received(values, axis):
    count = lax.axis_size(axis)
    return [values] + [
        lax.ppermute(values, axis, [(j, (j + s) % count) for j in range(count)])
        for s in range(1, count)
    ]


def head_project(pieces, weights, axis):
    row_count = lax.axis_size("row")
    count = len(pieces)
    rows, depth = pieces[0].shape
    part = weights[0].shape[1] // row_count
    groups = len(weights)
    index = jnp.stack([lax.axis_index(axis), lax.axis_index("row")]).astype(jnp.int32)

    def body(index_ref, *refs):
        x_refs = refs[:count]
        w_refs = refs[count : count + groups]
        o_ref = refs[-1]
        own = index_ref[0]
        for s in range(count):
            start = pl.multiple_of(((own - s + count) % count) * rows, 8)
            for g in range(groups):
                o_ref[0, pl.ds(start, rows), g * part : (g + 1) * part] = jnp.dot(
                    x_refs[s][...], w_refs[g][...], preferred_element_type=jnp.float32
                ).astype(o_ref.dtype)

    grid_spec = pltpu.PrefetchScalarGridSpec(
        num_scalar_prefetch=1,
        grid=(row_count,),
        in_specs=[pl.BlockSpec((rows, depth), lambda r, i: (0, 0)) for _ in pieces]
        + [pl.BlockSpec((depth, part), lambda r, i: (0, r)) for _ in weights],
        out_specs=pl.BlockSpec(
            (1, count * rows, groups * part),
            lambda r, i: ((r % 2 + i[1] % 2) % 2 + 2 * ((r // 2 + i[1] // 2) % 2), 0, 0),
        ),
    )
    summed = pl.pallas_call(
        body,
        grid_spec=grid_spec,
        out_shape=jax.ShapeDtypeStruct((row_count, count * rows, groups * part), jnp.bfloat16),
    )(index, *pieces, *weights)
    summed = summed.reshape(row_count * count * rows, groups * part)
    return scatter_row(summed)


def out_project_heads(attended, weight):
    row_count = lax.axis_size("row")
    whole = gather_row(attended)
    shaped = weight.reshape(row_count, weight.shape[0] // row_count, weight.shape[1])
    summed = jnp.einsum("rtf,rfo->to", whole, shaped, preferred_element_type=jnp.float32)
    return scatter_permute(summed.astype(jnp.bfloat16), "col")


def causal_attend(proj, blocks, shifts, place, carry=None, last=True):
    diagonal = 0 in shifts
    count = proj.shape[0]
    heads = proj.shape[1] // (3 * HD)
    steps = blocks.shape[0]
    scale = HD ** (-0.5)
    shift_table = jnp.asarray(shifts, jnp.int32)

    def body(place_ref, shift_ref, q_ref, kv_ref, *refs):
        if carry is None:
            outs = refs[:-3]
        else:
            peak_in, mass_in, acc_in = refs[:3]
            outs = refs[3:-3]
        peak_ref, mass_ref, acc_ref = refs[-3:]
        step = pl.program_id(0)
        shift = shift_ref[step]
        own = place_ref[0]

        @pl.when(step == 0)
        def _():
            if carry is None:
                peak_ref[...] = jnp.full(peak_ref.shape, -1e30, jnp.float32)
                mass_ref[...] = jnp.zeros(mass_ref.shape, jnp.float32)
                acc_ref[...] = jnp.zeros(acc_ref.shape, jnp.float32)
            else:
                peak_ref[...] = peak_in[...]
                mass_ref[...] = mass_in[...]
                acc_ref[...] = acc_in[...]

        def fold(masked):
            def one(h, unused):
                lane = pl.multiple_of(h * HD, HD)
                scores = lax.dot_general(
                    q_ref[:, pl.ds(lane, HD)],
                    kv_ref[:, pl.ds(lane, HD)],
                    (((1,), (1,)), ((), ())),
                    preferred_element_type=jnp.float32,
                ) * scale
                if masked:
                    rows = lax.broadcasted_iota(jnp.int32, scores.shape, 0)
                    cols = lax.broadcasted_iota(jnp.int32, scores.shape, 1)
                    allowed = cols <= rows
                    scores = jnp.where(allowed, scores, -1e30)
                old = peak_ref[h]
                new = jnp.maximum(old, jnp.max(scores, axis=1, keepdims=True))
                weights = jnp.exp(scores - new)
                if masked:
                    weights = jnp.where(allowed, weights, 0.0)
                shrink = jnp.exp(old - new)
                mass_ref[h] = shrink * mass_ref[h] + jnp.sum(weights, axis=1, keepdims=True)
                acc_ref[h] = shrink * acc_ref[h] + jnp.dot(
                    weights.astype(jnp.bfloat16),
                    kv_ref[:, pl.ds(lane + heads * HD, HD)],
                    preferred_element_type=jnp.float32,
                )
                peak_ref[h] = new
                return unused

            if diagonal:
                lax.fori_loop(0, heads, one, 0)
            else:
                for h in range(heads):
                    one(h, 0)

        if max(shifts) > 0:

            @pl.when((shift > 0) & (shift <= own))
            def _():
                fold(False)

        if diagonal:

            @pl.when(shift == 0)
            def _():
                fold(True)

        @pl.when(step == steps - 1)
        def _():
            if last:
                for h in range(heads):
                    outs[0][:, h * HD : (h + 1) * HD] = (acc_ref[h] / mass_ref[h]).astype(
                        outs[0].dtype
                    )
            else:
                outs[0][...] = peak_ref[...]
                outs[1][...] = mass_ref[...]
                outs[2][...] = acc_ref[...]

    state_specs = [
        pl.BlockSpec((heads, count, 1), lambda j, p, s: (0, 0, 0)),
        pl.BlockSpec((heads, count, 1), lambda j, p, s: (0, 0, 0)),
        pl.BlockSpec((heads, count, HD), lambda j, p, s: (0, 0, 0)),
    ]
    state_shapes = [
        jax.ShapeDtypeStruct((heads, count, 1), jnp.float32),
        jax.ShapeDtypeStruct((heads, count, 1), jnp.float32),
        jax.ShapeDtypeStruct((heads, count, HD), jnp.float32),
    ]
    in_specs = [
        pl.BlockSpec((count, heads * HD), lambda j, p, s: (0, 0)),
        pl.BlockSpec((None, count, 2 * heads * HD), lambda j, p, s: (j, 0, 0)),
    ]
    if carry is not None:
        in_specs = in_specs + state_specs
    if last:
        out_specs = pl.BlockSpec((count, heads * HD), lambda j, p, s: (0, 0))
        out_shape = jax.ShapeDtypeStruct((count, heads * HD), jnp.bfloat16)
    else:
        out_specs = state_specs
        out_shape = state_shapes
    grid_spec = pltpu.PrefetchScalarGridSpec(
        num_scalar_prefetch=2,
        grid=(steps,),
        in_specs=in_specs,
        out_specs=out_specs,
        scratch_shapes=[
            pltpu.VMEM((heads, count, 1), jnp.float32),
            pltpu.VMEM((heads, count, 1), jnp.float32),
            pltpu.VMEM((heads, count, HD), jnp.float32),
        ],
    )
    extra = () if carry is None else tuple(carry)
    return pl.pallas_call(
        body,
        grid_spec=grid_spec,
        out_shape=out_shape,
    )(place, shift_table, proj, blocks, *extra)


def per_device(
    text_embed,
    vis_embed,
    vis_segment,
    vis_valid,
    vis_gain,
    vis_wq,
    vis_wk,
    vis_wv,
    vis_wo,
    dec_gain,
    dec_wq,
    dec_wk,
    dec_wv,
    dec_wo,
):
    row_count = lax.axis_size("row")
    col_count = lax.axis_size("col")
    width = vis_wq.shape[1]
    local = width // row_count
    margin = MAXIMG - 1
    piece_ids = gather_permute(jnp.stack([vis_segment, vis_valid], axis=1), "col").T
    piece_len = piece_ids.shape[1]
    framed_ids = with_halo(piece_ids, (("req", 1),), margin)
    total_slots = piece_len * lax.axis_size("req")
    prompt_rows = text_embed.shape[0]
    prompt_total = prompt_rows * lax.axis_size("req") * col_count
    window_len = piece_len + 2 * margin
    window_start = lax.axis_index("req") * piece_len - margin
    window_index = jnp.arange(window_len, dtype=jnp.int32)
    key_slots = window_start + window_index
    inside = (key_slots >= 0) & (key_slots < total_slots)
    key_segment = framed_ids[0]
    key_valid = framed_ids[1]
    begins = jnp.concatenate([jnp.ones((1,), jnp.bool_), key_segment[1:] != key_segment[:-1]])
    begins = begins | (key_slots == 0)
    image_first = lax.cummax(jnp.where(begins, key_slots, window_start), axis=0)
    target_window = image_first * prompt_total // total_slots + key_slots - image_first
    vis_cols = received(norm_local(vis_embed, vis_gain), "col")
    vis_proj = head_project(vis_cols, (vis_wq, vis_wk, vis_wv), "col")
    vis_pairs = jnp.stack([vis_proj[:, local : 2 * local], vis_proj[:, 2 * local :]])
    framed = with_halo(vis_pairs, (("req", 1),), margin)
    query_local = margin + jnp.arange(piece_len, dtype=jnp.int32)
    query_slots = window_start + query_local
    query_segment = key_segment[query_local]
    seen = (
        inside[None, :]
        & (query_segment[:, None] == key_segment[None, :])
        & ((key_valid[None, :] == 1) | (query_slots[:, None] == key_slots[None, :]))
    )
    vis_att = attend_block(vis_proj[:, :local], framed[0], framed[1], seen)
    vis_out = (vis_embed.astype(jnp.float32) + out_project_heads(vis_att, vis_wo)).astype(
        jnp.bfloat16
    )
    device_place = lax.axis_index("req") * col_count + lax.axis_index("col")
    owned = device_place * prompt_rows + jnp.arange(prompt_rows, dtype=jnp.int32)
    slot_rows = vis_out.shape[0]
    following = passed_along(vis_out, ("req", "col"), -1)
    near_rows = jnp.concatenate([vis_out, following], axis=0)
    near_local = (
        margin + lax.axis_index("col") * slot_rows + jnp.arange(2 * slot_rows, dtype=jnp.int32)
    )
    near_slots = window_start + near_local
    present = near_slots < total_slots
    near_target = jnp.where(present, target_window[near_local], -1)
    near_valid = key_valid[near_local]
    onehot = ((owned[:, None] == near_target[None, :]) & (near_valid[None, :] == 1)).astype(
        jnp.bfloat16
    )
    carried = jnp.dot(onehot, near_rows, preferred_element_type=jnp.float32)
    mixed = (text_embed.astype(jnp.float32) + carried).astype(jnp.bfloat16)
    dec_cols = received(norm_local(mixed, dec_gain), "col")
    dec_proj = head_project(dec_cols, (dec_wq, dec_wk, dec_wv), "col")
    dec_rows = dec_proj.shape[0]
    keyvals = dec_proj[:, local:]
    req_count = lax.axis_size("req")
    earlier = [keyvals] + [
        lax.ppermute(keyvals, "req", [(j, j + s) for j in range(req_count - s)])
        for s in range(1, req_count)
    ]
    place = lax.axis_index("req").astype(jnp.int32).reshape(1)
    near = [0]
    far = list(range(1, req_count))
    state = causal_attend(
        dec_proj, jnp.stack([earlier[s] for s in near]), near, place, last=False
    )
    dec_att = causal_attend(
        dec_proj, jnp.stack([earlier[s] for s in far]), far, place, carry=state
    )
    return (mixed.astype(jnp.float32) + out_project_heads(dec_att, dec_wo)).astype(jnp.bfloat16)


def solution(mesh):
    return jax.shard_map(
        per_device,
        mesh=mesh,
        in_specs=(
            P(("req", "col"), "row"),
            P(("req", "col"), "row"),
            P(("req", "col")),
            P(("req", "col")),
            P("row"),
            P("row", "col"),
            P("row", "col"),
            P("row", "col"),
            P("col", "row"),
            P("row"),
            P("row", "col"),
            P("row", "col"),
            P("row", "col"),
            P("col", "row"),
        ),
        out_specs=P(("req", "col"), "row"),
        check_vma=False,
    )
```

```python
import jax
import jax.numpy as jnp
from jax import lax
from jax.sharding import PartitionSpec as P
from jax.experimental import pallas as pl
from jax.experimental.pallas import tpu as pltpu

D = 4096
HD = 128
MAXIMG = 256


def with_halo(cells, sides, width):
    for axis, dim in sides:
        count = lax.axis_size(axis)
        ends = count - 1
        head = lax.slice_in_dim(cells, 0, width, axis=dim)
        tail = lax.slice_in_dim(cells, cells.shape[dim] - width, cells.shape[dim], axis=dim)
        cells = jnp.concatenate(
            [
                lax.ppermute(tail, axis, [(i, (i + 1) % count) for i in range(ends)]),
                cells,
                lax.ppermute(head, axis, [((i + 1) % count, i) for i in range(ends)]),
            ],
            axis=dim,
        )
    return cells


def passed_along(shard, axis, by):
    size = lax.axis_size(axis)
    pairs = [(i, i + by) for i in range(size) if 0 <= i + by < size]
    return lax.ppermute(shard, axis, pairs)


def norm_local(values, gain):
    floats = values.astype(jnp.float32)
    squares = jnp.sum(floats * floats, axis=-1)
    totals = squares + flip(squares, "row", 1)
    totals = totals + flip(totals, "row", 2)
    factor = lax.rsqrt(totals / D + 1e-05)
    return (floats * factor[:, None] * gain.astype(jnp.float32)[None, :]).astype(jnp.bfloat16)


def gather_permute(values, axis):
    count = lax.axis_size(axis)
    index = lax.axis_index(axis)
    rows = values.shape[0]
    got = [values] + [
        lax.ppermute(values, axis, [(j, (j + s) % count) for j in range(count)])
        for s in range(1, count)
    ]
    ahead = jnp.concatenate([got[0]] + got[:0:-1], axis=0)
    twice = jnp.concatenate([ahead, ahead], axis=0)
    start = ((count - index) % count) * rows
    return lax.dynamic_slice_in_dim(twice, start, count * rows, axis=0)


def scatter_permute(values, axis):
    count = lax.axis_size(axis)
    index = lax.axis_index(axis)
    rows = values.shape[0] // count
    total = lax.dynamic_slice_in_dim(values, index * rows, rows, axis=0).astype(jnp.float32)
    for s in range(1, count):
        chunk = lax.dynamic_slice_in_dim(values, ((index + s) % count) * rows, rows, axis=0)
        total = total + lax.ppermute(
            chunk, axis, [(j, (j + s) % count) for j in range(count)]
        ).astype(jnp.float32)
    return total


def gather_cols(values):
    return gather_permute(values, "col")


def out_project(attended, weight):
    whole = lax.all_gather(attended, "row", axis=0, tiled=True)
    return lax.psum_scatter(
        jnp.dot(whole, weight, preferred_element_type=jnp.float32).astype(jnp.bfloat16),
        "col",
        scatter_dimension=0,
        tiled=True,
    ).astype(jnp.float32)


def split_heads(values):
    return values.reshape(values.shape[0], values.shape[1] // HD, HD)


def attend_block(queries, keys, values, allowed):
    query_heads = split_heads(queries)
    scores = jnp.einsum(
        "qhd,khd->hqk", query_heads, split_heads(keys), preferred_element_type=jnp.float32
    ) * HD ** (-0.5)
    scores = jnp.where(allowed[None], scores, -1e30)
    peak = jnp.max(scores, axis=-1, keepdims=True)
    weights = jnp.where(allowed[None], jnp.exp(scores - peak), 0.0)
    mass = jnp.sum(weights, axis=-1)
    summed = jnp.einsum(
        "hqk,khd->qhd",
        weights.astype(jnp.bfloat16),
        split_heads(values),
        preferred_element_type=jnp.float32,
    )
    result = summed / jnp.transpose(mass)[:, :, None]
    return result.reshape(queries.shape[0], queries.shape[1]).astype(jnp.bfloat16)


def fold_step(carry, query_heads, query_slots, key_heads, value_heads):
    peak, mass, accum = carry
    piece_slots = jnp.arange(key_heads.shape[0], dtype=jnp.int32)
    allowed = query_slots[:, None] >= piece_slots[None, :]
    scores = jnp.einsum(
        "qhd,khd->hqk", query_heads, key_heads, preferred_element_type=jnp.float32
    ) * HD ** (-0.5)
    scores = jnp.where(allowed[None], scores, -1e30)
    new_peak = jnp.maximum(peak, jnp.max(scores, axis=-1))
    weights = jnp.where(allowed[None], jnp.exp(scores - new_peak[:, :, None]), 0.0)
    summed = jnp.einsum(
        "hqk,khd->hqd",
        weights.astype(jnp.bfloat16),
        value_heads,
        preferred_element_type=jnp.float32,
    )
    return (new_peak, jnp.sum(weights, axis=-1), summed)


def start_state(head_count, query_count):
    return (
        jnp.full((head_count, query_count), -1e30, jnp.float32),
        jnp.zeros((head_count, query_count), jnp.float32),
        jnp.zeros((head_count, query_count, HD), jnp.float32),
    )


def flip(values, axis, bit):
    count = lax.axis_size(axis)
    return lax.ppermute(values, axis, [(j, j ^ bit) for j in range(count)])


def scatter_row(values):
    rows = values.shape[0] // 4
    chunk = [values[k * rows : (k + 1) * rows] for k in range(4)]
    sent = flip(jnp.concatenate([chunk[1], chunk[3]], axis=0), "row", 1)
    near = chunk[0].astype(jnp.float32) + sent[:rows].astype(jnp.float32)
    far = (chunk[2].astype(jnp.float32) + sent[rows:].astype(jnp.float32)).astype(jnp.bfloat16)
    return (near + flip(far, "row", 2).astype(jnp.float32)).astype(jnp.bfloat16)


def gather_row(values):
    count = lax.axis_size("row")
    index = lax.axis_index("row")
    got = [values] + [flip(values, "row", b) for b in range(1, count)]
    stacked = jnp.stack(got)
    order = jnp.arange(count, dtype=jnp.int32) ^ index
    return jnp.take(stacked, order, axis=0)


def received(values, axis):
    count = lax.axis_size(axis)
    return [values] + [
        lax.ppermute(values, axis, [(j, (j + s) % count) for j in range(count)])
        for s in range(1, count)
    ]


def head_project(pieces, weights, axis):
    row_count = lax.axis_size("row")
    count = len(pieces)
    rows, depth = pieces[0].shape
    part = weights[0].shape[1] // row_count
    groups = len(weights)
    index = jnp.stack([lax.axis_index(axis), lax.axis_index("row")]).astype(jnp.int32)

    def body(index_ref, *refs):
        x_refs = refs[:count]
        w_refs = refs[count : count + groups]
        o_ref = refs[-1]
        own = index_ref[0]
        for s in range(count):
            start = pl.multiple_of(((own - s + count) % count) * rows, 8)
            for g in range(groups):
                o_ref[0, pl.ds(start, rows), g * part : (g + 1) * part] = jnp.dot(
                    x_refs[s][...], w_refs[g][...], preferred_element_type=jnp.float32
                ).astype(o_ref.dtype)

    grid_spec = pltpu.PrefetchScalarGridSpec(
        num_scalar_prefetch=1,
        grid=(row_count,),
        in_specs=[pl.BlockSpec((rows, depth), lambda r, i: (0, 0)) for _ in pieces]
        + [pl.BlockSpec((depth, part), lambda r, i: (0, r)) for _ in weights],
        out_specs=pl.BlockSpec(
            (1, count * rows, groups * part),
            lambda r, i: ((r % 2 + i[1] % 2) % 2 + 2 * ((r // 2 + i[1] // 2) % 2), 0, 0),
        ),
    )
    summed = pl.pallas_call(
        body,
        grid_spec=grid_spec,
        out_shape=jax.ShapeDtypeStruct((row_count, count * rows, groups * part), jnp.bfloat16),
    )(index, *pieces, *weights)
    summed = summed.reshape(row_count * count * rows, groups * part)
    return scatter_row(summed)


def out_project_heads(attended, weight):
    row_count = lax.axis_size("row")
    whole = gather_row(attended)
    shaped = weight.reshape(row_count, weight.shape[0] // row_count, weight.shape[1])
    summed = jnp.einsum("rtf,rfo->to", whole, shaped, preferred_element_type=jnp.float32)
    return scatter_permute(summed.astype(jnp.bfloat16), "col")


def causal_attend(proj, blocks, shifts, place, carry=None, last=True):
    diagonal = 0 in shifts
    count = proj.shape[0]
    heads = proj.shape[1] // (3 * HD)
    steps = blocks.shape[0]
    scale = HD ** (-0.5)
    shift_table = jnp.asarray(shifts, jnp.int32)

    def body(place_ref, shift_ref, q_ref, kv_ref, *refs):
        if carry is None:
            outs = refs[:-3]
        else:
            peak_in, mass_in, acc_in = refs[:3]
            outs = refs[3:-3]
        peak_ref, mass_ref, acc_ref = refs[-3:]
        step = pl.program_id(0)
        shift = shift_ref[step]
        own = place_ref[0]

        @pl.when(step == 0)
        def _():
            if carry is None:
                peak_ref[...] = jnp.full(peak_ref.shape, -1e30, jnp.float32)
                mass_ref[...] = jnp.zeros(mass_ref.shape, jnp.float32)
                acc_ref[...] = jnp.zeros(acc_ref.shape, jnp.float32)
            else:
                peak_ref[...] = peak_in[...]
                mass_ref[...] = mass_in[...]
                acc_ref[...] = acc_in[...]

        def fold(masked):
            def one(h, unused):
                lane = pl.multiple_of(h * HD, HD)
                scores = lax.dot_general(
                    q_ref[:, pl.ds(lane, HD)],
                    kv_ref[:, pl.ds(lane, HD)],
                    (((1,), (1,)), ((), ())),
                    preferred_element_type=jnp.float32,
                ) * scale
                if masked:
                    rows = lax.broadcasted_iota(jnp.int32, scores.shape, 0)
                    cols = lax.broadcasted_iota(jnp.int32, scores.shape, 1)
                    allowed = cols <= rows
                    scores = jnp.where(allowed, scores, -1e30)
                old = peak_ref[h]
                new = jnp.maximum(old, jnp.max(scores, axis=1, keepdims=True))
                weights = jnp.exp(scores - new)
                if masked:
                    weights = jnp.where(allowed, weights, 0.0)
                shrink = jnp.exp(old - new)
                mass_ref[h] = shrink * mass_ref[h] + jnp.sum(weights, axis=1, keepdims=True)
                acc_ref[h] = shrink * acc_ref[h] + jnp.dot(
                    weights.astype(jnp.bfloat16),
                    kv_ref[:, pl.ds(lane + heads * HD, HD)],
                    preferred_element_type=jnp.float32,
                )
                peak_ref[h] = new
                return unused

            if diagonal:
                lax.fori_loop(0, heads, one, 0)
            else:
                for h in range(heads):
                    one(h, 0)

        if max(shifts) > 0:

            @pl.when((shift > 0) & (shift <= own))
            def _():
                fold(False)

        if diagonal:

            @pl.when(shift == 0)
            def _():
                fold(True)

        @pl.when(step == steps - 1)
        def _():
            if last:
                for h in range(heads):
                    outs[0][:, h * HD : (h + 1) * HD] = (acc_ref[h] / mass_ref[h]).astype(
                        outs[0].dtype
                    )
            else:
                outs[0][...] = peak_ref[...]
                outs[1][...] = mass_ref[...]
                outs[2][...] = acc_ref[...]

    state_specs = [
        pl.BlockSpec((heads, count, 1), lambda j, p, s: (0, 0, 0)),
        pl.BlockSpec((heads, count, 1), lambda j, p, s: (0, 0, 0)),
        pl.BlockSpec((heads, count, HD), lambda j, p, s: (0, 0, 0)),
    ]
    state_shapes = [
        jax.ShapeDtypeStruct((heads, count, 1), jnp.float32),
        jax.ShapeDtypeStruct((heads, count, 1), jnp.float32),
        jax.ShapeDtypeStruct((heads, count, HD), jnp.float32),
    ]
    in_specs = [
        pl.BlockSpec((count, heads * HD), lambda j, p, s: (0, 0)),
        pl.BlockSpec((None, count, 2 * heads * HD), lambda j, p, s: (j, 0, 0)),
    ]
    if carry is not None:
        in_specs = in_specs + state_specs
    if last:
        out_specs = pl.BlockSpec((count, heads * HD), lambda j, p, s: (0, 0))
        out_shape = jax.ShapeDtypeStruct((count, heads * HD), jnp.bfloat16)
    else:
        out_specs = state_specs
        out_shape = state_shapes
    grid_spec = pltpu.PrefetchScalarGridSpec(
        num_scalar_prefetch=2,
        grid=(steps,),
        in_specs=in_specs,
        out_specs=out_specs,
        scratch_shapes=[
            pltpu.VMEM((heads, count, 1), jnp.float32),
            pltpu.VMEM((heads, count, 1), jnp.float32),
            pltpu.VMEM((heads, count, HD), jnp.float32),
        ],
    )
    extra = () if carry is None else tuple(carry)
    return pl.pallas_call(
        body,
        grid_spec=grid_spec,
        out_shape=out_shape,
    )(place, shift_table, proj, blocks, *extra)


def per_device(
    text_embed,
    vis_embed,
    vis_segment,
    vis_valid,
    vis_gain,
    vis_wq,
    vis_wk,
    vis_wv,
    vis_wo,
    dec_gain,
    dec_wq,
    dec_wk,
    dec_wv,
    dec_wo,
):
    row_count = lax.axis_size("row")
    col_count = lax.axis_size("col")
    width = vis_wq.shape[1]
    local = width // row_count
    margin = MAXIMG - 1
    piece_ids = gather_permute(jnp.stack([vis_segment, vis_valid], axis=1), "col").T
    piece_len = piece_ids.shape[1]
    total_slots = piece_len * lax.axis_size("req")
    prompt_rows = text_embed.shape[0]
    prompt_total = prompt_rows * lax.axis_size("req") * col_count
    window_len = piece_len + 2 * margin
    window_start = lax.axis_index("req") * piece_len - margin
    window_index = jnp.arange(window_len, dtype=jnp.int32)
    key_slots = window_start + window_index
    inside = (key_slots >= 0) & (key_slots < total_slots)
    vis_cols = received(norm_local(vis_embed, vis_gain), "col")
    vis_proj = head_project(vis_cols, (vis_wq, vis_wk, vis_wv), "col")
    id_plane = jnp.concatenate(
        [piece_ids.T.astype(jnp.bfloat16), jnp.zeros((piece_len, local - 2), jnp.bfloat16)], axis=1
    )
    vis_pairs = jnp.stack([vis_proj[:, local : 2 * local], vis_proj[:, 2 * local :], id_plane])
    framed = with_halo(vis_pairs, (("req", 1),), margin)
    key_segment = framed[2, :, 0].astype(jnp.int32)
    key_valid = framed[2, :, 1].astype(jnp.int32)
    begins = jnp.concatenate([jnp.ones((1,), jnp.bool_), key_segment[1:] != key_segment[:-1]])
    begins = begins | (key_slots == 0)
    image_first = lax.cummax(jnp.where(begins, key_slots, window_start), axis=0)
    target_window = image_first * prompt_total // total_slots + key_slots - image_first
    query_local = margin + jnp.arange(piece_len, dtype=jnp.int32)
    query_slots = window_start + query_local
    query_segment = key_segment[query_local]
    seen = (
        inside[None, :]
        & (query_segment[:, None] == key_segment[None, :])
        & ((key_valid[None, :] == 1) | (query_slots[:, None] == key_slots[None, :]))
    )
    vis_att = attend_block(vis_proj[:, :local], framed[0], framed[1], seen)
    vis_out = (vis_embed.astype(jnp.float32) + out_project_heads(vis_att, vis_wo)).astype(
        jnp.bfloat16
    )
    device_place = lax.axis_index("req") * col_count + lax.axis_index("col")
    owned = device_place * prompt_rows + jnp.arange(prompt_rows, dtype=jnp.int32)
    slot_rows = vis_out.shape[0]
    following = passed_along(vis_out, ("req", "col"), -1)
    near_rows = jnp.concatenate([vis_out, following], axis=0)
    near_local = (
        margin + lax.axis_index("col") * slot_rows + jnp.arange(2 * slot_rows, dtype=jnp.int32)
    )
    near_slots = window_start + near_local
    present = near_slots < total_slots
    near_target = jnp.where(present, target_window[near_local], -1)
    near_valid = key_valid[near_local]
    onehot = ((owned[:, None] == near_target[None, :]) & (near_valid[None, :] == 1)).astype(
        jnp.bfloat16
    )
    carried = jnp.dot(onehot, near_rows, preferred_element_type=jnp.float32)
    mixed = (text_embed.astype(jnp.float32) + carried).astype(jnp.bfloat16)
    dec_cols = received(norm_local(mixed, dec_gain), "col")
    dec_proj = head_project(dec_cols, (dec_wq, dec_wk, dec_wv), "col")
    dec_rows = dec_proj.shape[0]
    keyvals = dec_proj[:, local:]
    req_count = lax.axis_size("req")
    earlier = [keyvals] + [
        lax.ppermute(keyvals, "req", [(j, j + s) for j in range(req_count - s)])
        for s in range(1, req_count)
    ]
    place = lax.axis_index("req").astype(jnp.int32).reshape(1)
    near = [0]
    far = list(range(1, req_count))
    state = causal_attend(
        dec_proj, jnp.stack([earlier[s] for s in near]), near, place, last=False
    )
    dec_att = causal_attend(
        dec_proj, jnp.stack([earlier[s] for s in far]), far, place, carry=state
    )
    return (mixed.astype(jnp.float32) + out_project_heads(dec_att, dec_wo)).astype(jnp.bfloat16)


def solution(mesh):
    return jax.shard_map(
        per_device,
        mesh=mesh,
        in_specs=(
            P(("req", "col"), "row"),
            P(("req", "col"), "row"),
            P(("req", "col")),
            P(("req", "col")),
            P("row"),
            P("row", "col"),
            P("row", "col"),
            P("row", "col"),
            P("col", "row"),
            P("row"),
            P("row", "col"),
            P("row", "col"),
            P("row", "col"),
            P("col", "row"),
        ),
        out_specs=P(("req", "col"), "row"),
        check_vma=False,
    )
```

```python
import jax
import jax.numpy as jnp
from jax import lax
from jax.sharding import PartitionSpec as P
from jax.experimental import pallas as pl
from jax.experimental.pallas import tpu as pltpu

D = 4096
HD = 128
MAXIMG = 256


def with_halo(cells, sides, width):
    for axis, dim in sides:
        count = lax.axis_size(axis)
        ends = count - 1
        head = lax.slice_in_dim(cells, 0, width, axis=dim)
        tail = lax.slice_in_dim(cells, cells.shape[dim] - width, cells.shape[dim], axis=dim)
        cells = jnp.concatenate(
            [
                lax.ppermute(tail, axis, [(i, (i + 1) % count) for i in range(ends)]),
                cells,
                lax.ppermute(head, axis, [((i + 1) % count, i) for i in range(ends)]),
            ],
            axis=dim,
        )
    return cells


def passed_along(shard, axis, by):
    size = lax.axis_size(axis)
    pairs = [(i, i + by) for i in range(size) if 0 <= i + by < size]
    return lax.ppermute(shard, axis, pairs)


def norm_local(values, gain):
    floats = values.astype(jnp.float32)
    squares = jnp.sum(floats * floats, axis=-1)
    totals = squares + flip(squares, "row", 1)
    totals = totals + flip(totals, "row", 2)
    factor = lax.rsqrt(totals / D + 1e-05)
    return (floats * factor[:, None] * gain.astype(jnp.float32)[None, :]).astype(jnp.bfloat16)


def gather_permute(values, axis):
    count = lax.axis_size(axis)
    index = lax.axis_index(axis)
    rows = values.shape[0]
    got = [values] + [
        lax.ppermute(values, axis, [(j, (j + s) % count) for j in range(count)])
        for s in range(1, count)
    ]
    ahead = jnp.concatenate([got[0]] + got[:0:-1], axis=0)
    twice = jnp.concatenate([ahead, ahead], axis=0)
    start = ((count - index) % count) * rows
    return lax.dynamic_slice_in_dim(twice, start, count * rows, axis=0)


def scatter_permute(values, axis):
    count = lax.axis_size(axis)
    index = lax.axis_index(axis)
    rows = values.shape[0] // count
    total = lax.dynamic_slice_in_dim(values, index * rows, rows, axis=0).astype(jnp.float32)
    for s in range(1, count):
        chunk = lax.dynamic_slice_in_dim(values, ((index + s) % count) * rows, rows, axis=0)
        total = total + lax.ppermute(
            chunk, axis, [(j, (j + s) % count) for j in range(count)]
        ).astype(jnp.float32)
    return total


def gather_cols(values):
    return gather_permute(values, "col")


def out_project(attended, weight):
    whole = lax.all_gather(attended, "row", axis=0, tiled=True)
    return lax.psum_scatter(
        jnp.dot(whole, weight, preferred_element_type=jnp.float32).astype(jnp.bfloat16),
        "col",
        scatter_dimension=0,
        tiled=True,
    ).astype(jnp.float32)


def split_heads(values):
    return values.reshape(values.shape[0], values.shape[1] // HD, HD)


def attend_block(queries, keys, values, allowed):
    query_heads = split_heads(queries)
    scores = jnp.einsum(
        "qhd,khd->hqk", query_heads, split_heads(keys), preferred_element_type=jnp.float32
    ) * HD ** (-0.5)
    scores = jnp.where(allowed[None], scores, -1e30)
    peak = jnp.max(scores, axis=-1, keepdims=True)
    weights = jnp.where(allowed[None], jnp.exp(scores - peak), 0.0)
    mass = jnp.sum(weights, axis=-1)
    summed = jnp.einsum(
        "hqk,khd->qhd",
        weights.astype(jnp.bfloat16),
        split_heads(values),
        preferred_element_type=jnp.float32,
    )
    result = summed / jnp.transpose(mass)[:, :, None]
    return result.reshape(queries.shape[0], queries.shape[1]).astype(jnp.bfloat16)


def fold_step(carry, query_heads, query_slots, key_heads, value_heads):
    peak, mass, accum = carry
    piece_slots = jnp.arange(key_heads.shape[0], dtype=jnp.int32)
    allowed = query_slots[:, None] >= piece_slots[None, :]
    scores = jnp.einsum(
        "qhd,khd->hqk", query_heads, key_heads, preferred_element_type=jnp.float32
    ) * HD ** (-0.5)
    scores = jnp.where(allowed[None], scores, -1e30)
    new_peak = jnp.maximum(peak, jnp.max(scores, axis=-1))
    weights = jnp.where(allowed[None], jnp.exp(scores - new_peak[:, :, None]), 0.0)
    summed = jnp.einsum(
        "hqk,khd->hqd",
        weights.astype(jnp.bfloat16),
        value_heads,
        preferred_element_type=jnp.float32,
    )
    return (new_peak, jnp.sum(weights, axis=-1), summed)


def start_state(head_count, query_count):
    return (
        jnp.full((head_count, query_count), -1e30, jnp.float32),
        jnp.zeros((head_count, query_count), jnp.float32),
        jnp.zeros((head_count, query_count, HD), jnp.float32),
    )


def flip(values, axis, bit):
    count = lax.axis_size(axis)
    return lax.ppermute(values, axis, [(j, j ^ bit) for j in range(count)])


def scatter_row(values):
    rows = values.shape[0] // 4
    chunk = [values[k * rows : (k + 1) * rows] for k in range(4)]
    sent = flip(jnp.concatenate([chunk[1], chunk[3]], axis=0), "row", 1)
    near = chunk[0].astype(jnp.float32) + sent[:rows].astype(jnp.float32)
    far = (chunk[2].astype(jnp.float32) + sent[rows:].astype(jnp.float32)).astype(jnp.bfloat16)
    return (near + flip(far, "row", 2).astype(jnp.float32)).astype(jnp.bfloat16)


def gather_row(values):
    count = lax.axis_size("row")
    index = lax.axis_index("row")
    got = [values] + [flip(values, "row", b) for b in range(1, count)]
    stacked = jnp.stack(got)
    order = jnp.arange(count, dtype=jnp.int32) ^ index
    return jnp.take(stacked, order, axis=0)


def received(values, axis):
    count = lax.axis_size(axis)
    return [values] + [
        lax.ppermute(values, axis, [(j, (j + s) % count) for j in range(count)])
        for s in range(1, count)
    ]


def head_project(pieces, weights, axis):
    row_count = lax.axis_size("row")
    count = len(pieces)
    rows, depth = pieces[0].shape
    part = weights[0].shape[1] // row_count
    groups = len(weights)
    index = jnp.stack([lax.axis_index(axis), lax.axis_index("row")]).astype(jnp.int32)

    def body(index_ref, *refs):
        x_refs = refs[:count]
        w_refs = refs[count : count + groups]
        o_ref = refs[-1]
        own = index_ref[0]
        for s in range(count):
            start = pl.multiple_of(((own - s + count) % count) * rows, 8)
            for g in range(groups):
                o_ref[0, pl.ds(start, rows), g * part : (g + 1) * part] = jnp.dot(
                    x_refs[s][...], w_refs[g][...], preferred_element_type=jnp.float32
                ).astype(o_ref.dtype)

    grid_spec = pltpu.PrefetchScalarGridSpec(
        num_scalar_prefetch=1,
        grid=(row_count,),
        in_specs=[pl.BlockSpec((rows, depth), lambda r, i: (0, 0)) for _ in pieces]
        + [pl.BlockSpec((depth, part), lambda r, i: (0, r)) for _ in weights],
        out_specs=pl.BlockSpec(
            (1, count * rows, groups * part),
            lambda r, i: ((r % 2 + i[1] % 2) % 2 + 2 * ((r // 2 + i[1] // 2) % 2), 0, 0),
        ),
    )
    summed = pl.pallas_call(
        body,
        grid_spec=grid_spec,
        out_shape=jax.ShapeDtypeStruct((row_count, count * rows, groups * part), jnp.bfloat16),
    )(index, *pieces, *weights)
    summed = summed.reshape(row_count * count * rows, groups * part)
    return scatter_row(summed)


def out_project_heads(attended, weight):
    row_count = lax.axis_size("row")
    col_count = lax.axis_size("col")
    pieces = [attended] + [flip(attended, "row", b) for b in range(1, row_count)]
    count, width = attended.shape
    rows = count // col_count
    index = jnp.stack([lax.axis_index("row"), lax.axis_index("col")]).astype(jnp.int32)

    def body(index_ref, *refs):
        piece_refs = refs[:row_count]
        w_ref = refs[row_count]
        o_ref = refs[-1]
        own = index_ref[0]
        place = index_ref[1]
        for s in range(col_count):
            start = pl.multiple_of(((place + s) % col_count) * rows, 8)
            total = None
            for b in range(row_count):
                source = (own % 2 + b % 2) % 2 + 2 * ((own // 2 + b // 2) % 2)
                first = pl.multiple_of(source * width, 8)
                part = jnp.dot(
                    piece_refs[b][pl.ds(start, rows), :],
                    w_ref[pl.ds(first, width), :],
                    preferred_element_type=jnp.float32,
                )
                total = part if total is None else total + part
            o_ref[s] = total.astype(o_ref.dtype)

    grid_spec = pltpu.PrefetchScalarGridSpec(
        num_scalar_prefetch=1,
        grid=(1,),
        in_specs=[pl.BlockSpec((count, width), lambda i, x: (0, 0)) for _ in pieces]
        + [pl.BlockSpec(weight.shape, lambda i, x: (0, 0))],
        out_specs=pl.BlockSpec((col_count, rows, weight.shape[1]), lambda i, x: (0, 0, 0)),
    )
    parts = pl.pallas_call(
        body,
        grid_spec=grid_spec,
        out_shape=jax.ShapeDtypeStruct((col_count, rows, weight.shape[1]), jnp.bfloat16),
    )(index, *pieces, weight)
    total = parts[0].astype(jnp.float32)
    for s in range(1, col_count):
        total = total + lax.ppermute(
            parts[s], "col", [(j, (j + s) % col_count) for j in range(col_count)]
        ).astype(jnp.float32)
    return total


def causal_attend(proj, blocks, shifts, place, carry=None, last=True):
    diagonal = 0 in shifts
    count = proj.shape[0]
    heads = proj.shape[1] // (3 * HD)
    steps = blocks.shape[0]
    scale = HD ** (-0.5)
    shift_table = jnp.asarray(shifts, jnp.int32)

    def body(place_ref, shift_ref, q_ref, kv_ref, *refs):
        if carry is None:
            outs = refs[:-3]
        else:
            peak_in, mass_in, acc_in = refs[:3]
            outs = refs[3:-3]
        peak_ref, mass_ref, acc_ref = refs[-3:]
        step = pl.program_id(0)
        shift = shift_ref[step]
        own = place_ref[0]

        @pl.when(step == 0)
        def _():
            if carry is None:
                peak_ref[...] = jnp.full(peak_ref.shape, -1e30, jnp.float32)
                mass_ref[...] = jnp.zeros(mass_ref.shape, jnp.float32)
                acc_ref[...] = jnp.zeros(acc_ref.shape, jnp.float32)
            else:
                peak_ref[...] = peak_in[...]
                mass_ref[...] = mass_in[...]
                acc_ref[...] = acc_in[...]

        def fold(masked):
            def one(h, unused):
                lane = pl.multiple_of(h * HD, HD)
                scores = lax.dot_general(
                    q_ref[:, pl.ds(lane, HD)],
                    kv_ref[:, pl.ds(lane, HD)],
                    (((1,), (1,)), ((), ())),
                    preferred_element_type=jnp.float32,
                ) * scale
                if masked:
                    rows = lax.broadcasted_iota(jnp.int32, scores.shape, 0)
                    cols = lax.broadcasted_iota(jnp.int32, scores.shape, 1)
                    allowed = cols <= rows
                    scores = jnp.where(allowed, scores, -1e30)
                old = peak_ref[h]
                new = jnp.maximum(old, jnp.max(scores, axis=1, keepdims=True))
                weights = jnp.exp(scores - new)
                if masked:
                    weights = jnp.where(allowed, weights, 0.0)
                shrink = jnp.exp(old - new)
                mass_ref[h] = shrink * mass_ref[h] + jnp.sum(weights, axis=1, keepdims=True)
                acc_ref[h] = shrink * acc_ref[h] + jnp.dot(
                    weights.astype(jnp.bfloat16),
                    kv_ref[:, pl.ds(lane + heads * HD, HD)],
                    preferred_element_type=jnp.float32,
                )
                peak_ref[h] = new
                return unused

            if diagonal:
                lax.fori_loop(0, heads, one, 0)
            else:
                for h in range(heads):
                    one(h, 0)

        if max(shifts) > 0:

            @pl.when((shift > 0) & (shift <= own))
            def _():
                fold(False)

        if diagonal:

            @pl.when(shift == 0)
            def _():
                fold(True)

        @pl.when(step == steps - 1)
        def _():
            if last:
                for h in range(heads):
                    outs[0][:, h * HD : (h + 1) * HD] = (acc_ref[h] / mass_ref[h]).astype(
                        outs[0].dtype
                    )
            else:
                outs[0][...] = peak_ref[...]
                outs[1][...] = mass_ref[...]
                outs[2][...] = acc_ref[...]

    state_specs = [
        pl.BlockSpec((heads, count, 1), lambda j, p, s: (0, 0, 0)),
        pl.BlockSpec((heads, count, 1), lambda j, p, s: (0, 0, 0)),
        pl.BlockSpec((heads, count, HD), lambda j, p, s: (0, 0, 0)),
    ]
    state_shapes = [
        jax.ShapeDtypeStruct((heads, count, 1), jnp.float32),
        jax.ShapeDtypeStruct((heads, count, 1), jnp.float32),
        jax.ShapeDtypeStruct((heads, count, HD), jnp.float32),
    ]
    in_specs = [
        pl.BlockSpec((count, heads * HD), lambda j, p, s: (0, 0)),
        pl.BlockSpec((None, count, 2 * heads * HD), lambda j, p, s: (j, 0, 0)),
    ]
    if carry is not None:
        in_specs = in_specs + state_specs
    if last:
        out_specs = pl.BlockSpec((count, heads * HD), lambda j, p, s: (0, 0))
        out_shape = jax.ShapeDtypeStruct((count, heads * HD), jnp.bfloat16)
    else:
        out_specs = state_specs
        out_shape = state_shapes
    grid_spec = pltpu.PrefetchScalarGridSpec(
        num_scalar_prefetch=2,
        grid=(steps,),
        in_specs=in_specs,
        out_specs=out_specs,
        scratch_shapes=[
            pltpu.VMEM((heads, count, 1), jnp.float32),
            pltpu.VMEM((heads, count, 1), jnp.float32),
            pltpu.VMEM((heads, count, HD), jnp.float32),
        ],
    )
    extra = () if carry is None else tuple(carry)
    return pl.pallas_call(
        body,
        grid_spec=grid_spec,
        out_shape=out_shape,
    )(place, shift_table, proj, blocks, *extra)


def per_device(
    text_embed,
    vis_embed,
    vis_segment,
    vis_valid,
    vis_gain,
    vis_wq,
    vis_wk,
    vis_wv,
    vis_wo,
    dec_gain,
    dec_wq,
    dec_wk,
    dec_wv,
    dec_wo,
):
    row_count = lax.axis_size("row")
    col_count = lax.axis_size("col")
    width = vis_wq.shape[1]
    local = width // row_count
    margin = MAXIMG - 1
    piece_ids = gather_permute(jnp.stack([vis_segment, vis_valid], axis=1), "col").T
    piece_len = piece_ids.shape[1]
    framed_ids = with_halo(piece_ids, (("req", 1),), margin)
    total_slots = piece_len * lax.axis_size("req")
    prompt_rows = text_embed.shape[0]
    prompt_total = prompt_rows * lax.axis_size("req") * col_count
    window_len = piece_len + 2 * margin
    window_start = lax.axis_index("req") * piece_len - margin
    window_index = jnp.arange(window_len, dtype=jnp.int32)
    key_slots = window_start + window_index
    inside = (key_slots >= 0) & (key_slots < total_slots)
    key_segment = framed_ids[0]
    key_valid = framed_ids[1]
    begins = jnp.concatenate([jnp.ones((1,), jnp.bool_), key_segment[1:] != key_segment[:-1]])
    begins = begins | (key_slots == 0)
    image_first = lax.cummax(jnp.where(begins, key_slots, window_start), axis=0)
    target_window = image_first * prompt_total // total_slots + key_slots - image_first
    vis_cols = received(norm_local(vis_embed, vis_gain), "col")
    vis_proj = head_project(vis_cols, (vis_wq, vis_wk, vis_wv), "col")
    vis_pairs = jnp.stack([vis_proj[:, local : 2 * local], vis_proj[:, 2 * local :]])
    framed = with_halo(vis_pairs, (("req", 1),), margin)
    query_local = margin + jnp.arange(piece_len, dtype=jnp.int32)
    query_slots = window_start + query_local
    query_segment = key_segment[query_local]
    seen = (
        inside[None, :]
        & (query_segment[:, None] == key_segment[None, :])
        & ((key_valid[None, :] == 1) | (query_slots[:, None] == key_slots[None, :]))
    )
    vis_att = attend_block(vis_proj[:, :local], framed[0], framed[1], seen)
    vis_out = (vis_embed.astype(jnp.float32) + out_project_heads(vis_att, vis_wo)).astype(
        jnp.bfloat16
    )
    device_place = lax.axis_index("req") * col_count + lax.axis_index("col")
    owned = device_place * prompt_rows + jnp.arange(prompt_rows, dtype=jnp.int32)
    slot_rows = vis_out.shape[0]
    following = passed_along(vis_out, ("req", "col"), -1)
    near_rows = jnp.concatenate([vis_out, following], axis=0)
    near_local = (
        margin + lax.axis_index("col") * slot_rows + jnp.arange(2 * slot_rows, dtype=jnp.int32)
    )
    near_slots = window_start + near_local
    present = near_slots < total_slots
    near_target = jnp.where(present, target_window[near_local], -1)
    near_valid = key_valid[near_local]
    onehot = ((owned[:, None] == near_target[None, :]) & (near_valid[None, :] == 1)).astype(
        jnp.bfloat16
    )
    carried = jnp.dot(onehot, near_rows, preferred_element_type=jnp.float32)
    mixed = (text_embed.astype(jnp.float32) + carried).astype(jnp.bfloat16)
    dec_cols = received(norm_local(mixed, dec_gain), "col")
    dec_proj = head_project(dec_cols, (dec_wq, dec_wk, dec_wv), "col")
    dec_rows = dec_proj.shape[0]
    keyvals = dec_proj[:, local:]
    req_count = lax.axis_size("req")
    earlier = [keyvals] + [
        lax.ppermute(keyvals, "req", [(j, j + s) for j in range(req_count - s)])
        for s in range(1, req_count)
    ]
    place = lax.axis_index("req").astype(jnp.int32).reshape(1)
    near = [0]
    far = list(range(1, req_count))
    state = causal_attend(
        dec_proj, jnp.stack([earlier[s] for s in near]), near, place, last=False
    )
    dec_att = causal_attend(
        dec_proj, jnp.stack([earlier[s] for s in far]), far, place, carry=state
    )
    return (mixed.astype(jnp.float32) + out_project_heads(dec_att, dec_wo)).astype(jnp.bfloat16)


def solution(mesh):
    return jax.shard_map(
        per_device,
        mesh=mesh,
        in_specs=(
            P(("req", "col"), "row"),
            P(("req", "col"), "row"),
            P(("req", "col")),
            P(("req", "col")),
            P("row"),
            P("row", "col"),
            P("row", "col"),
            P("row", "col"),
            P("col", "row"),
            P("row"),
            P("row", "col"),
            P("row", "col"),
            P("row", "col"),
            P("col", "row"),
        ),
        out_specs=P(("req", "col"), "row"),
        check_vma=False,
    )
```

```python
import jax
import jax.numpy as jnp
from jax import lax
from jax.sharding import PartitionSpec as P
from jax.experimental import pallas as pl
from jax.experimental.pallas import tpu as pltpu

D = 4096
HD = 128
MAXIMG = 256


def with_halo(cells, sides, width):
    for axis, dim in sides:
        count = lax.axis_size(axis)
        ends = count - 1
        head = lax.slice_in_dim(cells, 0, width, axis=dim)
        tail = lax.slice_in_dim(cells, cells.shape[dim] - width, cells.shape[dim], axis=dim)
        cells = jnp.concatenate(
            [
                lax.ppermute(tail, axis, [(i, (i + 1) % count) for i in range(ends)]),
                cells,
                lax.ppermute(head, axis, [((i + 1) % count, i) for i in range(ends)]),
            ],
            axis=dim,
        )
    return cells


def passed_along(shard, axis, by):
    size = lax.axis_size(axis)
    pairs = [(i, i + by) for i in range(size) if 0 <= i + by < size]
    return lax.ppermute(shard, axis, pairs)


def norm_local(values, gain):
    floats = values.astype(jnp.float32)
    squares = jnp.sum(floats * floats, axis=-1)
    totals = squares + flip(squares, "row", 1)
    totals = totals + flip(totals, "row", 2)
    factor = lax.rsqrt(totals / D + 1e-05)
    return (floats * factor[:, None] * gain.astype(jnp.float32)[None, :]).astype(jnp.bfloat16)


def gather_permute(values, axis):
    count = lax.axis_size(axis)
    index = lax.axis_index(axis)
    rows = values.shape[0]
    got = [values] + [
        lax.ppermute(values, axis, [(j, (j + s) % count) for j in range(count)])
        for s in range(1, count)
    ]
    ahead = jnp.concatenate([got[0]] + got[:0:-1], axis=0)
    twice = jnp.concatenate([ahead, ahead], axis=0)
    start = ((count - index) % count) * rows
    return lax.dynamic_slice_in_dim(twice, start, count * rows, axis=0)


def scatter_permute(values, axis):
    count = lax.axis_size(axis)
    index = lax.axis_index(axis)
    rows = values.shape[0] // count
    total = lax.dynamic_slice_in_dim(values, index * rows, rows, axis=0).astype(jnp.float32)
    for s in range(1, count):
        chunk = lax.dynamic_slice_in_dim(values, ((index + s) % count) * rows, rows, axis=0)
        total = total + lax.ppermute(
            chunk, axis, [(j, (j + s) % count) for j in range(count)]
        ).astype(jnp.float32)
    return total


def gather_cols(values):
    return gather_permute(values, "col")


def out_project(attended, weight):
    whole = lax.all_gather(attended, "row", axis=0, tiled=True)
    return lax.psum_scatter(
        jnp.dot(whole, weight, preferred_element_type=jnp.float32).astype(jnp.bfloat16),
        "col",
        scatter_dimension=0,
        tiled=True,
    ).astype(jnp.float32)


def split_heads(values):
    return values.reshape(values.shape[0], values.shape[1] // HD, HD)


def attend_block(queries, keys, values, allowed):
    query_heads = split_heads(queries)
    scores = jnp.einsum(
        "qhd,khd->hqk", query_heads, split_heads(keys), preferred_element_type=jnp.float32
    ) * HD ** (-0.5)
    scores = jnp.where(allowed[None], scores, -1e30)
    peak = jnp.max(scores, axis=-1, keepdims=True)
    weights = jnp.where(allowed[None], jnp.exp(scores - peak), 0.0)
    mass = jnp.sum(weights, axis=-1)
    summed = jnp.einsum(
        "hqk,khd->qhd",
        weights.astype(jnp.bfloat16),
        split_heads(values),
        preferred_element_type=jnp.float32,
    )
    result = summed / jnp.transpose(mass)[:, :, None]
    return result.reshape(queries.shape[0], queries.shape[1]).astype(jnp.bfloat16)


def fold_step(carry, query_heads, query_slots, key_heads, value_heads):
    peak, mass, accum = carry
    piece_slots = jnp.arange(key_heads.shape[0], dtype=jnp.int32)
    allowed = query_slots[:, None] >= piece_slots[None, :]
    scores = jnp.einsum(
        "qhd,khd->hqk", query_heads, key_heads, preferred_element_type=jnp.float32
    ) * HD ** (-0.5)
    scores = jnp.where(allowed[None], scores, -1e30)
    new_peak = jnp.maximum(peak, jnp.max(scores, axis=-1))
    weights = jnp.where(allowed[None], jnp.exp(scores - new_peak[:, :, None]), 0.0)
    summed = jnp.einsum(
        "hqk,khd->hqd",
        weights.astype(jnp.bfloat16),
        value_heads,
        preferred_element_type=jnp.float32,
    )
    return (new_peak, jnp.sum(weights, axis=-1), summed)


def start_state(head_count, query_count):
    return (
        jnp.full((head_count, query_count), -1e30, jnp.float32),
        jnp.zeros((head_count, query_count), jnp.float32),
        jnp.zeros((head_count, query_count, HD), jnp.float32),
    )


def flip(values, axis, bit):
    count = lax.axis_size(axis)
    return lax.ppermute(values, axis, [(j, j ^ bit) for j in range(count)])


def scatter_row(keep, send):
    sent = flip(send, "row", 1)
    near = keep[0].astype(jnp.float32) + sent[0].astype(jnp.float32)
    far = (keep[1].astype(jnp.float32) + sent[1].astype(jnp.float32)).astype(jnp.bfloat16)
    return (near + flip(far, "row", 2).astype(jnp.float32)).astype(jnp.bfloat16)


def gather_row(values):
    count = lax.axis_size("row")
    index = lax.axis_index("row")
    got = [values] + [flip(values, "row", b) for b in range(1, count)]
    stacked = jnp.stack(got)
    order = jnp.arange(count, dtype=jnp.int32) ^ index
    return jnp.take(stacked, order, axis=0)


def received(values, axis):
    count = lax.axis_size(axis)
    return [values] + [
        lax.ppermute(values, axis, [(j, (j + s) % count) for j in range(count)])
        for s in range(1, count)
    ]


def head_project(pieces, weights, axis):
    row_count = lax.axis_size("row")
    count = len(pieces)
    rows, depth = pieces[0].shape
    part = weights[0].shape[1] // row_count
    groups = len(weights)
    index = jnp.stack([lax.axis_index(axis), lax.axis_index("row")]).astype(jnp.int32)

    def body(index_ref, *refs):
        x_refs = refs[:count]
        w_refs = refs[count : count + groups]
        keep_ref, send_ref = refs[-2:]
        own = index_ref[0]
        low = index_ref[1] % 2
        for s in range(count):
            start = pl.multiple_of(((own - s + count) % count) * rows, 8)
            for g in range(groups):
                both = jnp.dot(x_refs[s][...], w_refs[g][...], preferred_element_type=jnp.float32)
                first, second = both[:, :part], both[:, part:]
                kept = jnp.where(low == 0, first, second)
                given = jnp.where(low == 0, second, first)
                keep_ref[0, pl.ds(start, rows), g * part : (g + 1) * part] = kept.astype(
                    keep_ref.dtype
                )
                send_ref[0, pl.ds(start, rows), g * part : (g + 1) * part] = given.astype(
                    send_ref.dtype
                )

    half = row_count // 2
    block = pl.BlockSpec((1, count * rows, groups * part), lambda g, i: (g, 0, 0))
    grid_spec = pltpu.PrefetchScalarGridSpec(
        num_scalar_prefetch=1,
        grid=(half,),
        in_specs=[pl.BlockSpec((rows, depth), lambda g, i: (0, 0)) for _ in pieces]
        + [
            pl.BlockSpec((depth, 2 * part), lambda g, i: (0, (i[1] // 2 + g) % 2))
            for _ in weights
        ],
        out_specs=[block, block],
    )
    shape = jax.ShapeDtypeStruct((half, count * rows, groups * part), jnp.bfloat16)
    keep, send = pl.pallas_call(
        body,
        grid_spec=grid_spec,
        out_shape=[shape, shape],
    )(index, *pieces, *weights)
    return scatter_row(keep, send)


def out_project_heads(attended, weight):
    row_count = lax.axis_size("row")
    col_count = lax.axis_size("col")
    pieces = [attended] + [flip(attended, "row", b) for b in range(1, row_count)]
    count, width = attended.shape
    rows = count // col_count
    index = jnp.stack([lax.axis_index("row"), lax.axis_index("col")]).astype(jnp.int32)

    def body(index_ref, *refs):
        piece_refs = refs[:row_count]
        w_ref = refs[row_count]
        o_ref = refs[-1]
        own = index_ref[0]
        place = index_ref[1]
        for s in range(col_count):
            start = pl.multiple_of(((place + s) % col_count) * rows, 8)
            total = None
            for b in range(row_count):
                source = (own % 2 + b % 2) % 2 + 2 * ((own // 2 + b // 2) % 2)
                first = pl.multiple_of(source * width, 8)
                part = jnp.dot(
                    piece_refs[b][pl.ds(start, rows), :],
                    w_ref[pl.ds(first, width), :],
                    preferred_element_type=jnp.float32,
                )
                total = part if total is None else total + part
            o_ref[s] = total.astype(o_ref.dtype)

    grid_spec = pltpu.PrefetchScalarGridSpec(
        num_scalar_prefetch=1,
        grid=(1,),
        in_specs=[pl.BlockSpec((count, width), lambda i, x: (0, 0)) for _ in pieces]
        + [pl.BlockSpec(weight.shape, lambda i, x: (0, 0))],
        out_specs=pl.BlockSpec((col_count, rows, weight.shape[1]), lambda i, x: (0, 0, 0)),
    )
    parts = pl.pallas_call(
        body,
        grid_spec=grid_spec,
        out_shape=jax.ShapeDtypeStruct((col_count, rows, weight.shape[1]), jnp.bfloat16),
    )(index, *pieces, weight)
    total = parts[0].astype(jnp.float32)
    for s in range(1, col_count):
        total = total + lax.ppermute(
            parts[s], "col", [(j, (j + s) % col_count) for j in range(col_count)]
        ).astype(jnp.float32)
    return total


def causal_attend(proj, blocks, shifts, place, carry=None, last=True):
    diagonal = 0 in shifts
    count = proj.shape[0]
    heads = proj.shape[1] // (3 * HD)
    steps = blocks.shape[0]
    scale = HD ** (-0.5)
    shift_table = jnp.asarray(shifts, jnp.int32)

    def body(place_ref, shift_ref, q_ref, kv_ref, *refs):
        if carry is None:
            outs = refs[:-3]
        else:
            peak_in, mass_in, acc_in = refs[:3]
            outs = refs[3:-3]
        peak_ref, mass_ref, acc_ref = refs[-3:]
        step = pl.program_id(0)
        shift = shift_ref[step]
        own = place_ref[0]

        @pl.when(step == 0)
        def _():
            if carry is None:
                peak_ref[...] = jnp.full(peak_ref.shape, -1e30, jnp.float32)
                mass_ref[...] = jnp.zeros(mass_ref.shape, jnp.float32)
                acc_ref[...] = jnp.zeros(acc_ref.shape, jnp.float32)
            else:
                peak_ref[...] = peak_in[...]
                mass_ref[...] = mass_in[...]
                acc_ref[...] = acc_in[...]

        def fold(masked):
            def one(h, unused):
                lane = pl.multiple_of(h * HD, HD)
                scores = lax.dot_general(
                    q_ref[:, pl.ds(lane, HD)],
                    kv_ref[:, pl.ds(lane, HD)],
                    (((1,), (1,)), ((), ())),
                    preferred_element_type=jnp.float32,
                ) * scale
                if masked:
                    rows = lax.broadcasted_iota(jnp.int32, scores.shape, 0)
                    cols = lax.broadcasted_iota(jnp.int32, scores.shape, 1)
                    allowed = cols <= rows
                    scores = jnp.where(allowed, scores, -1e30)
                old = peak_ref[h]
                new = jnp.maximum(old, jnp.max(scores, axis=1, keepdims=True))
                weights = jnp.exp(scores - new)
                if masked:
                    weights = jnp.where(allowed, weights, 0.0)
                shrink = jnp.exp(old - new)
                mass_ref[h] = shrink * mass_ref[h] + jnp.sum(weights, axis=1, keepdims=True)
                acc_ref[h] = shrink * acc_ref[h] + jnp.dot(
                    weights.astype(jnp.bfloat16),
                    kv_ref[:, pl.ds(lane + heads * HD, HD)],
                    preferred_element_type=jnp.float32,
                )
                peak_ref[h] = new
                return unused

            if diagonal:
                lax.fori_loop(0, heads, one, 0)
            else:
                for h in range(heads):
                    one(h, 0)

        if max(shifts) > 0:

            @pl.when((shift > 0) & (shift <= own))
            def _():
                fold(False)

        if diagonal:

            @pl.when(shift == 0)
            def _():
                fold(True)

        @pl.when(step == steps - 1)
        def _():
            if last:
                for h in range(heads):
                    outs[0][:, h * HD : (h + 1) * HD] = (acc_ref[h] / mass_ref[h]).astype(
                        outs[0].dtype
                    )
            else:
                outs[0][...] = peak_ref[...]
                outs[1][...] = mass_ref[...]
                outs[2][...] = acc_ref[...]

    state_specs = [
        pl.BlockSpec((heads, count, 1), lambda j, p, s: (0, 0, 0)),
        pl.BlockSpec((heads, count, 1), lambda j, p, s: (0, 0, 0)),
        pl.BlockSpec((heads, count, HD), lambda j, p, s: (0, 0, 0)),
    ]
    state_shapes = [
        jax.ShapeDtypeStruct((heads, count, 1), jnp.float32),
        jax.ShapeDtypeStruct((heads, count, 1), jnp.float32),
        jax.ShapeDtypeStruct((heads, count, HD), jnp.float32),
    ]
    in_specs = [
        pl.BlockSpec((count, heads * HD), lambda j, p, s: (0, 0)),
        pl.BlockSpec((None, count, 2 * heads * HD), lambda j, p, s: (j, 0, 0)),
    ]
    if carry is not None:
        in_specs = in_specs + state_specs
    if last:
        out_specs = pl.BlockSpec((count, heads * HD), lambda j, p, s: (0, 0))
        out_shape = jax.ShapeDtypeStruct((count, heads * HD), jnp.bfloat16)
    else:
        out_specs = state_specs
        out_shape = state_shapes
    grid_spec = pltpu.PrefetchScalarGridSpec(
        num_scalar_prefetch=2,
        grid=(steps,),
        in_specs=in_specs,
        out_specs=out_specs,
        scratch_shapes=[
            pltpu.VMEM((heads, count, 1), jnp.float32),
            pltpu.VMEM((heads, count, 1), jnp.float32),
            pltpu.VMEM((heads, count, HD), jnp.float32),
        ],
    )
    extra = () if carry is None else tuple(carry)
    return pl.pallas_call(
        body,
        grid_spec=grid_spec,
        out_shape=out_shape,
    )(place, shift_table, proj, blocks, *extra)


def per_device(
    text_embed,
    vis_embed,
    vis_segment,
    vis_valid,
    vis_gain,
    vis_wq,
    vis_wk,
    vis_wv,
    vis_wo,
    dec_gain,
    dec_wq,
    dec_wk,
    dec_wv,
    dec_wo,
):
    row_count = lax.axis_size("row")
    col_count = lax.axis_size("col")
    width = vis_wq.shape[1]
    local = width // row_count
    margin = MAXIMG - 1
    piece_ids = gather_permute(jnp.stack([vis_segment, vis_valid], axis=1), "col").T
    piece_len = piece_ids.shape[1]
    framed_ids = with_halo(piece_ids, (("req", 1),), margin)
    total_slots = piece_len * lax.axis_size("req")
    prompt_rows = text_embed.shape[0]
    prompt_total = prompt_rows * lax.axis_size("req") * col_count
    window_len = piece_len + 2 * margin
    window_start = lax.axis_index("req") * piece_len - margin
    window_index = jnp.arange(window_len, dtype=jnp.int32)
    key_slots = window_start + window_index
    inside = (key_slots >= 0) & (key_slots < total_slots)
    key_segment = framed_ids[0]
    key_valid = framed_ids[1]
    begins = jnp.concatenate([jnp.ones((1,), jnp.bool_), key_segment[1:] != key_segment[:-1]])
    begins = begins | (key_slots == 0)
    image_first = lax.cummax(jnp.where(begins, key_slots, window_start), axis=0)
    target_window = image_first * prompt_total // total_slots + key_slots - image_first
    vis_cols = received(norm_local(vis_embed, vis_gain), "col")
    vis_proj = head_project(vis_cols, (vis_wq, vis_wk, vis_wv), "col")
    vis_pairs = jnp.stack([vis_proj[:, local : 2 * local], vis_proj[:, 2 * local :]])
    framed = with_halo(vis_pairs, (("req", 1),), margin)
    query_local = margin + jnp.arange(piece_len, dtype=jnp.int32)
    query_slots = window_start + query_local
    query_segment = key_segment[query_local]
    seen = (
        inside[None, :]
        & (query_segment[:, None] == key_segment[None, :])
        & ((key_valid[None, :] == 1) | (query_slots[:, None] == key_slots[None, :]))
    )
    vis_att = attend_block(vis_proj[:, :local], framed[0], framed[1], seen)
    vis_out = (vis_embed.astype(jnp.float32) + out_project_heads(vis_att, vis_wo)).astype(
        jnp.bfloat16
    )
    device_place = lax.axis_index("req") * col_count + lax.axis_index("col")
    owned = device_place * prompt_rows + jnp.arange(prompt_rows, dtype=jnp.int32)
    slot_rows = vis_out.shape[0]
    following = passed_along(vis_out, ("req", "col"), -1)
    near_rows = jnp.concatenate([vis_out, following], axis=0)
    near_local = (
        margin + lax.axis_index("col") * slot_rows + jnp.arange(2 * slot_rows, dtype=jnp.int32)
    )
    near_slots = window_start + near_local
    present = near_slots < total_slots
    near_target = jnp.where(present, target_window[near_local], -1)
    near_valid = key_valid[near_local]
    onehot = ((owned[:, None] == near_target[None, :]) & (near_valid[None, :] == 1)).astype(
        jnp.bfloat16
    )
    carried = jnp.dot(onehot, near_rows, preferred_element_type=jnp.float32)
    mixed = (text_embed.astype(jnp.float32) + carried).astype(jnp.bfloat16)
    dec_cols = received(norm_local(mixed, dec_gain), "col")
    dec_proj = head_project(dec_cols, (dec_wq, dec_wk, dec_wv), "col")
    dec_rows = dec_proj.shape[0]
    keyvals = dec_proj[:, local:]
    req_count = lax.axis_size("req")
    earlier = [keyvals] + [
        lax.ppermute(keyvals, "req", [(j, j + s) for j in range(req_count - s)])
        for s in range(1, req_count)
    ]
    place = lax.axis_index("req").astype(jnp.int32).reshape(1)
    near = [0]
    far = list(range(1, req_count))
    state = causal_attend(
        dec_proj, jnp.stack([earlier[s] for s in near]), near, place, last=False
    )
    dec_att = causal_attend(
        dec_proj, jnp.stack([earlier[s] for s in far]), far, place, carry=state
    )
    return (mixed.astype(jnp.float32) + out_project_heads(dec_att, dec_wo)).astype(jnp.bfloat16)


def solution(mesh):
    return jax.shard_map(
        per_device,
        mesh=mesh,
        in_specs=(
            P(("req", "col"), "row"),
            P(("req", "col"), "row"),
            P(("req", "col")),
            P(("req", "col")),
            P("row"),
            P("row", "col"),
            P("row", "col"),
            P("row", "col"),
            P("col", "row"),
            P("row"),
            P("row", "col"),
            P("row", "col"),
            P("row", "col"),
            P("col", "row"),
        ),
        out_specs=P(("req", "col"), "row"),
        check_vma=False,
    )
```

```python
import jax
import jax.numpy as jnp
from jax import lax
from jax.sharding import PartitionSpec as P
from jax.experimental import pallas as pl
from jax.experimental.pallas import tpu as pltpu

D = 4096
HD = 128
MAXIMG = 256


def with_halo(cells, sides, width):
    for axis, dim in sides:
        count = lax.axis_size(axis)
        ends = count - 1
        head = lax.slice_in_dim(cells, 0, width, axis=dim)
        tail = lax.slice_in_dim(cells, cells.shape[dim] - width, cells.shape[dim], axis=dim)
        cells = jnp.concatenate(
            [
                lax.ppermute(tail, axis, [(i, (i + 1) % count) for i in range(ends)]),
                cells,
                lax.ppermute(head, axis, [((i + 1) % count, i) for i in range(ends)]),
            ],
            axis=dim,
        )
    return cells


def passed_along(shard, axis, by):
    size = lax.axis_size(axis)
    pairs = [(i, i + by) for i in range(size) if 0 <= i + by < size]
    return lax.ppermute(shard, axis, pairs)


def norm_local(values, gain):
    floats = values.astype(jnp.float32)
    squares = jnp.sum(floats * floats, axis=-1)
    totals = squares + flip(squares, "row", 1)
    totals = totals + flip(totals, "row", 2)
    factor = lax.rsqrt(totals / D + 1e-05)
    return (floats * factor[:, None] * gain.astype(jnp.float32)[None, :]).astype(jnp.bfloat16)


def gather_permute(values, axis):
    count = lax.axis_size(axis)
    index = lax.axis_index(axis)
    rows = values.shape[0]
    got = [values] + [
        lax.ppermute(values, axis, [(j, (j + s) % count) for j in range(count)])
        for s in range(1, count)
    ]
    ahead = jnp.concatenate([got[0]] + got[:0:-1], axis=0)
    twice = jnp.concatenate([ahead, ahead], axis=0)
    start = ((count - index) % count) * rows
    return lax.dynamic_slice_in_dim(twice, start, count * rows, axis=0)


def scatter_permute(values, axis):
    count = lax.axis_size(axis)
    index = lax.axis_index(axis)
    rows = values.shape[0] // count
    total = lax.dynamic_slice_in_dim(values, index * rows, rows, axis=0).astype(jnp.float32)
    for s in range(1, count):
        chunk = lax.dynamic_slice_in_dim(values, ((index + s) % count) * rows, rows, axis=0)
        total = total + lax.ppermute(
            chunk, axis, [(j, (j + s) % count) for j in range(count)]
        ).astype(jnp.float32)
    return total


def gather_cols(values):
    return gather_permute(values, "col")


def out_project(attended, weight):
    whole = lax.all_gather(attended, "row", axis=0, tiled=True)
    return lax.psum_scatter(
        jnp.dot(whole, weight, preferred_element_type=jnp.float32).astype(jnp.bfloat16),
        "col",
        scatter_dimension=0,
        tiled=True,
    ).astype(jnp.float32)


def split_heads(values):
    return values.reshape(values.shape[0], values.shape[1] // HD, HD)


def attend_block(queries, keys, values, allowed):
    query_heads = split_heads(queries)
    scores = jnp.einsum(
        "qhd,khd->hqk", query_heads, split_heads(keys), preferred_element_type=jnp.float32
    ) * HD ** (-0.5)
    scores = jnp.where(allowed[None], scores, -1e30)
    peak = jnp.max(scores, axis=-1, keepdims=True)
    weights = jnp.where(allowed[None], jnp.exp(scores - peak), 0.0)
    mass = jnp.sum(weights, axis=-1)
    summed = jnp.einsum(
        "hqk,khd->qhd",
        weights.astype(jnp.bfloat16),
        split_heads(values),
        preferred_element_type=jnp.float32,
    )
    result = summed / jnp.transpose(mass)[:, :, None]
    return result.reshape(queries.shape[0], queries.shape[1]).astype(jnp.bfloat16)


def fold_step(carry, query_heads, query_slots, key_heads, value_heads):
    peak, mass, accum = carry
    piece_slots = jnp.arange(key_heads.shape[0], dtype=jnp.int32)
    allowed = query_slots[:, None] >= piece_slots[None, :]
    scores = jnp.einsum(
        "qhd,khd->hqk", query_heads, key_heads, preferred_element_type=jnp.float32
    ) * HD ** (-0.5)
    scores = jnp.where(allowed[None], scores, -1e30)
    new_peak = jnp.maximum(peak, jnp.max(scores, axis=-1))
    weights = jnp.where(allowed[None], jnp.exp(scores - new_peak[:, :, None]), 0.0)
    summed = jnp.einsum(
        "hqk,khd->hqd",
        weights.astype(jnp.bfloat16),
        value_heads,
        preferred_element_type=jnp.float32,
    )
    return (new_peak, jnp.sum(weights, axis=-1), summed)


def start_state(head_count, query_count):
    return (
        jnp.full((head_count, query_count), -1e30, jnp.float32),
        jnp.zeros((head_count, query_count), jnp.float32),
        jnp.zeros((head_count, query_count, HD), jnp.float32),
    )


def flip(values, axis, bit):
    count = lax.axis_size(axis)
    return lax.ppermute(values, axis, [(j, j ^ bit) for j in range(count)])


def scatter_row(keep, send):
    sent = flip(send, "row", 1)
    near = keep[0].astype(jnp.float32) + sent[0].astype(jnp.float32)
    far = (keep[1].astype(jnp.float32) + sent[1].astype(jnp.float32)).astype(jnp.bfloat16)
    return (near + flip(far, "row", 2).astype(jnp.float32)).astype(jnp.bfloat16)


def gather_row(values):
    count = lax.axis_size("row")
    index = lax.axis_index("row")
    got = [values] + [flip(values, "row", b) for b in range(1, count)]
    stacked = jnp.stack(got)
    order = jnp.arange(count, dtype=jnp.int32) ^ index
    return jnp.take(stacked, order, axis=0)


def received(values, axis):
    count = lax.axis_size(axis)
    return [values] + [
        lax.ppermute(values, axis, [(j, (j + s) % count) for j in range(count)])
        for s in range(1, count)
    ]


def head_project(pieces, weights, axis):
    row_count = lax.axis_size("row")
    count = len(pieces)
    rows, depth = pieces[0].shape
    part = weights[0].shape[1] // row_count
    groups = len(weights)
    index = jnp.stack([lax.axis_index(axis), lax.axis_index("row")]).astype(jnp.int32)

    def body(index_ref, *refs):
        x_refs = refs[:count]
        w_refs = refs[count : count + groups]
        keep_ref, send_ref = refs[-2:]
        own = index_ref[0]
        low = index_ref[1] % 2
        for s in range(count):
            start = pl.multiple_of(((own - s + count) % count) * rows, 8)
            for g in range(groups):
                both = jnp.dot(x_refs[s][...], w_refs[g][...], preferred_element_type=jnp.float32)
                first, second = both[:, :part], both[:, part:]
                kept = jnp.where(low == 0, first, second)
                given = jnp.where(low == 0, second, first)
                keep_ref[0, pl.ds(start, rows), g * part : (g + 1) * part] = kept.astype(
                    keep_ref.dtype
                )
                send_ref[0, pl.ds(start, rows), g * part : (g + 1) * part] = given.astype(
                    send_ref.dtype
                )

    half = row_count // 2
    block = pl.BlockSpec((1, count * rows, groups * part), lambda g, i: (g, 0, 0))
    grid_spec = pltpu.PrefetchScalarGridSpec(
        num_scalar_prefetch=1,
        grid=(half,),
        in_specs=[pl.BlockSpec((rows, depth), lambda g, i: (0, 0)) for _ in pieces]
        + [
            pl.BlockSpec((depth, 2 * part), lambda g, i: (0, (i[1] // 2 + g) % 2))
            for _ in weights
        ],
        out_specs=[block, block],
    )
    shape = jax.ShapeDtypeStruct((half, count * rows, groups * part), jnp.bfloat16)
    keep, send = pl.pallas_call(
        body,
        grid_spec=grid_spec,
        out_shape=[shape, shape],
    )(index, *pieces, *weights)
    return scatter_row(keep, send)


def out_project_heads(attended, weight):
    row_count = lax.axis_size("row")
    col_count = lax.axis_size("col")
    pieces = [attended] + [flip(attended, "row", b) for b in range(1, row_count)]
    count, width = attended.shape
    rows = count // col_count
    index = jnp.stack([lax.axis_index("row"), lax.axis_index("col")]).astype(jnp.int32)

    def body(index_ref, *refs):
        piece_refs = refs[:row_count]
        w_ref = refs[row_count]
        own = index_ref[0]
        place = index_ref[1]
        for s in range(col_count):
            start = pl.multiple_of(((place + s) % col_count) * rows, 8)
            total = None
            for b in range(row_count):
                source = (own % 2 + b % 2) % 2 + 2 * ((own // 2 + b // 2) % 2)
                first = pl.multiple_of(source * width, 8)
                part = jnp.dot(
                    piece_refs[b][pl.ds(start, rows), :],
                    w_ref[pl.ds(first, width), :],
                    preferred_element_type=jnp.float32,
                )
                total = part if total is None else total + part
            refs[row_count + 1 + s][...] = total.astype(jnp.bfloat16)

    grid_spec = pltpu.PrefetchScalarGridSpec(
        num_scalar_prefetch=1,
        grid=(1,),
        in_specs=[pl.BlockSpec((count, width), lambda i, x: (0, 0)) for _ in pieces]
        + [pl.BlockSpec(weight.shape, lambda i, x: (0, 0))],
        out_specs=[pl.BlockSpec((rows, weight.shape[1]), lambda i, x: (0, 0)) for _ in range(col_count)],
    )
    parts = pl.pallas_call(
        body,
        grid_spec=grid_spec,
        out_shape=[jax.ShapeDtypeStruct((rows, weight.shape[1]), jnp.bfloat16) for _ in range(col_count)],
    )(index, *pieces, weight)
    total = parts[0].astype(jnp.float32)
    for s in range(1, col_count):
        total = total + lax.ppermute(
            parts[s], "col", [(j, (j + s) % col_count) for j in range(col_count)]
        ).astype(jnp.float32)
    return total


def causal_attend(proj, blocks, shifts, place, carry=None, last=True):
    diagonal = 0 in shifts
    count = proj.shape[0]
    heads = proj.shape[1] // (3 * HD)
    steps = blocks.shape[0]
    scale = HD ** (-0.5)
    shift_table = jnp.asarray(shifts, jnp.int32)

    def body(place_ref, shift_ref, q_ref, kv_ref, *refs):
        if carry is None:
            outs = refs[:-3]
        else:
            peak_in, mass_in, acc_in = refs[:3]
            outs = refs[3:-3]
        peak_ref, mass_ref, acc_ref = refs[-3:]
        step = pl.program_id(0)
        shift = shift_ref[step]
        own = place_ref[0]

        @pl.when(step == 0)
        def _():
            if carry is None:
                peak_ref[...] = jnp.full(peak_ref.shape, -1e30, jnp.float32)
                mass_ref[...] = jnp.zeros(mass_ref.shape, jnp.float32)
                acc_ref[...] = jnp.zeros(acc_ref.shape, jnp.float32)
            else:
                peak_ref[...] = peak_in[...]
                mass_ref[...] = mass_in[...]
                acc_ref[...] = acc_in[...]

        def fold(masked):
            def one(h, unused):
                lane = pl.multiple_of(h * HD, HD)
                scores = lax.dot_general(
                    q_ref[:, pl.ds(lane, HD)],
                    kv_ref[:, pl.ds(lane, HD)],
                    (((1,), (1,)), ((), ())),
                    preferred_element_type=jnp.float32,
                ) * scale
                if masked:
                    rows = lax.broadcasted_iota(jnp.int32, scores.shape, 0)
                    cols = lax.broadcasted_iota(jnp.int32, scores.shape, 1)
                    allowed = cols <= rows
                    scores = jnp.where(allowed, scores, -1e30)
                old = peak_ref[h]
                new = jnp.maximum(old, jnp.max(scores, axis=1, keepdims=True))
                weights = jnp.exp(scores - new)
                if masked:
                    weights = jnp.where(allowed, weights, 0.0)
                shrink = jnp.exp(old - new)
                mass_ref[h] = shrink * mass_ref[h] + jnp.sum(weights, axis=1, keepdims=True)
                acc_ref[h] = shrink * acc_ref[h] + jnp.dot(
                    weights.astype(jnp.bfloat16),
                    kv_ref[:, pl.ds(lane + heads * HD, HD)],
                    preferred_element_type=jnp.float32,
                )
                peak_ref[h] = new
                return unused

            if diagonal:
                lax.fori_loop(0, heads, one, 0)
            else:
                for h in range(heads):
                    one(h, 0)

        if max(shifts) > 0:

            @pl.when((shift > 0) & (shift <= own))
            def _():
                fold(False)

        if diagonal:

            @pl.when(shift == 0)
            def _():
                fold(True)

        @pl.when(step == steps - 1)
        def _():
            if last:
                for h in range(heads):
                    outs[0][:, h * HD : (h + 1) * HD] = (acc_ref[h] / mass_ref[h]).astype(
                        outs[0].dtype
                    )
            else:
                outs[0][...] = peak_ref[...]
                outs[1][...] = mass_ref[...]
                outs[2][...] = acc_ref[...]

    state_specs = [
        pl.BlockSpec((heads, count, 1), lambda j, p, s: (0, 0, 0)),
        pl.BlockSpec((heads, count, 1), lambda j, p, s: (0, 0, 0)),
        pl.BlockSpec((heads, count, HD), lambda j, p, s: (0, 0, 0)),
    ]
    state_shapes = [
        jax.ShapeDtypeStruct((heads, count, 1), jnp.float32),
        jax.ShapeDtypeStruct((heads, count, 1), jnp.float32),
        jax.ShapeDtypeStruct((heads, count, HD), jnp.float32),
    ]
    in_specs = [
        pl.BlockSpec((count, heads * HD), lambda j, p, s: (0, 0)),
        pl.BlockSpec((None, count, 2 * heads * HD), lambda j, p, s: (j, 0, 0)),
    ]
    if carry is not None:
        in_specs = in_specs + state_specs
    if last:
        out_specs = pl.BlockSpec((count, heads * HD), lambda j, p, s: (0, 0))
        out_shape = jax.ShapeDtypeStruct((count, heads * HD), jnp.bfloat16)
    else:
        out_specs = state_specs
        out_shape = state_shapes
    grid_spec = pltpu.PrefetchScalarGridSpec(
        num_scalar_prefetch=2,
        grid=(steps,),
        in_specs=in_specs,
        out_specs=out_specs,
        scratch_shapes=[
            pltpu.VMEM((heads, count, 1), jnp.float32),
            pltpu.VMEM((heads, count, 1), jnp.float32),
            pltpu.VMEM((heads, count, HD), jnp.float32),
        ],
    )
    extra = () if carry is None else tuple(carry)
    return pl.pallas_call(
        body,
        grid_spec=grid_spec,
        out_shape=out_shape,
    )(place, shift_table, proj, blocks, *extra)


def per_device(
    text_embed,
    vis_embed,
    vis_segment,
    vis_valid,
    vis_gain,
    vis_wq,
    vis_wk,
    vis_wv,
    vis_wo,
    dec_gain,
    dec_wq,
    dec_wk,
    dec_wv,
    dec_wo,
):
    row_count = lax.axis_size("row")
    col_count = lax.axis_size("col")
    width = vis_wq.shape[1]
    local = width // row_count
    margin = MAXIMG - 1
    piece_ids = gather_permute(jnp.stack([vis_segment, vis_valid], axis=1), "col").T
    piece_len = piece_ids.shape[1]
    framed_ids = with_halo(piece_ids, (("req", 1),), margin)
    total_slots = piece_len * lax.axis_size("req")
    prompt_rows = text_embed.shape[0]
    prompt_total = prompt_rows * lax.axis_size("req") * col_count
    window_len = piece_len + 2 * margin
    window_start = lax.axis_index("req") * piece_len - margin
    window_index = jnp.arange(window_len, dtype=jnp.int32)
    key_slots = window_start + window_index
    inside = (key_slots >= 0) & (key_slots < total_slots)
    key_segment = framed_ids[0]
    key_valid = framed_ids[1]
    begins = jnp.concatenate([jnp.ones((1,), jnp.bool_), key_segment[1:] != key_segment[:-1]])
    begins = begins | (key_slots == 0)
    image_first = lax.cummax(jnp.where(begins, key_slots, window_start), axis=0)
    target_window = image_first * prompt_total // total_slots + key_slots - image_first
    vis_cols = received(norm_local(vis_embed, vis_gain), "col")
    vis_proj = head_project(vis_cols, (vis_wq, vis_wk, vis_wv), "col")
    vis_pairs = jnp.stack([vis_proj[:, local : 2 * local], vis_proj[:, 2 * local :]])
    framed = with_halo(vis_pairs, (("req", 1),), margin)
    query_local = margin + jnp.arange(piece_len, dtype=jnp.int32)
    query_slots = window_start + query_local
    query_segment = key_segment[query_local]
    seen = (
        inside[None, :]
        & (query_segment[:, None] == key_segment[None, :])
        & ((key_valid[None, :] == 1) | (query_slots[:, None] == key_slots[None, :]))
    )
    vis_att = attend_block(vis_proj[:, :local], framed[0], framed[1], seen)
    vis_out = (vis_embed.astype(jnp.float32) + out_project_heads(vis_att, vis_wo)).astype(
        jnp.bfloat16
    )
    device_place = lax.axis_index("req") * col_count + lax.axis_index("col")
    owned = device_place * prompt_rows + jnp.arange(prompt_rows, dtype=jnp.int32)
    slot_rows = vis_out.shape[0]
    following = passed_along(vis_out, ("req", "col"), -1)
    near_rows = jnp.concatenate([vis_out, following], axis=0)
    near_local = (
        margin + lax.axis_index("col") * slot_rows + jnp.arange(2 * slot_rows, dtype=jnp.int32)
    )
    near_slots = window_start + near_local
    present = near_slots < total_slots
    near_target = jnp.where(present, target_window[near_local], -1)
    near_valid = key_valid[near_local]
    onehot = ((owned[:, None] == near_target[None, :]) & (near_valid[None, :] == 1)).astype(
        jnp.bfloat16
    )
    carried = jnp.dot(onehot, near_rows, preferred_element_type=jnp.float32)
    mixed = (text_embed.astype(jnp.float32) + carried).astype(jnp.bfloat16)
    dec_cols = received(norm_local(mixed, dec_gain), "col")
    dec_proj = head_project(dec_cols, (dec_wq, dec_wk, dec_wv), "col")
    dec_rows = dec_proj.shape[0]
    keyvals = dec_proj[:, local:]
    req_count = lax.axis_size("req")
    earlier = [keyvals] + [
        lax.ppermute(keyvals, "req", [(j, j + s) for j in range(req_count - s)])
        for s in range(1, req_count)
    ]
    place = lax.axis_index("req").astype(jnp.int32).reshape(1)
    near = [0]
    far = list(range(1, req_count))
    state = causal_attend(
        dec_proj, jnp.stack([earlier[s] for s in near]), near, place, last=False
    )
    dec_att = causal_attend(
        dec_proj, jnp.stack([earlier[s] for s in far]), far, place, carry=state
    )
    return (mixed.astype(jnp.float32) + out_project_heads(dec_att, dec_wo)).astype(jnp.bfloat16)


def solution(mesh):
    return jax.shard_map(
        per_device,
        mesh=mesh,
        in_specs=(
            P(("req", "col"), "row"),
            P(("req", "col"), "row"),
            P(("req", "col")),
            P(("req", "col")),
            P("row"),
            P("row", "col"),
            P("row", "col"),
            P("row", "col"),
            P("col", "row"),
            P("row"),
            P("row", "col"),
            P("row", "col"),
            P("row", "col"),
            P("col", "row"),
        ),
        out_specs=P(("req", "col"), "row"),
        check_vma=False,
    )
```

```python
import jax
import jax.numpy as jnp
from jax import lax
from jax.sharding import PartitionSpec as P
from jax.experimental import pallas as pl
from jax.experimental.pallas import tpu as pltpu

D = 4096
HD = 128
MAXIMG = 256


def with_halo(cells, sides, width):
    for axis, dim in sides:
        count = lax.axis_size(axis)
        ends = count - 1
        head = lax.slice_in_dim(cells, 0, width, axis=dim)
        tail = lax.slice_in_dim(cells, cells.shape[dim] - width, cells.shape[dim], axis=dim)
        cells = jnp.concatenate(
            [
                lax.ppermute(tail, axis, [(i, (i + 1) % count) for i in range(ends)]),
                cells,
                lax.ppermute(head, axis, [((i + 1) % count, i) for i in range(ends)]),
            ],
            axis=dim,
        )
    return cells


def passed_along(shard, axis, by):
    size = lax.axis_size(axis)
    pairs = [(i, i + by) for i in range(size) if 0 <= i + by < size]
    return lax.ppermute(shard, axis, pairs)


def norm_local(values, gain):
    floats = values.astype(jnp.float32)
    squares = jnp.sum(floats * floats, axis=-1)
    totals = squares + flip(squares, "row", 1)
    totals = totals + flip(totals, "row", 2)
    factor = lax.rsqrt(totals / D + 1e-05)
    return (floats * factor[:, None] * gain.astype(jnp.float32)[None, :]).astype(jnp.bfloat16)


def gather_permute(values, axis):
    count = lax.axis_size(axis)
    index = lax.axis_index(axis)
    rows = values.shape[0]
    got = [values] + [
        lax.ppermute(values, axis, [(j, (j + s) % count) for j in range(count)])
        for s in range(1, count)
    ]
    ahead = jnp.concatenate([got[0]] + got[:0:-1], axis=0)
    twice = jnp.concatenate([ahead, ahead], axis=0)
    start = ((count - index) % count) * rows
    return lax.dynamic_slice_in_dim(twice, start, count * rows, axis=0)


def scatter_permute(values, axis):
    count = lax.axis_size(axis)
    index = lax.axis_index(axis)
    rows = values.shape[0] // count
    total = lax.dynamic_slice_in_dim(values, index * rows, rows, axis=0).astype(jnp.float32)
    for s in range(1, count):
        chunk = lax.dynamic_slice_in_dim(values, ((index + s) % count) * rows, rows, axis=0)
        total = total + lax.ppermute(
            chunk, axis, [(j, (j + s) % count) for j in range(count)]
        ).astype(jnp.float32)
    return total


def gather_cols(values):
    return gather_permute(values, "col")


def out_project(attended, weight):
    whole = lax.all_gather(attended, "row", axis=0, tiled=True)
    return lax.psum_scatter(
        jnp.dot(whole, weight, preferred_element_type=jnp.float32).astype(jnp.bfloat16),
        "col",
        scatter_dimension=0,
        tiled=True,
    ).astype(jnp.float32)


def split_heads(values):
    return values.reshape(values.shape[0], values.shape[1] // HD, HD)


def attend_block(queries, keys, values, allowed):
    query_heads = split_heads(queries)
    scores = jnp.einsum(
        "qhd,khd->hqk", query_heads, split_heads(keys), preferred_element_type=jnp.float32
    ) * HD ** (-0.5)
    scores = jnp.where(allowed[None], scores, -1e30)
    peak = jnp.max(scores, axis=-1, keepdims=True)
    weights = jnp.where(allowed[None], jnp.exp(scores - peak), 0.0)
    mass = jnp.sum(weights, axis=-1)
    summed = jnp.einsum(
        "hqk,khd->qhd",
        weights.astype(jnp.bfloat16),
        split_heads(values),
        preferred_element_type=jnp.float32,
    )
    result = summed / jnp.transpose(mass)[:, :, None]
    return result.reshape(queries.shape[0], queries.shape[1]).astype(jnp.bfloat16)


def fold_step(carry, query_heads, query_slots, key_heads, value_heads):
    peak, mass, accum = carry
    piece_slots = jnp.arange(key_heads.shape[0], dtype=jnp.int32)
    allowed = query_slots[:, None] >= piece_slots[None, :]
    scores = jnp.einsum(
        "qhd,khd->hqk", query_heads, key_heads, preferred_element_type=jnp.float32
    ) * HD ** (-0.5)
    scores = jnp.where(allowed[None], scores, -1e30)
    new_peak = jnp.maximum(peak, jnp.max(scores, axis=-1))
    weights = jnp.where(allowed[None], jnp.exp(scores - new_peak[:, :, None]), 0.0)
    summed = jnp.einsum(
        "hqk,khd->hqd",
        weights.astype(jnp.bfloat16),
        value_heads,
        preferred_element_type=jnp.float32,
    )
    return (new_peak, jnp.sum(weights, axis=-1), summed)


def start_state(head_count, query_count):
    return (
        jnp.full((head_count, query_count), -1e30, jnp.float32),
        jnp.zeros((head_count, query_count), jnp.float32),
        jnp.zeros((head_count, query_count, HD), jnp.float32),
    )


def flip(values, axis, bit):
    count = lax.axis_size(axis)
    return lax.ppermute(values, axis, [(j, j ^ bit) for j in range(count)])


def scatter_row(keep, send, cut=None):
    sent = flip(send, "row", 1)
    near = keep[0].astype(jnp.float32) + sent[0].astype(jnp.float32)
    far = (keep[1].astype(jnp.float32) + sent[1].astype(jnp.float32)).astype(jnp.bfloat16)
    total = near + flip(far, "row", 2).astype(jnp.float32)
    if cut is None:
        return total.astype(jnp.bfloat16)
    return total[:, :cut].astype(jnp.bfloat16), total[:, cut:].astype(jnp.bfloat16)


def gather_row(values):
    count = lax.axis_size("row")
    index = lax.axis_index("row")
    got = [values] + [flip(values, "row", b) for b in range(1, count)]
    stacked = jnp.stack(got)
    order = jnp.arange(count, dtype=jnp.int32) ^ index
    return jnp.take(stacked, order, axis=0)


def received(values, axis):
    count = lax.axis_size(axis)
    return [values] + [
        lax.ppermute(values, axis, [(j, (j + s) % count) for j in range(count)])
        for s in range(1, count)
    ]


def head_project(pieces, weights, axis, cut=None):
    row_count = lax.axis_size("row")
    count = len(pieces)
    rows, depth = pieces[0].shape
    part = weights[0].shape[1] // row_count
    groups = len(weights)
    index = jnp.stack([lax.axis_index(axis), lax.axis_index("row")]).astype(jnp.int32)

    def body(index_ref, *refs):
        x_refs = refs[:count]
        w_refs = refs[count : count + groups]
        keep_ref, send_ref = refs[-2:]
        own = index_ref[0]
        low = index_ref[1] % 2
        for s in range(count):
            start = pl.multiple_of(((own - s + count) % count) * rows, 8)
            for g in range(groups):
                both = jnp.dot(x_refs[s][...], w_refs[g][...], preferred_element_type=jnp.float32)
                first, second = both[:, :part], both[:, part:]
                kept = jnp.where(low == 0, first, second)
                given = jnp.where(low == 0, second, first)
                keep_ref[0, pl.ds(start, rows), g * part : (g + 1) * part] = kept.astype(
                    keep_ref.dtype
                )
                send_ref[0, pl.ds(start, rows), g * part : (g + 1) * part] = given.astype(
                    send_ref.dtype
                )

    half = row_count // 2
    block = pl.BlockSpec((1, count * rows, groups * part), lambda g, i: (g, 0, 0))
    grid_spec = pltpu.PrefetchScalarGridSpec(
        num_scalar_prefetch=1,
        grid=(half,),
        in_specs=[pl.BlockSpec((rows, depth), lambda g, i: (0, 0)) for _ in pieces]
        + [
            pl.BlockSpec((depth, 2 * part), lambda g, i: (0, (i[1] // 2 + g) % 2))
            for _ in weights
        ],
        out_specs=[block, block],
    )
    shape = jax.ShapeDtypeStruct((half, count * rows, groups * part), jnp.bfloat16)
    keep, send = pl.pallas_call(
        body,
        grid_spec=grid_spec,
        out_shape=[shape, shape],
    )(index, *pieces, *weights)
    return scatter_row(keep, send, cut)


def out_project_heads(attended, weight):
    row_count = lax.axis_size("row")
    col_count = lax.axis_size("col")
    pieces = [attended] + [flip(attended, "row", b) for b in range(1, row_count)]
    count, width = attended.shape
    rows = count // col_count
    index = jnp.stack([lax.axis_index("row"), lax.axis_index("col")]).astype(jnp.int32)

    def body(index_ref, *refs):
        piece_refs = refs[:row_count]
        w_ref = refs[row_count]
        own = index_ref[0]
        place = index_ref[1]
        for s in range(col_count):
            start = pl.multiple_of(((place + s) % col_count) * rows, 8)
            total = None
            for b in range(row_count):
                source = (own % 2 + b % 2) % 2 + 2 * ((own // 2 + b // 2) % 2)
                first = pl.multiple_of(source * width, 8)
                part = jnp.dot(
                    piece_refs[b][pl.ds(start, rows), :],
                    w_ref[pl.ds(first, width), :],
                    preferred_element_type=jnp.float32,
                )
                total = part if total is None else total + part
            refs[row_count + 1 + s][...] = total.astype(jnp.bfloat16)

    grid_spec = pltpu.PrefetchScalarGridSpec(
        num_scalar_prefetch=1,
        grid=(1,),
        in_specs=[pl.BlockSpec((count, width), lambda i, x: (0, 0)) for _ in pieces]
        + [pl.BlockSpec(weight.shape, lambda i, x: (0, 0))],
        out_specs=[pl.BlockSpec((rows, weight.shape[1]), lambda i, x: (0, 0)) for _ in range(col_count)],
    )
    parts = pl.pallas_call(
        body,
        grid_spec=grid_spec,
        out_shape=[jax.ShapeDtypeStruct((rows, weight.shape[1]), jnp.bfloat16) for _ in range(col_count)],
    )(index, *pieces, weight)
    total = parts[0].astype(jnp.float32)
    for s in range(1, col_count):
        total = total + lax.ppermute(
            parts[s], "col", [(j, (j + s) % col_count) for j in range(col_count)]
        ).astype(jnp.float32)
    return total


def causal_attend(proj, blocks, shifts, place, carry=None, last=True):
    diagonal = 0 in shifts
    count = proj.shape[0]
    heads = proj.shape[1] // HD
    steps = blocks.shape[0]
    scale = HD ** (-0.5)
    shift_table = jnp.asarray(shifts, jnp.int32)

    def body(place_ref, shift_ref, q_ref, kv_ref, *refs):
        if carry is None:
            outs = refs[:-3]
        else:
            peak_in, mass_in, acc_in = refs[:3]
            outs = refs[3:-3]
        peak_ref, mass_ref, acc_ref = refs[-3:]
        step = pl.program_id(0)
        shift = shift_ref[step]
        own = place_ref[0]

        @pl.when(step == 0)
        def _():
            if carry is None:
                peak_ref[...] = jnp.full(peak_ref.shape, -1e30, jnp.float32)
                mass_ref[...] = jnp.zeros(mass_ref.shape, jnp.float32)
                acc_ref[...] = jnp.zeros(acc_ref.shape, jnp.float32)
            else:
                peak_ref[...] = peak_in[...]
                mass_ref[...] = mass_in[...]
                acc_ref[...] = acc_in[...]

        def fold(masked):
            def one(h, unused):
                lane = pl.multiple_of(h * HD, HD)
                scores = lax.dot_general(
                    q_ref[:, pl.ds(lane, HD)],
                    kv_ref[:, pl.ds(lane, HD)],
                    (((1,), (1,)), ((), ())),
                    preferred_element_type=jnp.float32,
                ) * scale
                if masked:
                    rows = lax.broadcasted_iota(jnp.int32, scores.shape, 0)
                    cols = lax.broadcasted_iota(jnp.int32, scores.shape, 1)
                    allowed = cols <= rows
                    scores = jnp.where(allowed, scores, -1e30)
                old = peak_ref[h]
                new = jnp.maximum(old, jnp.max(scores, axis=1, keepdims=True))
                weights = jnp.exp(scores - new)
                if masked:
                    weights = jnp.where(allowed, weights, 0.0)
                shrink = jnp.exp(old - new)
                mass_ref[h] = shrink * mass_ref[h] + jnp.sum(weights, axis=1, keepdims=True)
                acc_ref[h] = shrink * acc_ref[h] + jnp.dot(
                    weights.astype(jnp.bfloat16),
                    kv_ref[:, pl.ds(lane + heads * HD, HD)],
                    preferred_element_type=jnp.float32,
                )
                peak_ref[h] = new
                return unused

            if diagonal:
                lax.fori_loop(0, heads, one, 0)
            else:
                for h in range(heads):
                    one(h, 0)

        if max(shifts) > 0:

            @pl.when((shift > 0) & (shift <= own))
            def _():
                fold(False)

        if diagonal:

            @pl.when(shift == 0)
            def _():
                fold(True)

        @pl.when(step == steps - 1)
        def _():
            if last:
                for h in range(heads):
                    outs[0][:, h * HD : (h + 1) * HD] = (acc_ref[h] / mass_ref[h]).astype(
                        outs[0].dtype
                    )
            else:
                outs[0][...] = peak_ref[...]
                outs[1][...] = mass_ref[...]
                outs[2][...] = acc_ref[...]

    state_specs = [
        pl.BlockSpec((heads, count, 1), lambda j, p, s: (0, 0, 0)),
        pl.BlockSpec((heads, count, 1), lambda j, p, s: (0, 0, 0)),
        pl.BlockSpec((heads, count, HD), lambda j, p, s: (0, 0, 0)),
    ]
    state_shapes = [
        jax.ShapeDtypeStruct((heads, count, 1), jnp.float32),
        jax.ShapeDtypeStruct((heads, count, 1), jnp.float32),
        jax.ShapeDtypeStruct((heads, count, HD), jnp.float32),
    ]
    in_specs = [
        pl.BlockSpec((count, heads * HD), lambda j, p, s: (0, 0)),
        pl.BlockSpec((None, count, 2 * heads * HD), lambda j, p, s: (j, 0, 0)),
    ]
    if carry is not None:
        in_specs = in_specs + state_specs
    if last:
        out_specs = pl.BlockSpec((count, heads * HD), lambda j, p, s: (0, 0))
        out_shape = jax.ShapeDtypeStruct((count, heads * HD), jnp.bfloat16)
    else:
        out_specs = state_specs
        out_shape = state_shapes
    grid_spec = pltpu.PrefetchScalarGridSpec(
        num_scalar_prefetch=2,
        grid=(steps,),
        in_specs=in_specs,
        out_specs=out_specs,
        scratch_shapes=[
            pltpu.VMEM((heads, count, 1), jnp.float32),
            pltpu.VMEM((heads, count, 1), jnp.float32),
            pltpu.VMEM((heads, count, HD), jnp.float32),
        ],
    )
    extra = () if carry is None else tuple(carry)
    return pl.pallas_call(
        body,
        grid_spec=grid_spec,
        out_shape=out_shape,
    )(place, shift_table, proj, blocks, *extra)


def per_device(
    text_embed,
    vis_embed,
    vis_segment,
    vis_valid,
    vis_gain,
    vis_wq,
    vis_wk,
    vis_wv,
    vis_wo,
    dec_gain,
    dec_wq,
    dec_wk,
    dec_wv,
    dec_wo,
):
    row_count = lax.axis_size("row")
    col_count = lax.axis_size("col")
    width = vis_wq.shape[1]
    local = width // row_count
    margin = MAXIMG - 1
    piece_ids = gather_permute(jnp.stack([vis_segment, vis_valid], axis=1), "col").T
    piece_len = piece_ids.shape[1]
    framed_ids = with_halo(piece_ids, (("req", 1),), margin)
    total_slots = piece_len * lax.axis_size("req")
    prompt_rows = text_embed.shape[0]
    prompt_total = prompt_rows * lax.axis_size("req") * col_count
    window_len = piece_len + 2 * margin
    window_start = lax.axis_index("req") * piece_len - margin
    window_index = jnp.arange(window_len, dtype=jnp.int32)
    key_slots = window_start + window_index
    inside = (key_slots >= 0) & (key_slots < total_slots)
    key_segment = framed_ids[0]
    key_valid = framed_ids[1]
    begins = jnp.concatenate([jnp.ones((1,), jnp.bool_), key_segment[1:] != key_segment[:-1]])
    begins = begins | (key_slots == 0)
    image_first = lax.cummax(jnp.where(begins, key_slots, window_start), axis=0)
    target_window = image_first * prompt_total // total_slots + key_slots - image_first
    vis_cols = received(norm_local(vis_embed, vis_gain), "col")
    vis_proj = head_project(vis_cols, (vis_wq, vis_wk, vis_wv), "col")
    vis_pairs = jnp.stack([vis_proj[:, local : 2 * local], vis_proj[:, 2 * local :]])
    framed = with_halo(vis_pairs, (("req", 1),), margin)
    query_local = margin + jnp.arange(piece_len, dtype=jnp.int32)
    query_slots = window_start + query_local
    query_segment = key_segment[query_local]
    seen = (
        inside[None, :]
        & (query_segment[:, None] == key_segment[None, :])
        & ((key_valid[None, :] == 1) | (query_slots[:, None] == key_slots[None, :]))
    )
    vis_att = attend_block(vis_proj[:, :local], framed[0], framed[1], seen)
    vis_out = (vis_embed.astype(jnp.float32) + out_project_heads(vis_att, vis_wo)).astype(
        jnp.bfloat16
    )
    device_place = lax.axis_index("req") * col_count + lax.axis_index("col")
    owned = device_place * prompt_rows + jnp.arange(prompt_rows, dtype=jnp.int32)
    slot_rows = vis_out.shape[0]
    following = passed_along(vis_out, ("req", "col"), -1)
    near_rows = jnp.concatenate([vis_out, following], axis=0)
    near_local = (
        margin + lax.axis_index("col") * slot_rows + jnp.arange(2 * slot_rows, dtype=jnp.int32)
    )
    near_slots = window_start + near_local
    present = near_slots < total_slots
    near_target = jnp.where(present, target_window[near_local], -1)
    near_valid = key_valid[near_local]
    onehot = ((owned[:, None] == near_target[None, :]) & (near_valid[None, :] == 1)).astype(
        jnp.bfloat16
    )
    carried = jnp.dot(onehot, near_rows, preferred_element_type=jnp.float32)
    mixed = (text_embed.astype(jnp.float32) + carried).astype(jnp.bfloat16)
    dec_cols = received(norm_local(mixed, dec_gain), "col")
    dec_proj, keyvals = head_project(dec_cols, (dec_wq, dec_wk, dec_wv), "col", local)
    dec_rows = dec_proj.shape[0]
    req_count = lax.axis_size("req")
    earlier = [keyvals] + [
        lax.ppermute(keyvals, "req", [(j, j + s) for j in range(req_count - s)])
        for s in range(1, req_count)
    ]
    place = lax.axis_index("req").astype(jnp.int32).reshape(1)
    near = [0]
    far = list(range(1, req_count))
    state = causal_attend(
        dec_proj, jnp.stack([earlier[s] for s in near]), near, place, last=False
    )
    dec_att = causal_attend(
        dec_proj, jnp.stack([earlier[s] for s in far]), far, place, carry=state
    )
    return (mixed.astype(jnp.float32) + out_project_heads(dec_att, dec_wo)).astype(jnp.bfloat16)


def solution(mesh):
    return jax.shard_map(
        per_device,
        mesh=mesh,
        in_specs=(
            P(("req", "col"), "row"),
            P(("req", "col"), "row"),
            P(("req", "col")),
            P(("req", "col")),
            P("row"),
            P("row", "col"),
            P("row", "col"),
            P("row", "col"),
            P("col", "row"),
            P("row"),
            P("row", "col"),
            P("row", "col"),
            P("row", "col"),
            P("col", "row"),
        ),
        out_specs=P(("req", "col"), "row"),
        check_vma=False,
    )
```
